128 devices in a mesh: req: 16 (over y, x), kv: 8 (over z, core).
Axes of the slice: x: 4, y: 4, z: 4, core: 2. Of those that a mesh axis runs over, the one named last changes fastest.
Arguments:
- hidden: bfloat16 [1024, 1536], P('req', 'kv'), may hold values from -6 to 6
- perm: int32 [1024], replicated, may hold values from 0 to 1023, as said below
- seq_lens: int32 [1024], P('req'), may hold values from 1 to 4096, as said below
- page_table: int32 [1024, 32], P('req'), may hold values from 0 to 319, as said below
- kv_cache: bfloat16 [5120, 8, 128, 128], P('req', 'kv'), may hold values from -52 to 52
- attn_gain: float32 [1536], replicated, may hold values from 0.1 to 1.9
- qkv_weight: bfloat16 [8, 1536, 320], P('kv'), may hold values from -0.15625 to 0.15625
- out_weight: bfloat16 [8, 192, 1536], P('kv'), may hold values from -1 to 1
- ffn_gain: float32 [1536], replicated, may hold values from 0.1 to 1.9
- router: bfloat16 [1536, 16], replicated, may hold values from -0.15625 to 0.15625
- routes: int32 [1024, 2], P(('req', 'kv')), may hold values from 0 to 15, all different within a row; in each aligned block of 8 rows (0 to 7, 8 to 15, ...) at most 2 rows name the same one
- gate_up: bfloat16 [16, 1536, 2048], P('req'), may hold values from -0.15625 to 0.15625
- down: bfloat16 [16, 1024, 1536], P('req'), may hold values from -0.1875 to 0.1875
Outputs:
- mixed: bfloat16 [1024, 1536], P(('req', 'kv'))
The draws below stay inside these ranges and needn't reach their ends.
Inputs may be any that keep to these rules, and one draw needn't show every extreme that they name: A permutation of the 1024 requests: slot s holds request perm[s]. The 64 slots of each index of req hold exactly 4 requests from each block of 64 consecutive requests. `seq_lens`: the length 4096 is reached on every index of req. `page_table`: entries 0 to (seq_lens[s] + 127) // 128 - 1 of row s are used; no page of one index of req is used by two of its slots; later entries name arbitrary pages.
All inputs are finite; a program needn't handle non-finite values.
Results may differ from the reference program's by a relative error of at most 0.017.
Values may be sent and summed in bfloat16 or wider, within the bound.
No kernel may reach another device: no remote copies, remote signals or barrier semaphores. Data moves between devices by JAX's collectives and lax.ppermute only.
A program may use at most 128 MiB of HBM per device.

```python
import math
import jax
import jax.numpy as jnp
import numpy as np
from jax import lax

MODEL_WIDTH = 1536
KVH = 8
HD = 64
G = 3
FFE = 1024
EXPERTS = 16
REQ_DEV = 64
REQUEST_TOTAL = 1024
DEAL = 4
SUB = 8
CAP = 2
PAGE = 128
MAXP = 32
POOL_DEV = 320
POOL = 5120
N_REQ = 16


def plan_pages(key):
    base_key = jax.random.fold_in(key, 7)
    device_keys = jax.random.split(base_key, N_REQ)

    def one_device(device_key):
        key_count, key_order, key_long, key_short, key_tail, key_pool = jax.random.split(device_key, 6)
        long_count = jax.random.randint(key_count, (), 1, 7)
        ranking = jax.random.permutation(key_order, REQ_DEV)
        long_pages = jax.random.randint(key_long, (REQ_DEV,), MAXP // 2, MAXP + 1)
        short_pages = jax.random.randint(key_short, (REQ_DEV,), 1, 3)
        page_count = jnp.where(ranking < long_count, long_pages, short_pages)
        page_count = jnp.where(ranking == 0, MAXP, page_count)
        tail_len = jax.random.randint(key_tail, (REQ_DEV,), 1, PAGE + 1)
        tail_len = jnp.where(ranking == 0, PAGE, tail_len)
        lengths = (page_count - 1) * PAGE + tail_len
        starts = jnp.cumsum(page_count) - page_count
        pool_order = jax.random.permutation(key_pool, POOL_DEV)
        offsets = (starts[:, None] + jnp.arange(MAXP)[None, :]) % POOL_DEV
        return (lengths.astype(jnp.int32), pool_order[offsets].astype(jnp.int32))
    lengths, tables = jax.vmap(one_device)(device_keys)
    return (lengths.reshape(REQUEST_TOTAL), tables.reshape(REQUEST_TOTAL, MAXP))


def draw_seq_lens(key, part):
    return plan_pages(key)[0]


def draw_page_table(key, part):
    return plan_pages(key)[1]


def draw_perm(key, part):
    many_keys = jax.random.split(jax.random.fold_in(key, 11), 2 * N_REQ)
    spread = jax.vmap(lambda one_key: jax.random.permutation(one_key, REQ_DEV))(many_keys[:N_REQ])
    request_ids = jnp.arange(N_REQ)[:, None] * REQ_DEV + spread
    dealt = request_ids.reshape(N_REQ, N_REQ, DEAL).transpose(1, 0, 2).reshape(N_REQ, REQ_DEV)
    shuffle = jax.vmap(lambda one_key: jax.random.permutation(one_key, REQ_DEV))(many_keys[N_REQ:])
    placed = jnp.take_along_axis(dealt, shuffle, axis=1)
    return placed.reshape(REQUEST_TOTAL).astype(jnp.int32)


def draw_kv_cache(key, part):
    shape = (POOL, KVH, 2 * HD, PAGE)
    key_values = jax.random.fold_in(jax.random.fold_in(key, 13), 0)
    values = jnp.clip(jax.random.normal(key_values, shape, jnp.float32), -6.0, 6.0)
    return values.astype(jnp.bfloat16)


def steps_of(key, extent, cuts, smallest, top_value):
    loudness, own = 1.0, jax.random.fold_in(key, 6)
    for dim, parts in cuts:
        draws = jnp.exp(jax.random.uniform(jax.random.fold_in(own, dim), (parts,), jnp.float32, smallest / len(cuts), top_value / len(cuts)))
        loudness = loudness * jnp.repeat(draws, extent[dim] // parts).reshape([-1 if axis == dim else 1 for axis in range(len(extent))])
    return loudness


def assign_block(own_key, own, number, rows, number_of, top, limit, slope):
    order = jax.random.permutation(own_key, number_of)
    packed, ordinary = portions_of(number_of, rows * top, limit, slope, True), portions_of(number_of, rows * top, limit, slope, False)
    places = jnp.arange(number_of)

    def named(sizes, rotation):
        used = int((sizes > 0).sum())
        fixed = max(1, used // 4)
        moved = fixed + (places - fixed + rotation * (used - fixed)) % max(1, number_of - fixed)
        return jnp.zeros((number_of,), jnp.int32).at[order[jnp.where(places < fixed, places, moved)]].set(jnp.asarray(sizes, jnp.int32))

    sizes = jnp.where(number % 4 == 0, named(packed, number // 4), named(ordinary, number - number // 4 - 1))
    mixed = jax.random.permutation(jax.random.fold_in(own, 3), number_of)
    giver, sink = mixed[0:number_of // 2 * 2:2], mixed[1:number_of // 2 * 2:2]
    room = jnp.minimum(sizes[giver] - 1, limit - sizes[sink]) // 2
    room = jnp.where((giver == order[0]) | (sink == order[0]) | (sizes[sink] == 0), 0, jnp.maximum(room, 0))
    moved = jax.random.randint(jax.random.fold_in(own, 4), (number_of // 2,), 0, 1 << 20) % (room + 1)
    sizes = sizes.at[giver].add(-moved).at[sink].add(moved)
    members = jnp.searchsorted(jnp.cumsum(sizes), jnp.arange(rows * top), side="right").astype(jnp.int32)
    grid = members.reshape(top, rows).T
    grid = grid[jax.random.permutation(jax.random.fold_in(own, 1), rows)]
    rotation = jax.random.randint(jax.random.fold_in(own, 2), (rows, 1), 0, top)
    return jnp.take_along_axis(grid, (jnp.arange(top)[None, :] + rotation) % top, axis=1)


def portions_of(number_of, total, bound, slope, full):
    weights = [(1 << 20) // math.isqrt(standing ** slope) + 1 for standing in range(1, number_of + 1)]
    largest = bound if full else min(bound, max(-(-total // number_of), total * weights[0] // sum(weights)))
    least = 1 if total - largest >= number_of - 1 else 0
    holding, surplus = [largest] + [least] * (number_of - 1), total - largest - least * (number_of - 1)
    while surplus > 0:
        movable = [i for i in range(1, number_of) if holding[i] < largest] or [i for i in range(1, number_of) if holding[i] < bound]
        mass, budget = sum([weights[i] for i in movable]), surplus
        for i in movable:
            addition = min(bound - holding[i], max(1, budget * weights[i] // mass), surplus)
            holding[i] = holding[i] + addition
            surplus = surplus - addition
    return np.array(holding)


def centred(stream_key, shape, scale, limit, cuts=(), kind=jnp.bfloat16):
    drawn = scale * jax.random.normal(stream_key, shape, jnp.float32)
    if cuts:
        drawn = drawn * steps_of(stream_key, shape, cuts, -0.22, 0.18)
    return jnp.clip(drawn, -limit, limit).astype(kind)


def setup_inputs(seed: int = 0) -> dict:
    key_of = jax.random.split(jax.random.key(seed), 14)
    hidden = centred(key_of[0], (REQUEST_TOTAL, MODEL_WIDTH), 1.0, 6.0, ((0, 16), (1, 8)))
    perm = draw_perm(jax.random.fold_in(key_of[13], 71), 0)
    seq_lens = draw_seq_lens(jax.random.fold_in(key_of[13], 71), 0)
    page_table = draw_page_table(jax.random.fold_in(key_of[13], 71), 0)
    kv_cache = draw_kv_cache(jax.random.fold_in(key_of[13], 71), 0)
    attn_gain = jnp.clip(1.0 + 0.18 * jax.random.normal(key_of[5], (MODEL_WIDTH,), jnp.float32), 0.1, 1.9)
    qkv_weight = centred(key_of[6], (KVH, MODEL_WIDTH, (G + 2) * HD), MODEL_WIDTH ** -0.5, 0.15625, ((0, 8),))
    out_weight = centred(key_of[7], (KVH, G * HD, MODEL_WIDTH), (HD // 2) ** -0.5, 1.0, ((0, 8),))
    ffn_gain = jnp.clip(1.0 + 0.18 * jax.random.normal(key_of[8], (MODEL_WIDTH,), jnp.float32), 0.1, 1.9)
    router = centred(key_of[9], (MODEL_WIDTH, EXPERTS), MODEL_WIDTH ** -0.5, 0.15625)
    routes_keys = jax.random.split(jax.random.fold_in(key_of[10], 1), REQUEST_TOTAL // SUB)
    routes_turns = jax.random.permutation(jax.random.fold_in(key_of[10], 3), REQUEST_TOTAL // SUB)
    routes = jax.vmap(lambda own, number: assign_block(jax.random.fold_in(key_of[10], 2), own, number, SUB, EXPERTS, 2, CAP, 2))(routes_keys, routes_turns).reshape((REQUEST_TOTAL, 2))
    gate_up = centred(key_of[11], (EXPERTS, MODEL_WIDTH, 2 * FFE), MODEL_WIDTH ** -0.5, 0.15625, ((0, 16),))
    down = centred(key_of[12], (EXPERTS, FFE, MODEL_WIDTH), FFE ** -0.5, 0.1875, ((0, 16),))
    return {"hidden": hidden, "perm": perm, "seq_lens": seq_lens, "page_table": page_table, "kv_cache": kv_cache, "attn_gain": attn_gain, "qkv_weight": qkv_weight, "out_weight": out_weight, "ffn_gain": ffn_gain, "router": router, "routes": routes, "gate_up": gate_up, "down": down}


NEG_FILL = -1e+30
EPS_NORM = 1e-05

def rms_norm(values, gain_vec):
    values = values.astype(jnp.float32)
    factor = lax.rsqrt(lax.optimization_barrier(jnp.mean(values * values, axis=-1, keepdims=True)) + EPS_NORM)
    return (values * factor * gain_vec.astype(jnp.float32)).astype(jnp.bfloat16)

def attend_device(operands):
    queries, key_new, value_new, lengths, table, pool = operands
    slot_count = queries.shape[0]
    page_need = (lengths + PAGE - 1) // PAGE
    page_ids = jnp.arange(MAXP, dtype=jnp.int32)
    in_use = page_ids[None, :] < page_need[:, None]
    target_page = jnp.where(in_use, table, POOL_DEV).reshape(-1)
    slot_ids = jnp.broadcast_to(jnp.arange(slot_count, dtype=jnp.int32)[:, None], (slot_count, MAXP)).reshape(-1)
    order_ids = jnp.broadcast_to(page_ids[None, :], (slot_count, MAXP)).reshape(-1)
    owner = jnp.full((POOL_DEV,), slot_count, jnp.int32).at[target_page].set(slot_ids, mode='drop')
    page_order = jnp.zeros((POOL_DEV,), jnp.int32).at[target_page].set(order_ids, mode='drop')
    owner_safe = jnp.minimum(owner, slot_count - 1)
    position = page_order[:, None] * PAGE + jnp.arange(PAGE, dtype=jnp.int32)[None, :]
    live = (owner[:, None] < slot_count) & (position < lengths[owner_safe][:, None])
    scale_factor = HD ** (-0.5)
    page_queries = queries[owner_safe].astype(jnp.float32)
    scores = jnp.einsum('pkgd,pkdt->pkgt', page_queries, pool[:, :, :HD, :].astype(jnp.float32), precision=lax.Precision.HIGHEST) * scale_factor
    scores = jnp.where(live[:, None, None, :], scores, NEG_FILL)
    score_new = jnp.einsum('skgd,skd->skg', queries.astype(jnp.float32), key_new.astype(jnp.float32), precision=lax.Precision.HIGHEST) * scale_factor
    page_peak = lax.optimization_barrier(jnp.max(scores, axis=3))
    slot_peak = jax.ops.segment_max(page_peak, owner_safe, num_segments=slot_count)
    slot_peak = jnp.maximum(slot_peak, score_new)
    weights = jnp.where(live[:, None, None, :], jnp.exp(scores - slot_peak[owner_safe][..., None]), 0.0)
    page_total = lax.optimization_barrier(jnp.sum(weights, axis=3))
    rounded = lax.optimization_barrier(weights.astype(jnp.bfloat16)).astype(jnp.float32)
    page_value = jnp.einsum('pkgt,pkdt->pkgd', rounded, pool[:, :, HD:, :].astype(jnp.float32), precision=lax.Precision.HIGHEST)
    total_sum = jax.ops.segment_sum(page_total, owner_safe, num_segments=slot_count)
    value_sum = jax.ops.segment_sum(page_value, owner_safe, num_segments=slot_count)
    weight_new = jnp.exp(score_new - slot_peak)
    total_sum = total_sum + weight_new
    rounded_new = lax.optimization_barrier(weight_new.astype(jnp.bfloat16)).astype(jnp.float32)
    value_sum = value_sum + rounded_new[..., None] * value_new.astype(jnp.float32)[:, :, None, :]
    return (value_sum / total_sum[..., None]).astype(jnp.bfloat16)

def run_expert(operands):
    rows_in, weight_gu, weight_down = operands
    projected_up = jnp.dot(rows_in, weight_gu, preferred_element_type=jnp.float32)
    acts = (jax.nn.silu(projected_up[:, :FFE]) * projected_up[:, FFE:]).astype(jnp.bfloat16)
    return jnp.dot(acts, weight_down, preferred_element_type=jnp.float32).astype(jnp.bfloat16)

def reference(hidden, perm, seq_lens, page_table, kv_cache, attn_gain, qkv_weight, out_weight, ffn_gain, router, routes, gate_up, down):
    tokens = jnp.take(hidden, perm, axis=0)
    normed = rms_norm(tokens, attn_gain)
    projected = jnp.einsum('sd,hdc->shc', normed.astype(jnp.float32), qkv_weight.astype(jnp.float32), precision=lax.Precision.HIGHEST)
    queries = projected[:, :, :G * HD].reshape(REQUEST_TOTAL, KVH, G, HD).astype(jnp.bfloat16)
    key_new = projected[:, :, G * HD:(G + 1) * HD].astype(jnp.bfloat16)
    value_new = projected[:, :, (G + 1) * HD:].astype(jnp.bfloat16)
    head_out = lax.map(attend_device, (queries.reshape(N_REQ, REQ_DEV, KVH, G, HD), key_new.reshape(N_REQ, REQ_DEV, KVH, HD), value_new.reshape(N_REQ, REQ_DEV, KVH, HD), seq_lens.reshape(N_REQ, REQ_DEV), page_table.reshape(N_REQ, REQ_DEV, MAXP), kv_cache.reshape(N_REQ, POOL_DEV, KVH, 2 * HD, PAGE)))
    head_out = head_out.reshape(REQUEST_TOTAL, KVH * G * HD)
    attn = jnp.dot(head_out, out_weight.reshape(KVH * G * HD, MODEL_WIDTH), preferred_element_type=jnp.float32)
    residual = (tokens.astype(jnp.float32) + attn).astype(jnp.bfloat16)
    normed_ffn = rms_norm(residual, ffn_gain)
    logits = jnp.dot(normed_ffn, router, preferred_element_type=jnp.float32)
    chosen = jnp.take_along_axis(logits, routes, axis=1)
    sigmoid_vals = jax.nn.sigmoid(chosen)
    gates = sigmoid_vals / lax.optimization_barrier(jnp.sum(sigmoid_vals, axis=1, keepdims=True))
    block_count = REQUEST_TOTAL // SUB
    route_blocks = routes.reshape(block_count, SUB * 2)
    onehot_int = (route_blocks[:, :, None] == jnp.arange(EXPERTS, dtype=jnp.int32)[None, None, :]).astype(jnp.int32)
    earlier = jnp.cumsum(onehot_int, axis=1) - onehot_int
    rank_in = lax.optimization_barrier(jnp.sum(earlier * onehot_int, axis=2))
    place_at = route_blocks * CAP + rank_in
    placement_plan = (place_at[:, :, None] == jnp.arange(EXPERTS * CAP, dtype=jnp.int32)[None, None, :]).astype(jnp.float32)
    paired_rows = jnp.repeat(normed_ffn, 2, axis=0).reshape(block_count, SUB * 2, MODEL_WIDTH).astype(jnp.float32)
    holding_arrays = jnp.einsum('nwy,nwl->nyl', placement_plan, paired_rows, precision=lax.Precision.HIGHEST).astype(jnp.bfloat16)
    by_expert = holding_arrays.reshape(block_count, EXPERTS, CAP, MODEL_WIDTH).transpose(1, 0, 2, 3).reshape(EXPERTS, block_count * CAP, MODEL_WIDTH)
    results = lax.map(run_expert, (by_expert, gate_up, down))
    return_trip = results.reshape(EXPERTS, block_count, CAP, MODEL_WIDTH).transpose(1, 0, 2, 3).reshape(block_count, EXPERTS * CAP, MODEL_WIDTH)
    paired_output = jnp.einsum('fgo,fou->fgu', placement_plan, return_trip.astype(jnp.float32), precision=lax.Precision.HIGHEST).reshape(REQUEST_TOTAL, 2, MODEL_WIDTH)
    mixed = residual.astype(jnp.float32) + lax.optimization_barrier(jnp.sum(gates[:, :, None] * paired_output, axis=1))
    return mixed.astype(jnp.bfloat16)
```

```python
import jax
import jax.numpy as jnp
from jax import lax
from jax.sharding import PartitionSpec as P

REQ_DEV = 64


NEG_FILL = -1e30
EPS_NORM = 1e-05


def rms_norm(values, gain_vec):
    values = values.astype(jnp.float32)
    factor = lax.rsqrt(jnp.mean(values * values, axis=-1, keepdims=True) + EPS_NORM)
    return (values * factor * gain_vec).astype(jnp.bfloat16)


def attend(normed, seq_lens, page_table, kv_cache, qkv_weight):
    pool_pages, local_heads, twice_hd, page_len = kv_cache.shape
    head_dim = twice_hd // 2
    slot_count = normed.shape[0]
    groups = qkv_weight.shape[2] // head_dim - 2
    max_pages = page_table.shape[1]
    projected = jnp.einsum("sd,hdc->shc", normed, qkv_weight, preferred_element_type=jnp.float32)
    queries = (
        projected[:, :, : groups * head_dim]
        .reshape(slot_count, local_heads, groups, head_dim)
        .astype(jnp.bfloat16)
    )
    key_new = projected[:, :, groups * head_dim : (groups + 1) * head_dim].astype(jnp.bfloat16)
    value_new = projected[:, :, (groups + 1) * head_dim :].astype(jnp.bfloat16)
    page_need = (seq_lens + page_len - 1) // page_len
    page_ids = jnp.arange(max_pages, dtype=jnp.int32)
    in_use = page_ids[None, :] < page_need[:, None]
    pool_ids = jnp.arange(pool_pages, dtype=jnp.int32)
    match = (page_table[:, :, None] == pool_ids[None, None, :]) & in_use[:, :, None]
    belongs = jnp.any(match, axis=1)
    page_order = jnp.sum(jnp.where(match, page_ids[None, :, None], 0), axis=(0, 1))
    owner_len = jnp.sum(jnp.where(belongs, seq_lens[:, None], 0), axis=0)
    position = page_order[:, None] * page_len + jnp.arange(page_len, dtype=jnp.int32)[None, :]
    live = position < owner_len[:, None]
    scale_factor = head_dim ** (-0.5)
    page_queries = jnp.dot(
        belongs.T.astype(jnp.bfloat16),
        queries.reshape(slot_count, -1),
        preferred_element_type=jnp.float32,
    ).astype(jnp.bfloat16).reshape(pool_pages, local_heads, groups, head_dim)
    scores = (
        jnp.einsum(
            "pkgd,pkdt->pkgt",
            page_queries,
            kv_cache[:, :, :head_dim, :],
            preferred_element_type=jnp.float32,
        )
        * scale_factor
    )
    scores = jnp.where(live[:, None, None, :], scores, NEG_FILL)
    score_new = (
        jnp.einsum("skgd,skd->skg", queries, key_new, preferred_element_type=jnp.float32)
        * scale_factor
    )
    page_peak = jnp.max(scores, axis=3)
    slot_peak = jnp.max(jnp.where(belongs[:, :, None, None], page_peak[None], NEG_FILL), axis=1)
    slot_peak = jnp.maximum(slot_peak, score_new)
    page_peak_of_owner = jnp.max(
        jnp.where(belongs[:, :, None, None], slot_peak[:, None], NEG_FILL), axis=0
    )
    weights = jnp.where(
        live[:, None, None, :],
        jnp.exp(scores - page_peak_of_owner[..., None]),
        0.0,
    )
    page_total = jnp.sum(weights, axis=3)
    page_value = jnp.einsum(
        "pkgt,pkdt->pkgd",
        weights.astype(jnp.bfloat16),
        kv_cache[:, :, head_dim:, :],
        preferred_element_type=jnp.float32,
    )
    belongs_f = belongs.astype(jnp.float32)
    total_sum = jnp.dot(
        belongs_f, page_total.reshape(pool_pages, -1), precision=lax.Precision.HIGHEST
    ).reshape(slot_count, local_heads, groups)
    value_sum = jnp.dot(
        belongs_f, page_value.reshape(pool_pages, -1), precision=lax.Precision.HIGHEST
    ).reshape(slot_count, local_heads, groups, head_dim)
    weight_new = jnp.exp(score_new - slot_peak)
    total_sum = total_sum + weight_new
    rounded_new = lax.optimization_barrier(weight_new.astype(jnp.bfloat16)).astype(jnp.float32)
    value_sum = value_sum + rounded_new[..., None] * value_new.astype(jnp.float32)[:, :, None, :]
    return (value_sum / total_sum[..., None]).astype(jnp.bfloat16).reshape(slot_count, -1)


def expert_apply(piece, gate_up, down):
    n_source, slot_num, local_experts, width = piece.shape
    rows_in = piece.transpose(2, 0, 1, 3).reshape(local_experts, n_source * slot_num, width)
    projected_up = jnp.einsum("erd,edf->erf", rows_in, gate_up, preferred_element_type=jnp.float32)
    hidden_units = gate_up.shape[2] // 2
    acts = (
        jax.nn.silu(projected_up[..., :hidden_units]) * projected_up[..., hidden_units:]
    ).astype(jnp.bfloat16)
    result = jnp.einsum("erf,efd->erd", acts, down, preferred_element_type=jnp.float32).astype(
        jnp.bfloat16
    )
    return result.reshape(local_experts, n_source, slot_num, width).transpose(1, 2, 0, 3)


def shards(
    hidden,
    perm,
    seq_lens,
    page_table,
    kv_cache,
    attn_gain,
    qkv_weight,
    out_weight,
    ffn_gain,
    router,
    routes,
    gate_up,
    down,
):
    req_index = lax.axis_index("req")
    kv_index = lax.axis_index("kv")
    every_row = lax.all_gather(hidden, "req", axis=0, tiled=True)
    my_perm = lax.dynamic_slice_in_dim(perm, req_index * REQ_DEV, REQ_DEV)
    pick = (
        my_perm[:, None] == jnp.arange(every_row.shape[0], dtype=jnp.int32)[None, :]
    ).astype(every_row.dtype)
    picked_rows = jnp.dot(pick, every_row, preferred_element_type=jnp.float32).astype(
        every_row.dtype
    )
    tokens = lax.all_gather(picked_rows, "kv", axis=1, tiled=True)
    normed = rms_norm(tokens, attn_gain)
    head_out = attend(normed, seq_lens, page_table, kv_cache, qkv_weight)
    sub_rows = routes.shape[0]
    width = tokens.shape[1]
    out_flat = out_weight.reshape(-1, out_weight.shape[2])
    attn_rows = lax.psum_scatter(
        jnp.dot(head_out, out_flat, preferred_element_type=jnp.float32).astype(jnp.bfloat16),
        "kv",
        scatter_dimension=0,
        tiled=True,
    ).astype(jnp.float32)
    own_tokens = lax.dynamic_slice_in_dim(tokens, kv_index * sub_rows, sub_rows, 0)
    residual = (own_tokens.astype(jnp.float32) + attn_rows).astype(jnp.bfloat16)
    normed_ffn = rms_norm(residual, ffn_gain)
    logits = jnp.dot(normed_ffn, router, preferred_element_type=jnp.float32)
    chosen = jnp.take_along_axis(logits, routes, axis=1)
    sigmoid_vals = jax.nn.sigmoid(chosen)
    gates = sigmoid_vals / jnp.sum(sigmoid_vals, axis=1, keepdims=True)
    experts_all = router.shape[1]
    n_req = lax.axis_size("req")
    local_experts = gate_up.shape[0]
    capacity = max(2, 2 * sub_rows // experts_all + 1)
    flat_routes = routes.reshape(-1)
    onehot_int = (flat_routes[:, None] == jnp.arange(experts_all, dtype=jnp.int32)[None, :]).astype(
        jnp.int32
    )
    earlier = jnp.cumsum(onehot_int, axis=0) - onehot_int
    rank_in = jnp.sum(earlier * onehot_int, axis=1)
    place_at = (
        flat_routes // local_experts * capacity * local_experts
        + rank_in * local_experts
        + flat_routes % local_experts
    )
    placement_plan = (
        place_at[:, None] == jnp.arange(experts_all * capacity, dtype=jnp.int32)[None, :]
    ).astype(jnp.bfloat16)
    paired_rows = jnp.repeat(normed_ffn, 2, axis=0)
    outgoing = jnp.einsum(
        "qe,qd->ed", placement_plan, paired_rows, preferred_element_type=jnp.float32
    )
    outgoing = outgoing.astype(jnp.bfloat16).reshape(n_req, capacity, local_experts, width)
    arrived = lax.all_to_all(outgoing, "req", split_axis=0, concat_axis=0, tiled=True)
    returned = lax.all_to_all(
        expert_apply(arrived, gate_up, down), "req", split_axis=0, concat_axis=0, tiled=True
    )
    back_rows = returned.reshape(experts_all * capacity, width)
    paired_output = jnp.dot(placement_plan, back_rows, preferred_element_type=jnp.float32).reshape(
        sub_rows, 2, width
    )
    mixed = residual.astype(jnp.float32) + jnp.sum(gates[:, :, None] * paired_output, axis=1)
    return mixed.astype(jnp.bfloat16)


def solution(mesh):
    in_specs = (
        P("req", "kv"),
        P(),
        P("req"),
        P("req", None),
        P("req", "kv", None, None),
        P(),
        P("kv", None, None),
        P("kv", None, None),
        P(),
        P(),
        P(("req", "kv"), None),
        P("req", None, None),
        P("req", None, None),
    )
    out_specs = P(("req", "kv"), None)
    return jax.shard_map(shards, mesh=mesh, in_specs=in_specs, out_specs=out_specs, check_vma=False)
```

```python
import jax
import jax.numpy as jnp
from jax import lax
from jax.sharding import PartitionSpec as P

REQ_DEV = 64


NEG_FILL = -1e30
EPS_NORM = 1e-05


def rms_norm(values, gain_vec):
    values = values.astype(jnp.float32)
    factor = lax.rsqrt(jnp.mean(values * values, axis=-1, keepdims=True) + EPS_NORM)
    return (values * factor * gain_vec).astype(jnp.bfloat16)


def attend(normed, seq_lens, page_table, kv_cache, qkv_weight):
    pool_pages, local_heads, twice_hd, page_len = kv_cache.shape
    head_dim = twice_hd // 2
    slot_count = normed.shape[0]
    groups = qkv_weight.shape[2] // head_dim - 2
    max_pages = page_table.shape[1]
    projected = jnp.einsum("sd,hdc->shc", normed, qkv_weight, preferred_element_type=jnp.float32)
    queries = (
        projected[:, :, : groups * head_dim]
        .reshape(slot_count, local_heads, groups, head_dim)
        .astype(jnp.bfloat16)
    )
    key_new = projected[:, :, groups * head_dim : (groups + 1) * head_dim].astype(jnp.bfloat16)
    value_new = projected[:, :, (groups + 1) * head_dim :].astype(jnp.bfloat16)
    page_need = (seq_lens + page_len - 1) // page_len
    page_ids = jnp.arange(max_pages, dtype=jnp.int32)
    in_use = page_ids[None, :] < page_need[:, None]
    pool_ids = jnp.arange(pool_pages, dtype=jnp.int32)
    match = (page_table[:, :, None] == pool_ids[None, None, :]) & in_use[:, :, None]
    belongs = jnp.any(match, axis=1)
    page_order = jnp.sum(jnp.where(match, page_ids[None, :, None], 0), axis=(0, 1))
    owner_len = jnp.sum(jnp.where(belongs, seq_lens[:, None], 0), axis=0)
    position = page_order[:, None] * page_len + jnp.arange(page_len, dtype=jnp.int32)[None, :]
    live = position < owner_len[:, None]
    scale_factor = head_dim ** (-0.5)
    page_queries = jnp.dot(
        belongs.T.astype(jnp.bfloat16),
        queries.reshape(slot_count, -1),
        preferred_element_type=jnp.float32,
    ).astype(jnp.bfloat16).reshape(pool_pages, local_heads, groups, head_dim)
    scores = (
        jnp.einsum(
            "pkgd,pkdt->pkgt",
            page_queries,
            kv_cache[:, :, :head_dim, :],
            preferred_element_type=jnp.float32,
        )
        * scale_factor
    )
    scores = jnp.where(live[:, None, None, :], scores, NEG_FILL)
    score_new = (
        jnp.einsum("skgd,skd->skg", queries, key_new, preferred_element_type=jnp.float32)
        * scale_factor
    )
    page_peak = jnp.max(scores, axis=3)
    slot_peak = jnp.max(jnp.where(belongs[:, :, None, None], page_peak[None], NEG_FILL), axis=1)
    slot_peak = jnp.maximum(slot_peak, score_new)
    page_peak_of_owner = jnp.max(
        jnp.where(belongs[:, :, None, None], slot_peak[:, None], NEG_FILL), axis=0
    )
    weights = jnp.where(
        live[:, None, None, :],
        jnp.exp(scores - page_peak_of_owner[..., None]),
        0.0,
    )
    page_total = jnp.sum(weights, axis=3)
    page_value = jnp.einsum(
        "pkgt,pkdt->pkgd",
        weights.astype(jnp.bfloat16),
        kv_cache[:, :, head_dim:, :],
        preferred_element_type=jnp.float32,
    )
    belongs_f = belongs.astype(jnp.float32)
    total_sum = jnp.dot(
        belongs_f, page_total.reshape(pool_pages, -1), precision=lax.Precision.HIGHEST
    ).reshape(slot_count, local_heads, groups)
    value_sum = jnp.dot(
        belongs_f, page_value.reshape(pool_pages, -1), precision=lax.Precision.HIGHEST
    ).reshape(slot_count, local_heads, groups, head_dim)
    weight_new = jnp.exp(score_new - slot_peak)
    total_sum = total_sum + weight_new
    rounded_new = lax.optimization_barrier(weight_new.astype(jnp.bfloat16)).astype(jnp.float32)
    value_sum = value_sum + rounded_new[..., None] * value_new.astype(jnp.float32)[:, :, None, :]
    return (value_sum / total_sum[..., None]).astype(jnp.bfloat16).reshape(slot_count, -1)


def expert_apply(piece, gate_up, down):
    n_source, slot_num, local_experts, width = piece.shape
    rows_in = piece.transpose(2, 0, 1, 3).reshape(local_experts, n_source * slot_num, width)
    projected_up = jnp.einsum("erd,edf->erf", rows_in, gate_up, preferred_element_type=jnp.float32)
    hidden_units = gate_up.shape[2] // 2
    acts = (
        jax.nn.silu(projected_up[..., :hidden_units]) * projected_up[..., hidden_units:]
    ).astype(jnp.bfloat16)
    result = jnp.einsum("erf,efd->erd", acts, down, preferred_element_type=jnp.float32).astype(
        jnp.bfloat16
    )
    return result.reshape(local_experts, n_source, slot_num, width).transpose(1, 2, 0, 3)


def shards(
    hidden,
    perm,
    seq_lens,
    page_table,
    kv_cache,
    attn_gain,
    qkv_weight,
    out_weight,
    ffn_gain,
    router,
    routes,
    gate_up,
    down,
):
    req_index = lax.axis_index("req")
    kv_index = lax.axis_index("kv")
    every_row = lax.all_gather(hidden, "req", axis=0, tiled=True)
    my_perm = lax.dynamic_slice_in_dim(perm, req_index * REQ_DEV, REQ_DEV)
    pick = (
        my_perm[:, None] == jnp.arange(every_row.shape[0], dtype=jnp.int32)[None, :]
    ).astype(every_row.dtype)
    picked_rows = jnp.dot(pick, every_row, preferred_element_type=jnp.float32).astype(
        every_row.dtype
    )
    tokens = lax.all_gather(picked_rows, "kv", axis=1, tiled=True)
    normed = rms_norm(tokens, attn_gain)
    head_out = attend(normed, seq_lens, page_table, kv_cache, qkv_weight)
    sub_rows = routes.shape[0]
    width = tokens.shape[1]
    out_flat = out_weight.reshape(-1, out_weight.shape[2])
    n_kv = lax.axis_size("kv")
    partial = jnp.dot(head_out, out_flat, preferred_element_type=jnp.float32).astype(jnp.bfloat16)
    partial_parts = lax.all_to_all(
        partial.reshape(n_kv, sub_rows, partial.shape[1]), "kv", split_axis=0, concat_axis=0, tiled=True
    )
    attn_rows = jnp.sum(partial_parts.astype(jnp.float32), axis=0)
    own_tokens = lax.dynamic_slice_in_dim(tokens, kv_index * sub_rows, sub_rows, 0)
    residual = (own_tokens.astype(jnp.float32) + attn_rows).astype(jnp.bfloat16)
    normed_ffn = rms_norm(residual, ffn_gain)
    logits = jnp.dot(normed_ffn, router, preferred_element_type=jnp.float32)
    chosen = jnp.take_along_axis(logits, routes, axis=1)
    sigmoid_vals = jax.nn.sigmoid(chosen)
    gates = sigmoid_vals / jnp.sum(sigmoid_vals, axis=1, keepdims=True)
    experts_all = router.shape[1]
    n_req = lax.axis_size("req")
    local_experts = gate_up.shape[0]
    capacity = max(2, 2 * sub_rows // experts_all + 1)
    flat_routes = routes.reshape(-1)
    onehot_int = (flat_routes[:, None] == jnp.arange(experts_all, dtype=jnp.int32)[None, :]).astype(
        jnp.int32
    )
    earlier = jnp.cumsum(onehot_int, axis=0) - onehot_int
    rank_in = jnp.sum(earlier * onehot_int, axis=1)
    place_at = (
        flat_routes // local_experts * capacity * local_experts
        + rank_in * local_experts
        + flat_routes % local_experts
    )
    placement_plan = (
        place_at[:, None] == jnp.arange(experts_all * capacity, dtype=jnp.int32)[None, :]
    ).astype(jnp.bfloat16)
    paired_rows = jnp.repeat(normed_ffn, 2, axis=0)
    outgoing = jnp.einsum(
        "qe,qd->ed", placement_plan, paired_rows, preferred_element_type=jnp.float32
    )
    outgoing = outgoing.astype(jnp.bfloat16).reshape(n_req, capacity, local_experts, width)
    arrived = lax.all_to_all(outgoing, "req", split_axis=0, concat_axis=0, tiled=True)
    returned = lax.all_to_all(
        expert_apply(arrived, gate_up, down), "req", split_axis=0, concat_axis=0, tiled=True
    )
    back_rows = returned.reshape(experts_all * capacity, width)
    paired_output = jnp.dot(placement_plan, back_rows, preferred_element_type=jnp.float32).reshape(
        sub_rows, 2, width
    )
    mixed = residual.astype(jnp.float32) + jnp.sum(gates[:, :, None] * paired_output, axis=1)
    return mixed.astype(jnp.bfloat16)


def solution(mesh):
    in_specs = (
        P("req", "kv"),
        P(),
        P("req"),
        P("req", None),
        P("req", "kv", None, None),
        P(),
        P("kv", None, None),
        P("kv", None, None),
        P(),
        P(),
        P(("req", "kv"), None),
        P("req", None, None),
        P("req", None, None),
    )
    out_specs = P(("req", "kv"), None)
    return jax.shard_map(shards, mesh=mesh, in_specs=in_specs, out_specs=out_specs, check_vma=False)
```

```python
import jax
import jax.numpy as jnp
from jax import lax
from jax.sharding import PartitionSpec as P

REQ_DEV = 64


NEG_FILL = -1e30
EPS_NORM = 1e-05


def rms_norm(values, gain_vec):
    values = values.astype(jnp.float32)
    factor = lax.rsqrt(jnp.mean(values * values, axis=-1, keepdims=True) + EPS_NORM)
    return (values * factor * gain_vec).astype(jnp.bfloat16)


def attend(normed, seq_lens, page_table, kv_cache, qkv_weight):
    pool_pages, local_heads, twice_hd, page_len = kv_cache.shape
    head_dim = twice_hd // 2
    slot_count = normed.shape[0]
    groups = qkv_weight.shape[2] // head_dim - 2
    max_pages = page_table.shape[1]
    projected = jnp.einsum("sd,hdc->shc", normed, qkv_weight, preferred_element_type=jnp.float32)
    queries = (
        projected[:, :, : groups * head_dim]
        .reshape(slot_count, local_heads, groups, head_dim)
        .astype(jnp.bfloat16)
    )
    key_new = projected[:, :, groups * head_dim : (groups + 1) * head_dim].astype(jnp.bfloat16)
    value_new = projected[:, :, (groups + 1) * head_dim :].astype(jnp.bfloat16)
    page_need = (seq_lens + page_len - 1) // page_len
    page_ids = jnp.arange(max_pages, dtype=jnp.int32)
    in_use = page_ids[None, :] < page_need[:, None]
    pool_ids = jnp.arange(pool_pages, dtype=jnp.int32)
    match = (page_table[:, :, None] == pool_ids[None, None, :]) & in_use[:, :, None]
    belongs = jnp.any(match, axis=1)
    page_order = jnp.sum(jnp.where(match, page_ids[None, :, None], 0), axis=(0, 1))
    owner_len = jnp.sum(jnp.where(belongs, seq_lens[:, None], 0), axis=0)
    position = page_order[:, None] * page_len + jnp.arange(page_len, dtype=jnp.int32)[None, :]
    live = position < owner_len[:, None]
    scale_factor = head_dim ** (-0.5)
    page_queries = jnp.dot(
        belongs.T.astype(jnp.bfloat16),
        queries.reshape(slot_count, -1),
        preferred_element_type=jnp.float32,
    ).astype(jnp.bfloat16).reshape(pool_pages, local_heads, groups, head_dim)
    scores = (
        jnp.einsum(
            "pkgd,pkdt->pkgt",
            page_queries,
            kv_cache[:, :, :head_dim, :],
            preferred_element_type=jnp.float32,
        )
        * scale_factor
    )
    scores = jnp.where(live[:, None, None, :], scores, NEG_FILL)
    score_new = (
        jnp.einsum("skgd,skd->skg", queries, key_new, preferred_element_type=jnp.float32)
        * scale_factor
    )
    page_peak = jnp.max(scores, axis=3)
    slot_peak = jnp.max(jnp.where(belongs[:, :, None, None], page_peak[None], NEG_FILL), axis=1)
    slot_peak = jnp.maximum(slot_peak, score_new)
    page_peak_of_owner = jnp.max(
        jnp.where(belongs[:, :, None, None], slot_peak[:, None], NEG_FILL), axis=0
    )
    weights = jnp.where(
        live[:, None, None, :],
        jnp.exp(scores - page_peak_of_owner[..., None]),
        0.0,
    )
    page_total = jnp.sum(weights, axis=3)
    page_value = jnp.einsum(
        "pkgt,pkdt->pkgd",
        weights.astype(jnp.bfloat16),
        kv_cache[:, :, head_dim:, :],
        preferred_element_type=jnp.float32,
    )
    belongs_f = belongs.astype(jnp.float32)
    total_sum = jnp.dot(
        belongs_f, page_total.reshape(pool_pages, -1), precision=lax.Precision.HIGHEST
    ).reshape(slot_count, local_heads, groups)
    value_sum = jnp.dot(
        belongs_f, page_value.reshape(pool_pages, -1), precision=lax.Precision.HIGHEST
    ).reshape(slot_count, local_heads, groups, head_dim)
    weight_new = jnp.exp(score_new - slot_peak)
    total_sum = total_sum + weight_new
    rounded_new = lax.optimization_barrier(weight_new.astype(jnp.bfloat16)).astype(jnp.float32)
    value_sum = value_sum + rounded_new[..., None] * value_new.astype(jnp.float32)[:, :, None, :]
    return (value_sum / total_sum[..., None]).astype(jnp.bfloat16).reshape(slot_count, -1)


def expert_apply(piece, gate_up, down):
    n_source, slot_num, local_experts, width = piece.shape
    rows_in = piece.transpose(2, 0, 1, 3).reshape(local_experts, n_source * slot_num, width)
    projected_up = jnp.einsum("erd,edf->erf", rows_in, gate_up, preferred_element_type=jnp.float32)
    hidden_units = gate_up.shape[2] // 2
    acts = (
        jax.nn.silu(projected_up[..., :hidden_units]) * projected_up[..., hidden_units:]
    ).astype(jnp.bfloat16)
    result = jnp.einsum("erf,efd->erd", acts, down, preferred_element_type=jnp.float32).astype(
        jnp.bfloat16
    )
    return result.reshape(local_experts, n_source, slot_num, width).transpose(1, 2, 0, 3)


def shards(
    hidden,
    perm,
    seq_lens,
    page_table,
    kv_cache,
    attn_gain,
    qkv_weight,
    out_weight,
    ffn_gain,
    router,
    routes,
    gate_up,
    down,
):
    req_index = lax.axis_index("req")
    kv_index = lax.axis_index("kv")
    n_req = lax.axis_size("req")
    n_kv = lax.axis_size("kv")
    local_rows, col_width = hidden.shape
    deal = local_rows // n_req
    source_block = (perm // local_rows).reshape(n_req, local_rows)
    source_row = (perm % local_rows).reshape(n_req, local_rows)
    mine = source_block == req_index
    rank_sent = jnp.cumsum(mine.astype(jnp.int32), axis=1) - 1
    send_key = jnp.where(mine, rank_sent * local_rows + source_row, -1)
    send_ids = jnp.arange(deal * local_rows, dtype=jnp.int32)
    send_pick = jnp.any(send_key[:, :, None] == send_ids[None, None, :], axis=1)
    send_pick = send_pick.reshape(n_req * deal, local_rows).astype(hidden.dtype)
    outgoing_rows = jnp.dot(send_pick, hidden, preferred_element_type=jnp.float32).astype(
        hidden.dtype
    )
    arrived_rows = lax.all_to_all(
        outgoing_rows.reshape(n_req, deal, col_width), "req", split_axis=0, concat_axis=0, tiled=True
    ).reshape(n_req * deal, col_width)
    my_source = lax.dynamic_slice_in_dim(perm, req_index * local_rows, local_rows) // local_rows
    slot_ids = jnp.arange(local_rows, dtype=jnp.int32)
    same_before = (my_source[None, :] == my_source[:, None]) & (slot_ids[None, :] < slot_ids[:, None])
    rank_got = jnp.sum(same_before.astype(jnp.int32), axis=1)
    take_key = my_source * deal + rank_got
    take_pick = (take_key[:, None] == slot_ids[None, :]).astype(hidden.dtype)
    picked_rows = jnp.dot(take_pick, arrived_rows, preferred_element_type=jnp.float32).astype(
        hidden.dtype
    )
    spread = jnp.broadcast_to(picked_rows[None], (n_kv, local_rows, col_width))
    gathered = lax.all_to_all(spread, "kv", split_axis=0, concat_axis=0, tiled=True)
    tokens = gathered.transpose(1, 0, 2).reshape(local_rows, n_kv * col_width)
    normed = rms_norm(tokens, attn_gain)
    head_out = attend(normed, seq_lens, page_table, kv_cache, qkv_weight)
    sub_rows = routes.shape[0]
    width = tokens.shape[1]
    out_flat = out_weight.reshape(-1, out_weight.shape[2])
    partial = jnp.dot(head_out, out_flat, preferred_element_type=jnp.float32).astype(jnp.bfloat16)
    partial_parts = lax.all_to_all(
        partial.reshape(n_kv, sub_rows, partial.shape[1]), "kv", split_axis=0, concat_axis=0, tiled=True
    )
    attn_rows = jnp.sum(partial_parts.astype(jnp.float32), axis=0)
    own_tokens = lax.dynamic_slice_in_dim(tokens, kv_index * sub_rows, sub_rows, 0)
    residual = (own_tokens.astype(jnp.float32) + attn_rows).astype(jnp.bfloat16)
    normed_ffn = rms_norm(residual, ffn_gain)
    logits = jnp.dot(normed_ffn, router, preferred_element_type=jnp.float32)
    chosen = jnp.take_along_axis(logits, routes, axis=1)
    sigmoid_vals = jax.nn.sigmoid(chosen)
    gates = sigmoid_vals / jnp.sum(sigmoid_vals, axis=1, keepdims=True)
    experts_all = router.shape[1]
    local_experts = gate_up.shape[0]
    capacity = max(2, 2 * sub_rows // experts_all + 1)
    flat_routes = routes.reshape(-1)
    onehot_int = (flat_routes[:, None] == jnp.arange(experts_all, dtype=jnp.int32)[None, :]).astype(
        jnp.int32
    )
    earlier = jnp.cumsum(onehot_int, axis=0) - onehot_int
    rank_in = jnp.sum(earlier * onehot_int, axis=1)
    place_at = (
        flat_routes // local_experts * capacity * local_experts
        + rank_in * local_experts
        + flat_routes % local_experts
    )
    placement_plan = (
        place_at[:, None] == jnp.arange(experts_all * capacity, dtype=jnp.int32)[None, :]
    ).astype(jnp.bfloat16)
    paired_rows = jnp.repeat(normed_ffn, 2, axis=0)
    outgoing = jnp.einsum(
        "qe,qd->ed", placement_plan, paired_rows, preferred_element_type=jnp.float32
    )
    outgoing = outgoing.astype(jnp.bfloat16).reshape(n_req, capacity, local_experts, width)
    arrived = lax.all_to_all(outgoing, "req", split_axis=0, concat_axis=0, tiled=True)
    returned = lax.all_to_all(
        expert_apply(arrived, gate_up, down), "req", split_axis=0, concat_axis=0, tiled=True
    )
    back_rows = returned.reshape(experts_all * capacity, width)
    paired_output = jnp.dot(placement_plan, back_rows, preferred_element_type=jnp.float32).reshape(
        sub_rows, 2, width
    )
    mixed = residual.astype(jnp.float32) + jnp.sum(gates[:, :, None] * paired_output, axis=1)
    return mixed.astype(jnp.bfloat16)


def solution(mesh):
    in_specs = (
        P("req", "kv"),
        P(),
        P("req"),
        P("req", None),
        P("req", "kv", None, None),
        P(),
        P("kv", None, None),
        P("kv", None, None),
        P(),
        P(),
        P(("req", "kv"), None),
        P("req", None, None),
        P("req", None, None),
    )
    out_specs = P(("req", "kv"), None)
    return jax.shard_map(shards, mesh=mesh, in_specs=in_specs, out_specs=out_specs, check_vma=False)
```

```python
import jax
import jax.numpy as jnp
from jax import lax
from jax.sharding import PartitionSpec as P
from jax.experimental import pallas as pl
import functools

REQ_DEV = 64


NEG_FILL = -1e30
EPS_NORM = 1e-05


def rms_norm(values, gain_vec):
    values = values.astype(jnp.float32)
    factor = lax.rsqrt(jnp.mean(values * values, axis=-1, keepdims=True) + EPS_NORM)
    return (values * factor * gain_vec).astype(jnp.bfloat16)


def page_attention_kernel(scale, head_dim, q_ref, live_ref, kv_ref, acc_ref, peak_ref, sum_ref):
    q = q_ref[...]
    keys = kv_ref[:, 0, :head_dim, :]
    values = kv_ref[:, 0, head_dim:, :]
    live = live_ref[...] > 0.5
    scores = jnp.einsum("pgd,pdt->pgt", q, keys, preferred_element_type=jnp.float32) * scale
    scores = jnp.where(live, scores, NEG_FILL)
    peak = jnp.max(scores, axis=2, keepdims=True)
    weights = jnp.where(live, jnp.exp(scores - peak), 0.0)
    peak_ref[...] = peak
    sum_ref[...] = jnp.sum(weights, axis=2, keepdims=True)
    acc_ref[...] = jnp.einsum(
        "pgt,pdt->pgd", weights.astype(values.dtype), values, preferred_element_type=jnp.float32
    )


def page_attention(page_queries, live_f, kv_cache, block_pages=32):
    pool_pages, rows, head_dim = page_queries.shape
    page_len = kv_cache.shape[3]
    grid = (pool_pages // block_pages,)
    kernel = functools.partial(page_attention_kernel, head_dim ** (-0.5), head_dim)
    return pl.pallas_call(
        kernel,
        grid=grid,
        in_specs=[
            pl.BlockSpec((block_pages, rows, head_dim), lambda i: (i, 0, 0)),
            pl.BlockSpec((block_pages, 1, page_len), lambda i: (i, 0, 0)),
            pl.BlockSpec((block_pages, 1, 2 * head_dim, page_len), lambda i: (i, 0, 0, 0)),
        ],
        out_specs=[
            pl.BlockSpec((block_pages, rows, head_dim), lambda i: (i, 0, 0)),
            pl.BlockSpec((block_pages, rows, 1), lambda i: (i, 0, 0)),
            pl.BlockSpec((block_pages, rows, 1), lambda i: (i, 0, 0)),
        ],
        out_shape=[
            jax.ShapeDtypeStruct((pool_pages, rows, head_dim), jnp.float32),
            jax.ShapeDtypeStruct((pool_pages, rows, 1), jnp.float32),
            jax.ShapeDtypeStruct((pool_pages, rows, 1), jnp.float32),
        ],
    )(page_queries, live_f, kv_cache)


def attend(normed, seq_lens, page_table, kv_cache, qkv_weight):
    pool_pages, local_heads, twice_hd, page_len = kv_cache.shape
    head_dim = twice_hd // 2
    slot_count = normed.shape[0]
    groups = qkv_weight.shape[2] // head_dim - 2
    max_pages = page_table.shape[1]
    projected = jnp.einsum("sd,hdc->shc", normed, qkv_weight, preferred_element_type=jnp.float32)
    queries = (
        projected[:, :, : groups * head_dim]
        .reshape(slot_count, local_heads, groups, head_dim)
        .astype(jnp.bfloat16)
    )
    key_new = projected[:, :, groups * head_dim : (groups + 1) * head_dim].astype(jnp.bfloat16)
    value_new = projected[:, :, (groups + 1) * head_dim :].astype(jnp.bfloat16)
    page_need = (seq_lens + page_len - 1) // page_len
    page_ids = jnp.arange(max_pages, dtype=jnp.int32)
    in_use = page_ids[None, :] < page_need[:, None]
    pool_ids = jnp.arange(pool_pages, dtype=jnp.int32)
    match = (page_table[:, :, None] == pool_ids[None, None, :]) & in_use[:, :, None]
    belongs = jnp.any(match, axis=1)
    page_order = jnp.sum(jnp.where(match, page_ids[None, :, None], 0), axis=(0, 1))
    owner_len = jnp.sum(jnp.where(belongs, seq_lens[:, None], 0), axis=0)
    position = page_order[:, None] * page_len + jnp.arange(page_len, dtype=jnp.int32)[None, :]
    live = position < owner_len[:, None]
    scale_factor = head_dim ** (-0.5)
    row_pad = 8
    padded_queries = jnp.pad(
        queries.reshape(slot_count, groups, head_dim), ((0, 0), (0, row_pad - groups), (0, 0))
    )
    page_queries = jnp.dot(
        belongs.T.astype(jnp.bfloat16),
        padded_queries.reshape(slot_count, -1),
        preferred_element_type=jnp.float32,
    ).astype(jnp.bfloat16).reshape(pool_pages, row_pad, head_dim)
    live_f = live.astype(jnp.float32).reshape(pool_pages, 1, page_len)
    page_value, page_peak, page_total = page_attention(page_queries, live_f, kv_cache)
    page_value = page_value[:, :groups, :]
    page_peak = page_peak[:, :groups, 0]
    page_total = page_total[:, :groups, 0]
    score_new = (
        jnp.einsum("skgd,skd->skg", queries, key_new, preferred_element_type=jnp.float32)
        * scale_factor
    ).reshape(slot_count, groups)
    slot_peak = jnp.max(jnp.where(belongs[:, :, None], page_peak[None], NEG_FILL), axis=1)
    slot_peak = jnp.maximum(slot_peak, score_new)
    page_peak_of_owner = jnp.max(jnp.where(belongs[:, :, None], slot_peak[:, None], NEG_FILL), axis=0)
    page_scale = jnp.exp(page_peak - page_peak_of_owner)
    belongs_f = belongs.astype(jnp.float32)
    total_sum = jnp.dot(belongs_f, page_total * page_scale, precision=lax.Precision.HIGHEST)
    value_sum = jnp.dot(
        belongs_f,
        (page_value * page_scale[..., None]).reshape(pool_pages, -1),
        precision=lax.Precision.HIGHEST,
    ).reshape(slot_count, groups, head_dim)
    weight_new = jnp.exp(score_new - slot_peak)
    total_sum = total_sum + weight_new
    rounded_new = lax.optimization_barrier(weight_new.astype(jnp.bfloat16)).astype(jnp.float32)
    value_sum = value_sum + rounded_new[..., None] * value_new.astype(jnp.float32).reshape(slot_count, 1, head_dim)
    return (value_sum / total_sum[..., None]).astype(jnp.bfloat16).reshape(slot_count, -1)


def expert_apply(piece, gate_up, down):
    n_source, slot_num, local_experts, width = piece.shape
    rows_in = piece.transpose(2, 0, 1, 3).reshape(local_experts, n_source * slot_num, width)
    projected_up = jnp.einsum("erd,edf->erf", rows_in, gate_up, preferred_element_type=jnp.float32)
    hidden_units = gate_up.shape[2] // 2
    acts = (
        jax.nn.silu(projected_up[..., :hidden_units]) * projected_up[..., hidden_units:]
    ).astype(jnp.bfloat16)
    result = jnp.einsum("erf,efd->erd", acts, down, preferred_element_type=jnp.float32).astype(
        jnp.bfloat16
    )
    return result.reshape(local_experts, n_source, slot_num, width).transpose(1, 2, 0, 3)


def shards(
    hidden,
    perm,
    seq_lens,
    page_table,
    kv_cache,
    attn_gain,
    qkv_weight,
    out_weight,
    ffn_gain,
    router,
    routes,
    gate_up,
    down,
):
    req_index = lax.axis_index("req")
    kv_index = lax.axis_index("kv")
    n_req = lax.axis_size("req")
    n_kv = lax.axis_size("kv")
    local_rows, col_width = hidden.shape
    deal = local_rows // n_req
    source_block = (perm // local_rows).reshape(n_req, local_rows)
    source_row = (perm % local_rows).reshape(n_req, local_rows)
    mine = source_block == req_index
    rank_sent = jnp.cumsum(mine.astype(jnp.int32), axis=1) - 1
    send_key = jnp.where(mine, rank_sent * local_rows + source_row, -1)
    send_ids = jnp.arange(deal * local_rows, dtype=jnp.int32)
    send_pick = jnp.any(send_key[:, :, None] == send_ids[None, None, :], axis=1)
    send_pick = send_pick.reshape(n_req * deal, local_rows).astype(hidden.dtype)
    outgoing_rows = jnp.dot(send_pick, hidden, preferred_element_type=jnp.float32).astype(
        hidden.dtype
    )
    arrived_rows = lax.all_to_all(
        outgoing_rows.reshape(n_req, deal, col_width), "req", split_axis=0, concat_axis=0, tiled=True
    ).reshape(n_req * deal, col_width)
    my_source = lax.dynamic_slice_in_dim(perm, req_index * local_rows, local_rows) // local_rows
    slot_ids = jnp.arange(local_rows, dtype=jnp.int32)
    same_before = (my_source[None, :] == my_source[:, None]) & (slot_ids[None, :] < slot_ids[:, None])
    rank_got = jnp.sum(same_before.astype(jnp.int32), axis=1)
    take_key = my_source * deal + rank_got
    take_pick = (take_key[:, None] == slot_ids[None, :]).astype(hidden.dtype)
    picked_rows = jnp.dot(take_pick, arrived_rows, preferred_element_type=jnp.float32).astype(
        hidden.dtype
    )
    spread = jnp.broadcast_to(picked_rows[None], (n_kv, local_rows, col_width))
    gathered = lax.all_to_all(spread, "kv", split_axis=0, concat_axis=0, tiled=True)
    tokens = gathered.transpose(1, 0, 2).reshape(local_rows, n_kv * col_width)
    normed = rms_norm(tokens, attn_gain)
    head_out = attend(normed, seq_lens, page_table, kv_cache, qkv_weight)
    sub_rows = routes.shape[0]
    width = tokens.shape[1]
    out_flat = out_weight.reshape(-1, out_weight.shape[2])
    partial = jnp.dot(head_out, out_flat, preferred_element_type=jnp.float32).astype(jnp.bfloat16)
    partial_parts = lax.all_to_all(
        partial.reshape(n_kv, sub_rows, partial.shape[1]), "kv", split_axis=0, concat_axis=0, tiled=True
    )
    attn_rows = jnp.sum(partial_parts.astype(jnp.float32), axis=0)
    own_tokens = lax.dynamic_slice_in_dim(tokens, kv_index * sub_rows, sub_rows, 0)
    residual = (own_tokens.astype(jnp.float32) + attn_rows).astype(jnp.bfloat16)
    normed_ffn = rms_norm(residual, ffn_gain)
    logits = jnp.dot(normed_ffn, router, preferred_element_type=jnp.float32)
    chosen = jnp.take_along_axis(logits, routes, axis=1)
    sigmoid_vals = jax.nn.sigmoid(chosen)
    gates = sigmoid_vals / jnp.sum(sigmoid_vals, axis=1, keepdims=True)
    experts_all = router.shape[1]
    local_experts = gate_up.shape[0]
    capacity = max(2, 2 * sub_rows // experts_all + 1)
    flat_routes = routes.reshape(-1)
    onehot_int = (flat_routes[:, None] == jnp.arange(experts_all, dtype=jnp.int32)[None, :]).astype(
        jnp.int32
    )
    earlier = jnp.cumsum(onehot_int, axis=0) - onehot_int
    rank_in = jnp.sum(earlier * onehot_int, axis=1)
    place_at = (
        flat_routes // local_experts * capacity * local_experts
        + rank_in * local_experts
        + flat_routes % local_experts
    )
    placement_plan = (
        place_at[:, None] == jnp.arange(experts_all * capacity, dtype=jnp.int32)[None, :]
    ).astype(jnp.bfloat16)
    paired_rows = jnp.repeat(normed_ffn, 2, axis=0)
    outgoing = jnp.einsum(
        "qe,qd->ed", placement_plan, paired_rows, preferred_element_type=jnp.float32
    )
    outgoing = outgoing.astype(jnp.bfloat16).reshape(n_req, capacity, local_experts, width)
    arrived = lax.all_to_all(outgoing, "req", split_axis=0, concat_axis=0, tiled=True)
    returned = lax.all_to_all(
        expert_apply(arrived, gate_up, down), "req", split_axis=0, concat_axis=0, tiled=True
    )
    back_rows = returned.reshape(experts_all * capacity, width)
    paired_output = jnp.dot(placement_plan, back_rows, preferred_element_type=jnp.float32).reshape(
        sub_rows, 2, width
    )
    mixed = residual.astype(jnp.float32) + jnp.sum(gates[:, :, None] * paired_output, axis=1)
    return mixed.astype(jnp.bfloat16)


def solution(mesh):
    in_specs = (
        P("req", "kv"),
        P(),
        P("req"),
        P("req", None),
        P("req", "kv", None, None),
        P(),
        P("kv", None, None),
        P("kv", None, None),
        P(),
        P(),
        P(("req", "kv"), None),
        P("req", None, None),
        P("req", None, None),
    )
    out_specs = P(("req", "kv"), None)
    return jax.shard_map(shards, mesh=mesh, in_specs=in_specs, out_specs=out_specs, check_vma=False)
```

```python
import jax
import jax.numpy as jnp
from jax import lax
from jax.sharding import PartitionSpec as P

REQ_DEV = 64


NEG_FILL = -1e30
EPS_NORM = 1e-05


def rms_norm(values, gain_vec):
    values = values.astype(jnp.float32)
    factor = lax.rsqrt(jnp.mean(values * values, axis=-1, keepdims=True) + EPS_NORM)
    return (values * factor * gain_vec).astype(jnp.bfloat16)


def attend(normed, seq_lens, page_table, kv_cache, qkv_weight):
    pool_pages, local_heads, twice_hd, page_len = kv_cache.shape
    head_dim = twice_hd // 2
    kv_parts, slot_count, part_width = normed.shape
    groups = qkv_weight.shape[2] // head_dim - 2
    max_pages = page_table.shape[1]
    weight_parts = qkv_weight.reshape(local_heads, kv_parts, part_width, qkv_weight.shape[2])
    projected = jnp.einsum(
        "ksd,hkdc->shc", normed, weight_parts, preferred_element_type=jnp.float32
    )
    queries = (
        projected[:, :, : groups * head_dim]
        .reshape(slot_count, local_heads, groups, head_dim)
        .astype(jnp.bfloat16)
    )
    key_new = projected[:, :, groups * head_dim : (groups + 1) * head_dim].astype(jnp.bfloat16)
    value_new = projected[:, :, (groups + 1) * head_dim :].astype(jnp.bfloat16)
    page_need = (seq_lens + page_len - 1) // page_len
    page_ids = jnp.arange(max_pages, dtype=jnp.int32)
    in_use = page_ids[None, :] < page_need[:, None]
    pool_ids = jnp.arange(pool_pages, dtype=jnp.int32)
    match = (page_table[:, :, None] == pool_ids[None, None, :]) & in_use[:, :, None]
    belongs = jnp.any(match, axis=1)
    page_order = jnp.sum(jnp.where(match, page_ids[None, :, None], 0), axis=(0, 1))
    owner_len = jnp.sum(jnp.where(belongs, seq_lens[:, None], 0), axis=0)
    position = page_order[:, None] * page_len + jnp.arange(page_len, dtype=jnp.int32)[None, :]
    live = position < owner_len[:, None]
    scale_factor = head_dim ** (-0.5)
    page_queries = jnp.einsum(
        "sp,skgd->pkgd", belongs.astype(jnp.bfloat16), queries, preferred_element_type=jnp.float32
    ).astype(jnp.bfloat16)
    scores = (
        jnp.einsum(
            "pkgd,pkdt->pkgt",
            page_queries,
            kv_cache[:, :, :head_dim, :],
            preferred_element_type=jnp.float32,
        )
        * scale_factor
    )
    scores = jnp.where(live[:, None, None, :], scores, NEG_FILL)
    score_new = (
        jnp.einsum("skgd,skd->skg", queries, key_new, preferred_element_type=jnp.float32)
        * scale_factor
    )
    page_peak = jnp.max(scores, axis=3)
    slot_peak = jnp.max(jnp.where(belongs[:, :, None, None], page_peak[None], NEG_FILL), axis=1)
    slot_peak = jnp.maximum(slot_peak, score_new)
    page_peak_of_owner = jnp.max(
        jnp.where(belongs[:, :, None, None], slot_peak[:, None], NEG_FILL), axis=0
    )
    weights = jnp.where(
        live[:, None, None, :],
        jnp.exp(scores - page_peak_of_owner[..., None]),
        0.0,
    )
    page_total = jnp.sum(weights, axis=3)
    page_value = jnp.einsum(
        "pkgt,pkdt->pkgd",
        weights.astype(jnp.bfloat16),
        kv_cache[:, :, head_dim:, :],
        preferred_element_type=jnp.float32,
    )
    belongs_f = belongs.astype(jnp.float32)
    total_sum = jnp.einsum("sp,pkg->skg", belongs_f, page_total, precision=lax.Precision.HIGHEST)
    value_sum = jnp.einsum(
        "sp,pkgd->skgd", belongs_f, page_value, precision=lax.Precision.HIGHEST
    )
    weight_new = jnp.exp(score_new - slot_peak)
    total_sum = total_sum + weight_new
    rounded_new = lax.optimization_barrier(weight_new.astype(jnp.bfloat16)).astype(jnp.float32)
    value_sum = value_sum + rounded_new[..., None] * value_new.astype(jnp.float32)[:, :, None, :]
    return (value_sum / total_sum[..., None]).astype(jnp.bfloat16).reshape(slot_count, -1)


def expert_apply(piece, gate_up, down):
    n_source, slot_num, local_experts, width = piece.shape
    rows_in = piece.transpose(2, 0, 1, 3).reshape(local_experts, n_source * slot_num, width)
    projected_up = jnp.einsum("erd,edf->erf", rows_in, gate_up, preferred_element_type=jnp.float32)
    hidden_units = gate_up.shape[2] // 2
    acts = (
        jax.nn.silu(projected_up[..., :hidden_units]) * projected_up[..., hidden_units:]
    ).astype(jnp.bfloat16)
    result = jnp.einsum("erf,efd->erd", acts, down, preferred_element_type=jnp.float32).astype(
        jnp.bfloat16
    )
    return result.reshape(local_experts, n_source, slot_num, width).transpose(1, 2, 0, 3)


def shards(
    hidden,
    perm,
    seq_lens,
    page_table,
    kv_cache,
    attn_gain,
    qkv_weight,
    out_weight,
    ffn_gain,
    router,
    routes,
    gate_up,
    down,
):
    req_index = lax.axis_index("req")
    kv_index = lax.axis_index("kv")
    n_req = lax.axis_size("req")
    n_kv = lax.axis_size("kv")
    local_rows, col_width = hidden.shape
    deal = local_rows // n_req
    source_block = (perm // local_rows).reshape(n_req, local_rows)
    source_row = (perm % local_rows).reshape(n_req, local_rows)
    mine = source_block == req_index
    rank_sent = jnp.cumsum(mine.astype(jnp.int32), axis=1) - 1
    send_key = jnp.where(mine, rank_sent * local_rows + source_row, -1)
    send_ids = jnp.arange(deal * local_rows, dtype=jnp.int32)
    send_pick = jnp.any(send_key[:, :, None] == send_ids[None, None, :], axis=1)
    send_pick = send_pick.reshape(n_req * deal, local_rows).astype(hidden.dtype)
    outgoing_rows = jnp.dot(send_pick, hidden, preferred_element_type=jnp.float32).astype(
        hidden.dtype
    )
    arrived_rows = lax.all_to_all(
        outgoing_rows.reshape(n_req, deal, col_width), "req", split_axis=0, concat_axis=0, tiled=True
    ).reshape(n_req * deal, col_width)
    my_source = lax.dynamic_slice_in_dim(perm, req_index * local_rows, local_rows) // local_rows
    slot_ids = jnp.arange(local_rows, dtype=jnp.int32)
    same_before = (my_source[None, :] == my_source[:, None]) & (slot_ids[None, :] < slot_ids[:, None])
    rank_got = jnp.sum(same_before.astype(jnp.int32), axis=1)
    take_key = my_source * deal + rank_got
    take_pick = (take_key[:, None] == slot_ids[None, :]).astype(hidden.dtype)
    picked_rows = jnp.dot(take_pick, arrived_rows, preferred_element_type=jnp.float32).astype(
        hidden.dtype
    )
    spread = jnp.broadcast_to(picked_rows[None], (n_kv, local_rows, col_width))
    gathered = lax.all_to_all(spread, "kv", split_axis=0, concat_axis=0, tiled=True)
    gathered_f = gathered.astype(jnp.float32)
    norm_factor = lax.rsqrt(
        jnp.sum(gathered_f * gathered_f, axis=(0, 2), keepdims=True) / (n_kv * col_width) + EPS_NORM
    )
    normed = (gathered_f * norm_factor * attn_gain.reshape(n_kv, 1, col_width)).astype(jnp.bfloat16)
    head_out = attend(normed, seq_lens, page_table, kv_cache, qkv_weight)
    sub_rows = routes.shape[0]
    width = n_kv * col_width
    out_flat = out_weight.reshape(-1, out_weight.shape[2])
    partial = jnp.dot(head_out, out_flat, preferred_element_type=jnp.float32).astype(jnp.bfloat16)
    partial_parts = lax.all_to_all(
        partial.reshape(n_kv, sub_rows, partial.shape[1]), "kv", split_axis=0, concat_axis=0, tiled=True
    )
    attn_rows = jnp.sum(partial_parts.astype(jnp.float32), axis=0)
    own_tokens = lax.dynamic_slice_in_dim(gathered, kv_index * sub_rows, sub_rows, 1)
    own_tokens = own_tokens.transpose(1, 0, 2).reshape(sub_rows, width)
    residual = (own_tokens.astype(jnp.float32) + attn_rows).astype(jnp.bfloat16)
    normed_ffn = rms_norm(residual, ffn_gain)
    logits = jnp.dot(normed_ffn, router, preferred_element_type=jnp.float32)
    chosen = jnp.take_along_axis(logits, routes, axis=1)
    sigmoid_vals = jax.nn.sigmoid(chosen)
    gates = sigmoid_vals / jnp.sum(sigmoid_vals, axis=1, keepdims=True)
    experts_all = router.shape[1]
    local_experts = gate_up.shape[0]
    capacity = max(2, 2 * sub_rows // experts_all + 1)
    flat_routes = routes.reshape(-1)
    onehot_int = (flat_routes[:, None] == jnp.arange(experts_all, dtype=jnp.int32)[None, :]).astype(
        jnp.int32
    )
    earlier = jnp.cumsum(onehot_int, axis=0) - onehot_int
    rank_in = jnp.sum(earlier * onehot_int, axis=1)
    place_at = (
        flat_routes // local_experts * capacity * local_experts
        + rank_in * local_experts
        + flat_routes % local_experts
    )
    placement_plan = (
        place_at[:, None] == jnp.arange(experts_all * capacity, dtype=jnp.int32)[None, :]
    ).astype(jnp.bfloat16)
    paired_rows = jnp.repeat(normed_ffn, 2, axis=0)
    outgoing = jnp.einsum(
        "qe,qd->ed", placement_plan, paired_rows, preferred_element_type=jnp.float32
    )
    outgoing = outgoing.astype(jnp.bfloat16).reshape(n_req, capacity, local_experts, width)
    arrived = lax.all_to_all(outgoing, "req", split_axis=0, concat_axis=0, tiled=True)
    returned = lax.all_to_all(
        expert_apply(arrived, gate_up, down), "req", split_axis=0, concat_axis=0, tiled=True
    )
    back_rows = returned.reshape(experts_all * capacity, width)
    paired_output = jnp.dot(placement_plan, back_rows, preferred_element_type=jnp.float32).reshape(
        sub_rows, 2, width
    )
    mixed = residual.astype(jnp.float32) + jnp.sum(gates[:, :, None] * paired_output, axis=1)
    return mixed.astype(jnp.bfloat16)


def solution(mesh):
    in_specs = (
        P("req", "kv"),
        P(),
        P("req"),
        P("req", None),
        P("req", "kv", None, None),
        P(),
        P("kv", None, None),
        P("kv", None, None),
        P(),
        P(),
        P(("req", "kv"), None),
        P("req", None, None),
        P("req", None, None),
    )
    out_specs = P(("req", "kv"), None)
    return jax.shard_map(shards, mesh=mesh, in_specs=in_specs, out_specs=out_specs, check_vma=False)
```

```python
import jax
import jax.numpy as jnp
from jax import lax
from jax.sharding import PartitionSpec as P

REQ_DEV = 64


NEG_FILL = -1e30
EPS_NORM = 1e-05


def rms_norm(values, gain_vec):
    values = values.astype(jnp.float32)
    factor = lax.rsqrt(jnp.mean(values * values, axis=-1, keepdims=True) + EPS_NORM)
    return (values * factor * gain_vec).astype(jnp.bfloat16)


def attend(normed, seq_lens, page_table, kv_cache, qkv_weight):
    pool_pages, local_heads, twice_hd, page_len = kv_cache.shape
    head_dim = twice_hd // 2
    slot_count = normed.shape[0]
    groups = qkv_weight.shape[2] // head_dim - 2
    max_pages = page_table.shape[1]
    projected = jnp.einsum("sd,hdc->shc", normed, qkv_weight, preferred_element_type=jnp.float32)
    queries = (
        projected[:, :, : groups * head_dim]
        .reshape(slot_count, local_heads, groups, head_dim)
        .astype(jnp.bfloat16)
    )
    key_new = projected[:, :, groups * head_dim : (groups + 1) * head_dim].astype(jnp.bfloat16)
    value_new = projected[:, :, (groups + 1) * head_dim :].astype(jnp.bfloat16)
    page_need = (seq_lens + page_len - 1) // page_len
    page_ids = jnp.arange(max_pages, dtype=jnp.int32)
    in_use = page_ids[None, :] < page_need[:, None]
    pool_ids = jnp.arange(pool_pages, dtype=jnp.int32)
    entry_slot = jnp.broadcast_to(
        jnp.arange(slot_count, dtype=jnp.int32)[:, None], (slot_count, max_pages)
    ).reshape(-1)
    entry_page = jnp.where(in_use, page_table, -1).reshape(-1)
    entry_order = jnp.broadcast_to(page_ids[None, :], (slot_count, max_pages)).reshape(-1)
    entry_len = jnp.broadcast_to(seq_lens[:, None], (slot_count, max_pages)).reshape(-1)
    len_unit = 64
    facts = jnp.concatenate(
        [
            (entry_slot[None, :] == jnp.arange(slot_count, dtype=jnp.int32)[:, None]).astype(jnp.float32),
            entry_order[None, :].astype(jnp.float32),
            (entry_len // len_unit)[None, :].astype(jnp.float32),
            (entry_len % len_unit)[None, :].astype(jnp.float32),
        ],
        axis=0,
    ).astype(jnp.bfloat16)
    entry_hit = (entry_page[:, None] == pool_ids[None, :]).astype(jnp.bfloat16)
    page_facts = jnp.dot(facts, entry_hit, preferred_element_type=jnp.float32)
    belongs = page_facts[:slot_count] > 0.5
    page_order = page_facts[slot_count].astype(jnp.int32)
    owner_len = (
        page_facts[slot_count + 1].astype(jnp.int32) * len_unit
        + page_facts[slot_count + 2].astype(jnp.int32)
    )
    position = page_order[:, None] * page_len + jnp.arange(page_len, dtype=jnp.int32)[None, :]
    live = position < owner_len[:, None]
    scale_factor = head_dim ** (-0.5)
    page_queries = jnp.einsum(
        "sp,skgd->pkgd", belongs.astype(jnp.bfloat16), queries, preferred_element_type=jnp.float32
    ).astype(jnp.bfloat16)
    scores = (
        jnp.einsum(
            "pkgd,pkdt->pkgt",
            page_queries,
            kv_cache[:, :, :head_dim, :],
            preferred_element_type=jnp.float32,
        )
        * scale_factor
    )
    scores = jnp.where(live[:, None, None, :], scores, NEG_FILL)
    score_new = (
        jnp.einsum("skgd,skd->skg", queries, key_new, preferred_element_type=jnp.float32)
        * scale_factor
    )
    page_peak = jnp.max(scores, axis=3)
    slot_peak = jnp.max(jnp.where(belongs[:, :, None, None], page_peak[None], NEG_FILL), axis=1)
    slot_peak = jnp.maximum(slot_peak, score_new)
    page_peak_of_owner = jnp.max(
        jnp.where(belongs[:, :, None, None], slot_peak[:, None], NEG_FILL), axis=0
    )
    weights = jnp.where(
        live[:, None, None, :],
        jnp.exp(scores - page_peak_of_owner[..., None]),
        0.0,
    )
    page_total = jnp.sum(weights, axis=3)
    page_value = jnp.einsum(
        "pkgt,pkdt->pkgd",
        weights.astype(jnp.bfloat16),
        kv_cache[:, :, head_dim:, :],
        preferred_element_type=jnp.float32,
    )
    belongs_f = belongs.astype(jnp.float32)
    total_sum = jnp.einsum("sp,pkg->skg", belongs_f, page_total, precision=lax.Precision.HIGHEST)
    value_sum = jnp.einsum(
        "sp,pkgd->skgd", belongs_f, page_value, precision=lax.Precision.HIGHEST
    )
    weight_new = jnp.exp(score_new - slot_peak)
    total_sum = total_sum + weight_new
    rounded_new = lax.optimization_barrier(weight_new.astype(jnp.bfloat16)).astype(jnp.float32)
    value_sum = value_sum + rounded_new[..., None] * value_new.astype(jnp.float32)[:, :, None, :]
    return (value_sum / total_sum[..., None]).astype(jnp.bfloat16).reshape(slot_count, -1)


def expert_apply(piece, gate_up, down):
    n_source, slot_num, local_experts, width = piece.shape
    rows_in = piece.transpose(2, 0, 1, 3).reshape(local_experts, n_source * slot_num, width)
    projected_up = jnp.einsum("erd,edf->erf", rows_in, gate_up, preferred_element_type=jnp.float32)
    hidden_units = gate_up.shape[2] // 2
    acts = (
        jax.nn.silu(projected_up[..., :hidden_units]) * projected_up[..., hidden_units:]
    ).astype(jnp.bfloat16)
    result = jnp.einsum("erf,efd->erd", acts, down, preferred_element_type=jnp.float32).astype(
        jnp.bfloat16
    )
    return result.reshape(local_experts, n_source, slot_num, width).transpose(1, 2, 0, 3)


def shards(
    hidden,
    perm,
    seq_lens,
    page_table,
    kv_cache,
    attn_gain,
    qkv_weight,
    out_weight,
    ffn_gain,
    router,
    routes,
    gate_up,
    down,
):
    req_index = lax.axis_index("req")
    kv_index = lax.axis_index("kv")
    n_req = lax.axis_size("req")
    n_kv = lax.axis_size("kv")
    local_rows, col_width = hidden.shape
    deal = local_rows // n_req
    source_block = (perm // local_rows).reshape(n_req, local_rows)
    source_row = (perm % local_rows).reshape(n_req, local_rows)
    mine = source_block == req_index
    rank_sent = jnp.cumsum(mine.astype(jnp.int32), axis=1) - 1
    send_key = jnp.where(mine, rank_sent * local_rows + source_row, -1)
    send_ids = jnp.arange(deal * local_rows, dtype=jnp.int32)
    send_pick = jnp.any(send_key[:, :, None] == send_ids[None, None, :], axis=1)
    send_pick = send_pick.reshape(n_req * deal, local_rows).astype(hidden.dtype)
    outgoing_rows = jnp.dot(send_pick, hidden, preferred_element_type=jnp.float32).astype(
        hidden.dtype
    )
    arrived_rows = lax.all_to_all(
        outgoing_rows.reshape(n_req, deal, col_width), "req", split_axis=0, concat_axis=0, tiled=True
    ).reshape(n_req * deal, col_width)
    my_source = lax.dynamic_slice_in_dim(perm, req_index * local_rows, local_rows) // local_rows
    slot_ids = jnp.arange(local_rows, dtype=jnp.int32)
    same_before = (my_source[None, :] == my_source[:, None]) & (slot_ids[None, :] < slot_ids[:, None])
    rank_got = jnp.sum(same_before.astype(jnp.int32), axis=1)
    take_key = my_source * deal + rank_got
    take_pick = (take_key[:, None] == slot_ids[None, :]).astype(hidden.dtype)
    picked_rows = jnp.dot(take_pick, arrived_rows, preferred_element_type=jnp.float32).astype(
        hidden.dtype
    )
    spread = jnp.broadcast_to(picked_rows[:, None], (local_rows, n_kv, col_width))
    tokens = lax.all_to_all(spread, "kv", split_axis=1, concat_axis=1, tiled=True).reshape(
        local_rows, n_kv * col_width
    )
    normed = rms_norm(tokens, attn_gain)
    head_out = attend(normed, seq_lens, page_table, kv_cache, qkv_weight)
    sub_rows = routes.shape[0]
    width = n_kv * col_width
    out_flat = out_weight.reshape(-1, out_weight.shape[2])
    partial = jnp.dot(head_out, out_flat, preferred_element_type=jnp.float32).astype(jnp.bfloat16)
    partial_parts = lax.all_to_all(
        partial.reshape(n_kv, sub_rows, partial.shape[1]), "kv", split_axis=0, concat_axis=0, tiled=True
    )
    attn_rows = jnp.sum(partial_parts.astype(jnp.float32), axis=0)
    own_tokens = lax.dynamic_slice_in_dim(tokens, kv_index * sub_rows, sub_rows, 0)
    residual = (own_tokens.astype(jnp.float32) + attn_rows).astype(jnp.bfloat16)
    normed_ffn = rms_norm(residual, ffn_gain)
    logits = jnp.dot(normed_ffn, router, preferred_element_type=jnp.float32)
    chosen = jnp.take_along_axis(logits, routes, axis=1)
    sigmoid_vals = jax.nn.sigmoid(chosen)
    gates = sigmoid_vals / jnp.sum(sigmoid_vals, axis=1, keepdims=True)
    experts_all = router.shape[1]
    local_experts = gate_up.shape[0]
    capacity = max(2, 2 * sub_rows // experts_all + 1)
    flat_routes = routes.reshape(-1)
    onehot_int = (flat_routes[:, None] == jnp.arange(experts_all, dtype=jnp.int32)[None, :]).astype(
        jnp.int32
    )
    earlier = jnp.cumsum(onehot_int, axis=0) - onehot_int
    rank_in = jnp.sum(earlier * onehot_int, axis=1)
    place_at = (
        flat_routes // local_experts * capacity * local_experts
        + rank_in * local_experts
        + flat_routes % local_experts
    )
    placement_plan = (
        place_at[:, None] == jnp.arange(experts_all * capacity, dtype=jnp.int32)[None, :]
    ).astype(jnp.bfloat16)
    paired_rows = jnp.repeat(normed_ffn, 2, axis=0)
    outgoing = jnp.einsum(
        "qe,qd->ed", placement_plan, paired_rows, preferred_element_type=jnp.float32
    )
    outgoing = outgoing.astype(jnp.bfloat16).reshape(n_req, capacity, local_experts, width)
    arrived = lax.all_to_all(outgoing, "req", split_axis=0, concat_axis=0, tiled=True)
    returned = lax.all_to_all(
        expert_apply(arrived, gate_up, down), "req", split_axis=0, concat_axis=0, tiled=True
    )
    back_rows = returned.reshape(experts_all * capacity, width)
    paired_output = jnp.dot(placement_plan, back_rows, preferred_element_type=jnp.float32).reshape(
        sub_rows, 2, width
    )
    mixed = residual.astype(jnp.float32) + jnp.sum(gates[:, :, None] * paired_output, axis=1)
    return mixed.astype(jnp.bfloat16)


def solution(mesh):
    in_specs = (
        P("req", "kv"),
        P(),
        P("req"),
        P("req", None),
        P("req", "kv", None, None),
        P(),
        P("kv", None, None),
        P("kv", None, None),
        P(),
        P(),
        P(("req", "kv"), None),
        P("req", None, None),
        P("req", None, None),
    )
    out_specs = P(("req", "kv"), None)
    return jax.shard_map(shards, mesh=mesh, in_specs=in_specs, out_specs=out_specs, check_vma=False)
```

```python
import jax
import jax.numpy as jnp
from jax import lax
from jax.sharding import PartitionSpec as P
from jax.experimental import pallas as pl
from jax.experimental.pallas import tpu as pltpu
import functools

REQ_DEV = 64


NEG_FILL = -1e30
EPS_NORM = 1e-05


def rms_norm(values, gain_vec):
    values = values.astype(jnp.float32)
    factor = lax.rsqrt(jnp.mean(values * values, axis=-1, keepdims=True) + EPS_NORM)
    return (values * factor * gain_vec).astype(jnp.bfloat16)


def paged_attention_kernel(
    scale, head_dim, block_pages, owner_ref, q_ref, live_ref, kv_ref, knew_ref, vnew_ref,
    out_ref, page_q, page_peak, page_sum, page_acc, slot_peak, slot_sum, slot_acc,
):
    step = pl.program_id(0)
    base = step * block_pages

    @pl.when(step == 0)
    def _():
        slot_peak[...] = jnp.full(slot_peak.shape, NEG_FILL, jnp.float32)
        slot_sum[...] = jnp.zeros(slot_sum.shape, jnp.float32)
        slot_acc[...] = jnp.zeros(slot_acc.shape, jnp.float32)

    def gather_one(p, carry):
        page_q[p] = q_ref[owner_ref[base + p]]
        return carry

    lax.fori_loop(0, block_pages, gather_one, 0)
    keys = kv_ref[:, 0, :head_dim, :]
    values = kv_ref[:, 0, head_dim:, :]
    token_ids = lax.broadcasted_iota(jnp.int32, (1, 1, keys.shape[2]), 2)
    live = token_ids < live_ref[...]
    scores = jnp.einsum(
        "pgd,pdt->pgt", page_q[...], keys, preferred_element_type=jnp.float32
    ) * scale
    scores = jnp.where(live, scores, NEG_FILL)
    peak = jnp.max(scores, axis=2, keepdims=True)
    weights = jnp.where(live, jnp.exp(scores - peak), 0.0)
    page_peak[...] = peak
    page_sum[...] = jnp.sum(weights, axis=2, keepdims=True)
    page_acc[...] = jnp.einsum(
        "pgt,pdt->pgd", weights.astype(values.dtype), values, preferred_element_type=jnp.float32
    )

    def fold_one(p, carry):
        owner = owner_ref[base + p]
        old_peak = slot_peak[owner]
        this_peak = page_peak[p]
        new_peak = jnp.maximum(old_peak, this_peak)
        keep = jnp.exp(old_peak - new_peak)
        add = jnp.exp(this_peak - new_peak)
        slot_sum[owner] = keep * slot_sum[owner] + add * page_sum[p]
        slot_acc[owner] = keep * slot_acc[owner] + add * page_acc[p]
        slot_peak[owner] = new_peak
        return carry

    lax.fori_loop(0, block_pages, fold_one, 0)

    @pl.when(step == pl.num_programs(0) - 1)
    def _():
        queries = q_ref[...].astype(jnp.float32)
        score_new = jnp.sum(queries * knew_ref[...].astype(jnp.float32), axis=2, keepdims=True) * scale
        peak_all = jnp.maximum(slot_peak[...], score_new)
        keep = jnp.exp(slot_peak[...] - peak_all)
        weight_new = jnp.exp(score_new - peak_all)
        total = slot_sum[...] * keep + weight_new
        rounded_new = weight_new.astype(jnp.bfloat16).astype(jnp.float32)
        value = slot_acc[...] * keep + rounded_new * vnew_ref[...].astype(jnp.float32)
        out_ref[...] = value / total


def paged_attention(owner, queries, live_len, kv_cache, key_new, value_new, block_pages=32):
    slot_count, rows, head_dim = queries.shape
    pool_pages = kv_cache.shape[0]
    page_len = kv_cache.shape[3]
    kernel = functools.partial(paged_attention_kernel, head_dim ** (-0.5), head_dim, block_pages)
    grid_spec = pltpu.PrefetchScalarGridSpec(
        num_scalar_prefetch=1,
        grid=(pool_pages // block_pages,),
        in_specs=[
            pl.BlockSpec((slot_count, rows, head_dim), lambda i, own: (0, 0, 0)),
            pl.BlockSpec((block_pages, 1, 1), lambda i, own: (i, 0, 0)),
            pl.BlockSpec((block_pages, 1, 2 * head_dim, page_len), lambda i, own: (i, 0, 0, 0)),
            pl.BlockSpec((slot_count, 1, head_dim), lambda i, own: (0, 0, 0)),
            pl.BlockSpec((slot_count, 1, head_dim), lambda i, own: (0, 0, 0)),
        ],
        out_specs=pl.BlockSpec((slot_count, rows, head_dim), lambda i, own: (0, 0, 0)),
        scratch_shapes=[
            pltpu.VMEM((block_pages, rows, head_dim), queries.dtype),
            pltpu.VMEM((block_pages, rows, 1), jnp.float32),
            pltpu.VMEM((block_pages, rows, 1), jnp.float32),
            pltpu.VMEM((block_pages, rows, head_dim), jnp.float32),
            pltpu.VMEM((slot_count, rows, 1), jnp.float32),
            pltpu.VMEM((slot_count, rows, 1), jnp.float32),
            pltpu.VMEM((slot_count, rows, head_dim), jnp.float32),
        ],
    )
    return pl.pallas_call(
        kernel,
        grid_spec=grid_spec,
        out_shape=jax.ShapeDtypeStruct((slot_count, rows, head_dim), jnp.float32),
        compiler_params=pltpu.CompilerParams(dimension_semantics=("arbitrary",)),
    )(owner, queries, live_len, kv_cache, key_new, value_new)


def attend(normed, seq_lens, page_table, kv_cache, qkv_weight):
    pool_pages, local_heads, twice_hd, page_len = kv_cache.shape
    head_dim = twice_hd // 2
    slot_count = normed.shape[0]
    groups = qkv_weight.shape[2] // head_dim - 2
    max_pages = page_table.shape[1]
    projected = jnp.einsum("sd,hdc->shc", normed, qkv_weight, preferred_element_type=jnp.float32)
    queries = (
        projected[:, :, : groups * head_dim]
        .reshape(slot_count, local_heads, groups, head_dim)
        .astype(jnp.bfloat16)
    )
    key_new = projected[:, :, groups * head_dim : (groups + 1) * head_dim].astype(jnp.bfloat16)
    value_new = projected[:, :, (groups + 1) * head_dim :].astype(jnp.bfloat16)
    page_need = (seq_lens + page_len - 1) // page_len
    page_ids = jnp.arange(max_pages, dtype=jnp.int32)
    in_use = page_ids[None, :] < page_need[:, None]
    pool_ids = jnp.arange(pool_pages, dtype=jnp.int32)
    entry_slot = jnp.broadcast_to(
        jnp.arange(slot_count, dtype=jnp.int32)[:, None], (slot_count, max_pages)
    ).reshape(-1)
    entry_page = jnp.where(in_use, page_table, -1).reshape(-1)
    entry_order = jnp.broadcast_to(page_ids[None, :], (slot_count, max_pages)).reshape(-1)
    entry_len = jnp.broadcast_to(seq_lens[:, None], (slot_count, max_pages)).reshape(-1)
    len_unit = 64
    facts = jnp.concatenate(
        [
            entry_slot[None, :].astype(jnp.float32),
            entry_order[None, :].astype(jnp.float32),
            (entry_len // len_unit)[None, :].astype(jnp.float32),
            (entry_len % len_unit)[None, :].astype(jnp.float32),
        ],
        axis=0,
    ).astype(jnp.bfloat16)
    entry_hit = (entry_page[:, None] == pool_ids[None, :]).astype(jnp.bfloat16)
    page_facts = jnp.dot(facts, entry_hit, preferred_element_type=jnp.float32)
    owner = page_facts[0].astype(jnp.int32)
    page_order = page_facts[1].astype(jnp.int32)
    owner_len = page_facts[2].astype(jnp.int32) * len_unit + page_facts[3].astype(jnp.int32)
    live_len = jnp.clip(owner_len - page_order * page_len, 0, page_len).reshape(pool_pages, 1, 1)
    row_pad = 8
    padded_queries = jnp.pad(
        queries.reshape(slot_count, groups, head_dim), ((0, 0), (0, row_pad - groups), (0, 0))
    )
    head_out = paged_attention(owner, padded_queries, live_len, kv_cache, key_new, value_new)
    return head_out[:, :groups, :].astype(jnp.bfloat16).reshape(slot_count, -1)


def expert_apply(piece, gate_up, down):
    n_source, slot_num, local_experts, width = piece.shape
    rows_in = piece.transpose(2, 0, 1, 3).reshape(local_experts, n_source * slot_num, width)
    projected_up = jnp.einsum("erd,edf->erf", rows_in, gate_up, preferred_element_type=jnp.float32)
    hidden_units = gate_up.shape[2] // 2
    acts = (
        jax.nn.silu(projected_up[..., :hidden_units]) * projected_up[..., hidden_units:]
    ).astype(jnp.bfloat16)
    result = jnp.einsum("erf,efd->erd", acts, down, preferred_element_type=jnp.float32).astype(
        jnp.bfloat16
    )
    return result.reshape(local_experts, n_source, slot_num, width).transpose(1, 2, 0, 3)


def shards(
    hidden,
    perm,
    seq_lens,
    page_table,
    kv_cache,
    attn_gain,
    qkv_weight,
    out_weight,
    ffn_gain,
    router,
    routes,
    gate_up,
    down,
):
    req_index = lax.axis_index("req")
    kv_index = lax.axis_index("kv")
    n_req = lax.axis_size("req")
    n_kv = lax.axis_size("kv")
    local_rows, col_width = hidden.shape
    deal = local_rows // n_req
    source_block = (perm // local_rows).reshape(n_req, local_rows)
    source_row = (perm % local_rows).reshape(n_req, local_rows)
    mine = source_block == req_index
    rank_sent = jnp.cumsum(mine.astype(jnp.int32), axis=1) - 1
    send_key = jnp.where(mine, rank_sent * local_rows + source_row, -1)
    send_ids = jnp.arange(deal * local_rows, dtype=jnp.int32)
    send_pick = jnp.any(send_key[:, :, None] == send_ids[None, None, :], axis=1)
    send_pick = send_pick.reshape(n_req * deal, local_rows).astype(hidden.dtype)
    outgoing_rows = jnp.dot(send_pick, hidden, preferred_element_type=jnp.float32).astype(
        hidden.dtype
    )
    arrived_rows = lax.all_to_all(
        outgoing_rows.reshape(n_req, deal, col_width), "req", split_axis=0, concat_axis=0, tiled=True
    ).reshape(n_req * deal, col_width)
    my_source = lax.dynamic_slice_in_dim(perm, req_index * local_rows, local_rows) // local_rows
    slot_ids = jnp.arange(local_rows, dtype=jnp.int32)
    same_before = (my_source[None, :] == my_source[:, None]) & (slot_ids[None, :] < slot_ids[:, None])
    rank_got = jnp.sum(same_before.astype(jnp.int32), axis=1)
    take_key = my_source * deal + rank_got
    take_pick = (take_key[:, None] == slot_ids[None, :]).astype(hidden.dtype)
    picked_rows = jnp.dot(take_pick, arrived_rows, preferred_element_type=jnp.float32).astype(
        hidden.dtype
    )
    spread = jnp.broadcast_to(picked_rows[:, None], (local_rows, n_kv, col_width))
    tokens = lax.all_to_all(spread, "kv", split_axis=1, concat_axis=1, tiled=True).reshape(
        local_rows, n_kv * col_width
    )
    normed = rms_norm(tokens, attn_gain)
    head_out = attend(normed, seq_lens, page_table, kv_cache, qkv_weight)
    sub_rows = routes.shape[0]
    width = n_kv * col_width
    out_flat = out_weight.reshape(-1, out_weight.shape[2])
    partial = jnp.dot(head_out, out_flat, preferred_element_type=jnp.float32).astype(jnp.bfloat16)
    partial_parts = lax.all_to_all(
        partial.reshape(n_kv, sub_rows, partial.shape[1]), "kv", split_axis=0, concat_axis=0, tiled=True
    )
    attn_rows = jnp.sum(partial_parts.astype(jnp.float32), axis=0)
    own_tokens = lax.dynamic_slice_in_dim(tokens, kv_index * sub_rows, sub_rows, 0)
    residual = (own_tokens.astype(jnp.float32) + attn_rows).astype(jnp.bfloat16)
    normed_ffn = rms_norm(residual, ffn_gain)
    logits = jnp.dot(normed_ffn, router, preferred_element_type=jnp.float32)
    chosen = jnp.take_along_axis(logits, routes, axis=1)
    sigmoid_vals = jax.nn.sigmoid(chosen)
    gates = sigmoid_vals / jnp.sum(sigmoid_vals, axis=1, keepdims=True)
    experts_all = router.shape[1]
    local_experts = gate_up.shape[0]
    capacity = max(2, 2 * sub_rows // experts_all + 1)
    flat_routes = routes.reshape(-1)
    onehot_int = (flat_routes[:, None] == jnp.arange(experts_all, dtype=jnp.int32)[None, :]).astype(
        jnp.int32
    )
    earlier = jnp.cumsum(onehot_int, axis=0) - onehot_int
    rank_in = jnp.sum(earlier * onehot_int, axis=1)
    place_at = (
        flat_routes // local_experts * capacity * local_experts
        + rank_in * local_experts
        + flat_routes % local_experts
    )
    placement_plan = (
        place_at[:, None] == jnp.arange(experts_all * capacity, dtype=jnp.int32)[None, :]
    ).astype(jnp.bfloat16)
    paired_rows = jnp.repeat(normed_ffn, 2, axis=0)
    outgoing = jnp.einsum(
        "qe,qd->ed", placement_plan, paired_rows, preferred_element_type=jnp.float32
    )
    outgoing = outgoing.astype(jnp.bfloat16).reshape(n_req, capacity, local_experts, width)
    arrived = lax.all_to_all(outgoing, "req", split_axis=0, concat_axis=0, tiled=True)
    returned = lax.all_to_all(
        expert_apply(arrived, gate_up, down), "req", split_axis=0, concat_axis=0, tiled=True
    )
    back_rows = returned.reshape(experts_all * capacity, width)
    paired_output = jnp.dot(placement_plan, back_rows, preferred_element_type=jnp.float32).reshape(
        sub_rows, 2, width
    )
    mixed = residual.astype(jnp.float32) + jnp.sum(gates[:, :, None] * paired_output, axis=1)
    return mixed.astype(jnp.bfloat16)


def solution(mesh):
    in_specs = (
        P("req", "kv"),
        P(),
        P("req"),
        P("req", None),
        P("req", "kv", None, None),
        P(),
        P("kv", None, None),
        P("kv", None, None),
        P(),
        P(),
        P(("req", "kv"), None),
        P("req", None, None),
        P("req", None, None),
    )
    out_specs = P(("req", "kv"), None)
    return jax.shard_map(shards, mesh=mesh, in_specs=in_specs, out_specs=out_specs, check_vma=False)
```

```python
import jax
import jax.numpy as jnp
from jax import lax
from jax.sharding import PartitionSpec as P

REQ_DEV = 64


NEG_FILL = -1e30
EPS_NORM = 1e-05


def rms_norm(values, gain_vec):
    values = values.astype(jnp.float32)
    factor = lax.rsqrt(jnp.mean(values * values, axis=-1, keepdims=True) + EPS_NORM)
    return (values * factor * gain_vec).astype(jnp.bfloat16)


def attend(normed, seq_lens, page_table, kv_cache, qkv_weight):
    pool_pages, local_heads, twice_hd, page_len = kv_cache.shape
    head_dim = twice_hd // 2
    slot_count = normed.shape[0]
    groups = qkv_weight.shape[2] // head_dim - 2
    max_pages = page_table.shape[1]
    projected = jnp.einsum("sd,hdc->shc", normed, qkv_weight, preferred_element_type=jnp.float32)
    queries = (
        projected[:, :, : groups * head_dim]
        .reshape(slot_count, local_heads, groups, head_dim)
        .astype(jnp.bfloat16)
    )
    key_new = projected[:, :, groups * head_dim : (groups + 1) * head_dim].astype(jnp.bfloat16)
    value_new = projected[:, :, (groups + 1) * head_dim :].astype(jnp.bfloat16)
    page_need = (seq_lens + page_len - 1) // page_len
    page_ids = jnp.arange(max_pages, dtype=jnp.int32)
    in_use = page_ids[None, :] < page_need[:, None]
    pool_ids = jnp.arange(pool_pages, dtype=jnp.int32)
    entry_slot = jnp.broadcast_to(
        jnp.arange(slot_count, dtype=jnp.int32)[:, None], (slot_count, max_pages)
    ).reshape(-1)
    entry_page = jnp.where(in_use, page_table, -1).reshape(-1)
    entry_order = jnp.broadcast_to(page_ids[None, :], (slot_count, max_pages)).reshape(-1)
    entry_len = jnp.broadcast_to(seq_lens[:, None], (slot_count, max_pages)).reshape(-1)
    len_unit = 64
    facts = jnp.concatenate(
        [
            (entry_slot[None, :] == jnp.arange(slot_count, dtype=jnp.int32)[:, None]).astype(jnp.float32),
            entry_order[None, :].astype(jnp.float32),
            (entry_len // len_unit)[None, :].astype(jnp.float32),
            (entry_len % len_unit)[None, :].astype(jnp.float32),
        ],
        axis=0,
    ).astype(jnp.bfloat16)
    entry_hit = (entry_page[:, None] == pool_ids[None, :]).astype(jnp.bfloat16)
    page_facts = jnp.dot(facts, entry_hit, preferred_element_type=jnp.float32)
    belongs = page_facts[:slot_count] > 0.5
    page_order = page_facts[slot_count].astype(jnp.int32)
    owner_len = (
        page_facts[slot_count + 1].astype(jnp.int32) * len_unit
        + page_facts[slot_count + 2].astype(jnp.int32)
    )
    position = page_order[:, None] * page_len + jnp.arange(page_len, dtype=jnp.int32)[None, :]
    live = position < owner_len[:, None]
    scale_factor = head_dim ** (-0.5)
    page_queries = jnp.einsum(
        "sp,skgd->pkgd", belongs.astype(jnp.bfloat16), queries, preferred_element_type=jnp.float32
    ).astype(jnp.bfloat16)
    scores = (
        jnp.einsum(
            "pkgd,pkdt->pkgt",
            page_queries,
            kv_cache[:, :, :head_dim, :],
            preferred_element_type=jnp.float32,
        )
        * scale_factor
    )
    scores = jnp.where(live[:, None, None, :], scores, NEG_FILL)
    score_new = (
        jnp.einsum("skgd,skd->skg", queries, key_new, preferred_element_type=jnp.float32)
        * scale_factor
    )
    page_peak = jnp.max(scores, axis=3)
    slot_peak = jnp.max(jnp.where(belongs[:, :, None, None], page_peak[None], NEG_FILL), axis=1)
    slot_peak = jnp.maximum(slot_peak, score_new)
    page_peak_of_owner = jnp.max(
        jnp.where(belongs[:, :, None, None], slot_peak[:, None], NEG_FILL), axis=0
    )
    weights = jnp.where(
        live[:, None, None, :],
        jnp.exp(scores - page_peak_of_owner[..., None]),
        0.0,
    )
    page_total = jnp.sum(weights, axis=3)
    page_value = jnp.einsum(
        "pkgt,pkdt->pkgd",
        weights.astype(jnp.bfloat16),
        kv_cache[:, :, head_dim:, :],
        preferred_element_type=jnp.float32,
    )
    belongs_f = belongs.astype(jnp.float32)
    total_sum = jnp.einsum("sp,pkg->skg", belongs_f, page_total, precision=lax.Precision.HIGHEST)
    value_sum = jnp.einsum(
        "sp,pkgd->skgd", belongs_f, page_value, precision=lax.Precision.HIGHEST
    )
    weight_new = jnp.exp(score_new - slot_peak)
    total_sum = total_sum + weight_new
    rounded_new = lax.optimization_barrier(weight_new.astype(jnp.bfloat16)).astype(jnp.float32)
    value_sum = value_sum + rounded_new[..., None] * value_new.astype(jnp.float32)[:, :, None, :]
    return (value_sum / total_sum[..., None]).astype(jnp.bfloat16).reshape(slot_count, -1)


def expert_apply(piece, gate_up, down):
    n_source, slot_num, local_experts, width = piece.shape
    rows_in = piece.transpose(2, 0, 1, 3).reshape(local_experts, n_source * slot_num, width)
    projected_up = jnp.einsum("erd,edf->erf", rows_in, gate_up, preferred_element_type=jnp.float32)
    hidden_units = gate_up.shape[2] // 2
    acts = (
        jax.nn.silu(projected_up[..., :hidden_units]) * projected_up[..., hidden_units:]
    ).astype(jnp.bfloat16)
    result = jnp.einsum("erf,efd->erd", acts, down, preferred_element_type=jnp.float32).astype(
        jnp.bfloat16
    )
    return result.reshape(local_experts, n_source, slot_num, width).transpose(1, 2, 0, 3)


def shards(
    hidden,
    perm,
    seq_lens,
    page_table,
    kv_cache,
    attn_gain,
    qkv_weight,
    out_weight,
    ffn_gain,
    router,
    routes,
    gate_up,
    down,
):
    req_index = lax.axis_index("req")
    kv_index = lax.axis_index("kv")
    n_req = lax.axis_size("req")
    n_kv = lax.axis_size("kv")
    local_rows, col_width = hidden.shape
    width = n_kv * col_width
    spread = jnp.broadcast_to(hidden[:, None], (local_rows, n_kv, col_width))
    block_rows = lax.all_to_all(spread, "kv", split_axis=1, concat_axis=1, tiled=True).reshape(
        local_rows, width
    )
    deal = local_rows // n_req
    source_block = (perm // local_rows).reshape(n_req, local_rows)
    source_row = (perm % local_rows).reshape(n_req, local_rows)
    mine = source_block == req_index
    rank_sent = jnp.cumsum(mine.astype(jnp.int32), axis=1) - 1
    send_key = jnp.where(mine, rank_sent * local_rows + source_row, -1)
    send_ids = jnp.arange(deal * local_rows, dtype=jnp.int32)
    send_pick = jnp.any(send_key[:, :, None] == send_ids[None, None, :], axis=1)
    send_pick = send_pick.reshape(n_req * deal, local_rows).astype(hidden.dtype)
    outgoing_rows = jnp.dot(send_pick, block_rows, preferred_element_type=jnp.float32).astype(
        hidden.dtype
    )
    arrived_rows = lax.all_to_all(
        outgoing_rows.reshape(n_req, deal, width), "req", split_axis=0, concat_axis=0, tiled=True
    ).reshape(n_req * deal, width)
    my_source = lax.dynamic_slice_in_dim(perm, req_index * local_rows, local_rows) // local_rows
    slot_ids = jnp.arange(local_rows, dtype=jnp.int32)
    same_before = (my_source[None, :] == my_source[:, None]) & (slot_ids[None, :] < slot_ids[:, None])
    rank_got = jnp.sum(same_before.astype(jnp.int32), axis=1)
    take_key = my_source * deal + rank_got
    take_pick = (take_key[:, None] == slot_ids[None, :]).astype(hidden.dtype)
    tokens = jnp.dot(take_pick, arrived_rows, preferred_element_type=jnp.float32).astype(
        hidden.dtype
    )
    normed = rms_norm(tokens, attn_gain)
    head_out = attend(normed, seq_lens, page_table, kv_cache, qkv_weight)
    sub_rows = routes.shape[0]
    width = n_kv * col_width
    out_flat = out_weight.reshape(-1, out_weight.shape[2])
    partial = jnp.dot(head_out, out_flat, preferred_element_type=jnp.float32).astype(jnp.bfloat16)
    partial_parts = lax.all_to_all(
        partial.reshape(n_kv, sub_rows, partial.shape[1]), "kv", split_axis=0, concat_axis=0, tiled=True
    )
    attn_rows = jnp.sum(partial_parts.astype(jnp.float32), axis=0)
    own_tokens = lax.dynamic_slice_in_dim(tokens, kv_index * sub_rows, sub_rows, 0)
    residual = (own_tokens.astype(jnp.float32) + attn_rows).astype(jnp.bfloat16)
    normed_ffn = rms_norm(residual, ffn_gain)
    logits = jnp.dot(normed_ffn, router, preferred_element_type=jnp.float32)
    chosen = jnp.take_along_axis(logits, routes, axis=1)
    sigmoid_vals = jax.nn.sigmoid(chosen)
    gates = sigmoid_vals / jnp.sum(sigmoid_vals, axis=1, keepdims=True)
    experts_all = router.shape[1]
    local_experts = gate_up.shape[0]
    capacity = max(2, 2 * sub_rows // experts_all + 1)
    flat_routes = routes.reshape(-1)
    onehot_int = (flat_routes[:, None] == jnp.arange(experts_all, dtype=jnp.int32)[None, :]).astype(
        jnp.int32
    )
    earlier = jnp.cumsum(onehot_int, axis=0) - onehot_int
    rank_in = jnp.sum(earlier * onehot_int, axis=1)
    place_at = (
        flat_routes // local_experts * capacity * local_experts
        + rank_in * local_experts
        + flat_routes % local_experts
    )
    placement_plan = (
        place_at[:, None] == jnp.arange(experts_all * capacity, dtype=jnp.int32)[None, :]
    ).astype(jnp.bfloat16)
    paired_rows = jnp.repeat(normed_ffn, 2, axis=0)
    outgoing = jnp.einsum(
        "qe,qd->ed", placement_plan, paired_rows, preferred_element_type=jnp.float32
    )
    outgoing = outgoing.astype(jnp.bfloat16).reshape(n_req, capacity * local_experts, width)
    arrived = lax.all_to_all(outgoing, "req", split_axis=0, concat_axis=0, tiled=True)
    expert_rows = expert_apply(
        arrived.reshape(n_req, capacity, local_experts, width), gate_up, down
    ).reshape(n_req, capacity * local_experts, width)
    returned = lax.all_to_all(expert_rows, "req", split_axis=0, concat_axis=0, tiled=True)
    back_rows = returned.reshape(experts_all * capacity, width)
    paired_output = jnp.dot(placement_plan, back_rows, preferred_element_type=jnp.float32).reshape(
        sub_rows, 2, width
    )
    mixed = residual.astype(jnp.float32) + jnp.sum(gates[:, :, None] * paired_output, axis=1)
    return mixed.astype(jnp.bfloat16)


def solution(mesh):
    in_specs = (
        P("req", "kv"),
        P(),
        P("req"),
        P("req", None),
        P("req", "kv", None, None),
        P(),
        P("kv", None, None),
        P("kv", None, None),
        P(),
        P(),
        P(("req", "kv"), None),
        P("req", None, None),
        P("req", None, None),
    )
    out_specs = P(("req", "kv"), None)
    return jax.shard_map(shards, mesh=mesh, in_specs=in_specs, out_specs=out_specs, check_vma=False)
```

```python
import jax
import jax.numpy as jnp
from jax import lax
from jax.sharding import PartitionSpec as P

REQ_DEV = 64


NEG_FILL = -1e30
EPS_NORM = 1e-05


def rms_norm(values, gain_vec):
    values = values.astype(jnp.float32)
    factor = lax.rsqrt(jnp.mean(values * values, axis=-1, keepdims=True) + EPS_NORM)
    return (values * factor * gain_vec).astype(jnp.bfloat16)


def attend(normed, seq_lens, page_table, kv_cache, qkv_weight):
    pool_pages, local_heads, twice_hd, page_len = kv_cache.shape
    head_dim = twice_hd // 2
    slot_count = normed.shape[0]
    groups = qkv_weight.shape[2] // head_dim - 2
    max_pages = page_table.shape[1]
    projected = jnp.einsum("sd,hdc->shc", normed, qkv_weight, preferred_element_type=jnp.float32)
    queries = (
        projected[:, :, : groups * head_dim]
        .reshape(slot_count, local_heads, groups, head_dim)
        .astype(jnp.bfloat16)
    )
    key_new = projected[:, :, groups * head_dim : (groups + 1) * head_dim].astype(jnp.bfloat16)
    value_new = projected[:, :, (groups + 1) * head_dim :].astype(jnp.bfloat16)
    page_need = (seq_lens + page_len - 1) // page_len
    page_ids = jnp.arange(max_pages, dtype=jnp.int32)
    in_use = page_ids[None, :] < page_need[:, None]
    pool_ids = jnp.arange(pool_pages, dtype=jnp.int32)
    entry_slot = jnp.broadcast_to(
        jnp.arange(slot_count, dtype=jnp.int32)[:, None], (slot_count, max_pages)
    ).reshape(-1)
    entry_page = jnp.where(in_use, page_table, -1).reshape(-1)
    entry_order = jnp.broadcast_to(page_ids[None, :], (slot_count, max_pages)).reshape(-1)
    entry_len = jnp.broadcast_to(seq_lens[:, None], (slot_count, max_pages)).reshape(-1)
    len_unit = 64
    facts = jnp.concatenate(
        [
            (entry_slot[None, :] == jnp.arange(slot_count, dtype=jnp.int32)[:, None]).astype(jnp.float32),
            entry_order[None, :].astype(jnp.float32),
            (entry_len // len_unit)[None, :].astype(jnp.float32),
            (entry_len % len_unit)[None, :].astype(jnp.float32),
        ],
        axis=0,
    ).astype(jnp.bfloat16)
    entry_hit = (entry_page[:, None] == pool_ids[None, :]).astype(jnp.bfloat16)
    page_facts = jnp.dot(facts, entry_hit, preferred_element_type=jnp.float32)
    belongs = page_facts[:slot_count] > 0.5
    page_order = page_facts[slot_count].astype(jnp.int32)
    owner_len = (
        page_facts[slot_count + 1].astype(jnp.int32) * len_unit
        + page_facts[slot_count + 2].astype(jnp.int32)
    )
    position = page_order[:, None] * page_len + jnp.arange(page_len, dtype=jnp.int32)[None, :]
    live = position < owner_len[:, None]
    scale_factor = head_dim ** (-0.5)
    page_queries = jnp.einsum(
        "sp,skgd->pkgd", belongs.astype(jnp.bfloat16), queries, preferred_element_type=jnp.float32
    ).astype(jnp.bfloat16)
    scores = (
        jnp.einsum(
            "pkgd,pkdt->pkgt",
            page_queries,
            kv_cache[:, :, :head_dim, :],
            preferred_element_type=jnp.float32,
        )
        * scale_factor
    )
    scores = jnp.where(live[:, None, None, :], scores, NEG_FILL)
    score_new = (
        jnp.einsum("skgd,skd->skg", queries, key_new, preferred_element_type=jnp.float32)
        * scale_factor
    )
    page_peak = jnp.max(scores, axis=3)
    slot_peak = jnp.max(jnp.where(belongs[:, :, None, None], page_peak[None], NEG_FILL), axis=1)
    slot_peak = jnp.maximum(slot_peak, score_new)
    page_peak_of_owner = jnp.max(
        jnp.where(belongs[:, :, None, None], slot_peak[:, None], NEG_FILL), axis=0
    )
    weights = jnp.where(
        live[:, None, None, :],
        jnp.exp(scores - page_peak_of_owner[..., None]),
        0.0,
    )
    page_total = jnp.sum(weights, axis=3)
    page_value = jnp.einsum(
        "pkgt,pkdt->pkgd",
        weights.astype(jnp.bfloat16),
        kv_cache[:, :, head_dim:, :],
        preferred_element_type=jnp.float32,
    )
    belongs_f = belongs.astype(jnp.float32)
    total_sum = jnp.einsum("sp,pkg->skg", belongs_f, page_total, precision=lax.Precision.HIGHEST)
    value_sum = jnp.einsum(
        "sp,pkgd->skgd", belongs_f, page_value, precision=lax.Precision.HIGHEST
    )
    weight_new = jnp.exp(score_new - slot_peak)
    total_sum = total_sum + weight_new
    rounded_new = lax.optimization_barrier(weight_new.astype(jnp.bfloat16)).astype(jnp.float32)
    value_sum = value_sum + rounded_new[..., None] * value_new.astype(jnp.float32)[:, :, None, :]
    return (value_sum / total_sum[..., None]).astype(jnp.bfloat16).reshape(slot_count, -1)


def expert_apply(piece, gate_up, down):
    n_source, slot_num, local_experts, width = piece.shape
    rows_in = piece.transpose(2, 0, 1, 3).reshape(local_experts, n_source * slot_num, width)
    projected_up = jnp.einsum("erd,edf->erf", rows_in, gate_up, preferred_element_type=jnp.float32)
    hidden_units = gate_up.shape[2] // 2
    acts = (
        jax.nn.silu(projected_up[..., :hidden_units]) * projected_up[..., hidden_units:]
    ).astype(jnp.bfloat16)
    result = jnp.einsum("erf,efd->erd", acts, down, preferred_element_type=jnp.float32).astype(
        jnp.bfloat16
    )
    return result.reshape(local_experts, n_source, slot_num, width).transpose(1, 2, 0, 3)


def shards(
    hidden,
    perm,
    seq_lens,
    page_table,
    kv_cache,
    attn_gain,
    qkv_weight,
    out_weight,
    ffn_gain,
    router,
    routes,
    gate_up,
    down,
):
    req_index = lax.axis_index("req")
    kv_index = lax.axis_index("kv")
    n_req = lax.axis_size("req")
    n_kv = lax.axis_size("kv")
    local_rows, col_width = hidden.shape
    width = n_kv * col_width
    spread = jnp.broadcast_to(hidden[:, None], (local_rows, n_kv, col_width))
    block_rows = lax.all_to_all(spread, "kv", split_axis=1, concat_axis=1, tiled=True).reshape(
        local_rows, width
    )
    deal = local_rows // n_req
    source_block = (perm // local_rows).reshape(n_req, local_rows)
    source_row = (perm % local_rows).reshape(n_req, local_rows)
    mine = source_block == req_index
    rank_sent = jnp.cumsum(mine.astype(jnp.int32), axis=1) - 1
    send_key = jnp.where(mine, rank_sent * local_rows + source_row, -1)
    send_ids = jnp.arange(deal * local_rows, dtype=jnp.int32)
    send_pick = jnp.any(send_key[:, :, None] == send_ids[None, None, :], axis=1)
    send_pick = send_pick.reshape(n_req, deal, local_rows).astype(hidden.dtype)
    outgoing_rows = jnp.einsum(
        "dir,rc->dic", send_pick, block_rows, preferred_element_type=jnp.float32
    ).astype(hidden.dtype)
    arrived_rows = lax.all_to_all(outgoing_rows, "req", split_axis=0, concat_axis=0, tiled=True)
    my_source = lax.dynamic_slice_in_dim(perm, req_index * local_rows, local_rows) // local_rows
    slot_ids = jnp.arange(local_rows, dtype=jnp.int32)
    same_before = (my_source[None, :] == my_source[:, None]) & (slot_ids[None, :] < slot_ids[:, None])
    rank_got = jnp.sum(same_before.astype(jnp.int32), axis=1)
    take_key = my_source * deal + rank_got
    take_pick = (take_key[:, None] == slot_ids[None, :]).astype(hidden.dtype)
    tokens = jnp.einsum(
        "sri,ric->sc", take_pick.reshape(local_rows, n_req, deal), arrived_rows,
        preferred_element_type=jnp.float32,
    ).astype(hidden.dtype)
    normed = rms_norm(tokens, attn_gain)
    head_out = attend(normed, seq_lens, page_table, kv_cache, qkv_weight)
    sub_rows = routes.shape[0]
    width = n_kv * col_width
    out_flat = out_weight.reshape(-1, out_weight.shape[2])
    partial = jnp.dot(head_out, out_flat, preferred_element_type=jnp.float32).astype(jnp.bfloat16)
    partial_parts = lax.all_to_all(
        partial.reshape(n_kv, sub_rows, partial.shape[1]), "kv", split_axis=0, concat_axis=0, tiled=True
    )
    attn_rows = jnp.sum(partial_parts.astype(jnp.float32), axis=0)
    own_tokens = lax.dynamic_slice_in_dim(tokens, kv_index * sub_rows, sub_rows, 0)
    residual = (own_tokens.astype(jnp.float32) + attn_rows).astype(jnp.bfloat16)
    normed_ffn = rms_norm(residual, ffn_gain)
    logits = jnp.dot(normed_ffn, router, preferred_element_type=jnp.float32)
    expert_ids = jnp.arange(logits.shape[1], dtype=jnp.int32)
    chosen = jnp.sum(
        jnp.where(routes[:, :, None] == expert_ids[None, None, :], logits[:, None, :], 0.0), axis=2
    )
    sigmoid_vals = jax.nn.sigmoid(chosen)
    gates = sigmoid_vals / jnp.sum(sigmoid_vals, axis=1, keepdims=True)
    experts_all = router.shape[1]
    local_experts = gate_up.shape[0]
    capacity = max(2, 2 * sub_rows // experts_all + 1)
    flat_routes = routes.reshape(-1)
    onehot_int = (flat_routes[:, None] == jnp.arange(experts_all, dtype=jnp.int32)[None, :]).astype(
        jnp.int32
    )
    earlier = jnp.cumsum(onehot_int, axis=0) - onehot_int
    rank_in = jnp.sum(earlier * onehot_int, axis=1)
    place_at = (
        flat_routes // local_experts * capacity * local_experts
        + rank_in * local_experts
        + flat_routes % local_experts
    )
    slots_per_dest = capacity * local_experts
    dest_slot = (
        jnp.arange(n_req, dtype=jnp.int32)[:, None] * slots_per_dest
        + jnp.arange(slots_per_dest, dtype=jnp.int32)[None, :]
    )
    placement_plan = (
        place_at.reshape(sub_rows, 2)[:, :, None, None] == dest_slot[None, None, :, :]
    ).astype(jnp.bfloat16)
    outgoing = jnp.einsum(
        "rjnc,rd->ncd", placement_plan, normed_ffn, preferred_element_type=jnp.float32
    ).astype(jnp.bfloat16)
    arrived = lax.all_to_all(outgoing, "req", split_axis=0, concat_axis=0, tiled=True)
    expert_rows = expert_apply(
        arrived.reshape(n_req, capacity, local_experts, width), gate_up, down
    ).reshape(n_req, slots_per_dest, width)
    returned = lax.all_to_all(expert_rows, "req", split_axis=0, concat_axis=0, tiled=True)
    paired_output = jnp.einsum(
        "rjnc,ncd->rjd", placement_plan, returned, preferred_element_type=jnp.float32
    )
    mixed = residual.astype(jnp.float32) + jnp.sum(gates[:, :, None] * paired_output, axis=1)
    return mixed.astype(jnp.bfloat16)


def solution(mesh):
    in_specs = (
        P("req", "kv"),
        P(),
        P("req"),
        P("req", None),
        P("req", "kv", None, None),
        P(),
        P("kv", None, None),
        P("kv", None, None),
        P(),
        P(),
        P(("req", "kv"), None),
        P("req", None, None),
        P("req", None, None),
    )
    out_specs = P(("req", "kv"), None)
    return jax.shard_map(shards, mesh=mesh, in_specs=in_specs, out_specs=out_specs, check_vma=False)
```

```python
import jax
import jax.numpy as jnp
from jax import lax
from jax.sharding import PartitionSpec as P

REQ_DEV = 64


NEG_FILL = -1e30
EPS_NORM = 1e-05


def rms_norm(values, gain_vec):
    values = values.astype(jnp.float32)
    factor = lax.rsqrt(jnp.mean(values * values, axis=-1, keepdims=True) + EPS_NORM)
    return (values * factor * gain_vec).astype(jnp.bfloat16)


def attend(normed, seq_lens, page_table, kv_cache, qkv_weight):
    pool_pages, local_heads, twice_hd, page_len = kv_cache.shape
    head_dim = twice_hd // 2
    slot_count = normed.shape[0]
    groups = qkv_weight.shape[2] // head_dim - 2
    max_pages = page_table.shape[1]
    projected = jnp.einsum("sd,hdc->shc", normed, qkv_weight, preferred_element_type=jnp.float32)
    queries = (
        projected[:, :, : groups * head_dim]
        .reshape(slot_count, local_heads, groups, head_dim)
        .astype(jnp.bfloat16)
    )
    key_new = projected[:, :, groups * head_dim : (groups + 1) * head_dim].astype(jnp.bfloat16)
    value_new = projected[:, :, (groups + 1) * head_dim :].astype(jnp.bfloat16)
    page_need = (seq_lens + page_len - 1) // page_len
    page_ids = jnp.arange(max_pages, dtype=jnp.int32)
    in_use = page_ids[None, :] < page_need[:, None]
    pool_ids = jnp.arange(pool_pages, dtype=jnp.int32)
    entry_slot = jnp.broadcast_to(
        jnp.arange(slot_count, dtype=jnp.int32)[:, None], (slot_count, max_pages)
    ).reshape(-1)
    entry_page = jnp.where(in_use, page_table, -1).reshape(-1)
    entry_order = jnp.broadcast_to(page_ids[None, :], (slot_count, max_pages)).reshape(-1)
    entry_len = jnp.broadcast_to(seq_lens[:, None], (slot_count, max_pages)).reshape(-1)
    len_unit = 64
    facts = jnp.concatenate(
        [
            (entry_slot[None, :] == jnp.arange(slot_count, dtype=jnp.int32)[:, None]).astype(jnp.float32),
            entry_order[None, :].astype(jnp.float32),
            (entry_len // len_unit)[None, :].astype(jnp.float32),
            (entry_len % len_unit)[None, :].astype(jnp.float32),
        ],
        axis=0,
    ).astype(jnp.bfloat16)
    entry_hit = (entry_page[:, None] == pool_ids[None, :]).astype(jnp.bfloat16)
    page_facts = jnp.dot(facts, entry_hit, preferred_element_type=jnp.float32)
    belongs = page_facts[:slot_count] > 0.5
    page_order = page_facts[slot_count].astype(jnp.int32)
    owner_len = (
        page_facts[slot_count + 1].astype(jnp.int32) * len_unit
        + page_facts[slot_count + 2].astype(jnp.int32)
    )
    position = page_order[:, None] * page_len + jnp.arange(page_len, dtype=jnp.int32)[None, :]
    live = position < owner_len[:, None]
    scale_factor = head_dim ** (-0.5)
    page_queries = jnp.einsum(
        "sp,skgd->pkgd", belongs.astype(jnp.bfloat16), queries, preferred_element_type=jnp.float32
    ).astype(jnp.bfloat16)
    scores = (
        jnp.einsum(
            "pkgd,pkdt->pkgt",
            page_queries,
            kv_cache[:, :, :head_dim, :],
            preferred_element_type=jnp.float32,
        )
        * scale_factor
    )
    scores = jnp.where(live[:, None, None, :], scores, NEG_FILL)
    score_new = (
        jnp.einsum("skgd,skd->skg", queries, key_new, preferred_element_type=jnp.float32)
        * scale_factor
    )
    page_peak = jnp.max(scores, axis=3)
    slot_peak = jnp.max(jnp.where(belongs[:, :, None, None], page_peak[None], NEG_FILL), axis=1)
    slot_peak = jnp.maximum(slot_peak, score_new)
    page_peak_of_owner = jnp.max(
        jnp.where(belongs[:, :, None, None], slot_peak[:, None], NEG_FILL), axis=0
    )
    weights = jnp.where(
        live[:, None, None, :],
        jnp.exp(scores - page_peak_of_owner[..., None]),
        0.0,
    )
    page_total = jnp.sum(weights, axis=3)
    page_value = jnp.einsum(
        "pkgt,pkdt->pkgd",
        weights.astype(jnp.bfloat16),
        kv_cache[:, :, head_dim:, :],
        preferred_element_type=jnp.float32,
    )
    belongs_f = belongs.astype(jnp.float32)
    total_sum = jnp.einsum("sp,pkg->skg", belongs_f, page_total, precision=lax.Precision.HIGHEST)
    value_sum = jnp.einsum(
        "sp,pkgd->skgd", belongs_f, page_value, precision=lax.Precision.HIGHEST
    )
    weight_new = jnp.exp(score_new - slot_peak)
    total_sum = total_sum + weight_new
    rounded_new = lax.optimization_barrier(weight_new.astype(jnp.bfloat16)).astype(jnp.float32)
    value_sum = value_sum + rounded_new[..., None] * value_new.astype(jnp.float32)[:, :, None, :]
    return (value_sum / total_sum[..., None]).astype(jnp.bfloat16).reshape(slot_count, -1)


def expert_apply(piece, gate_up, down):
    n_source, slot_num, local_experts, width = piece.shape
    rows_in = piece.transpose(2, 0, 1, 3).reshape(local_experts, n_source * slot_num, width)
    projected_up = jnp.einsum("erd,edf->erf", rows_in, gate_up, preferred_element_type=jnp.float32)
    hidden_units = gate_up.shape[2] // 2
    acts = (
        jax.nn.silu(projected_up[..., :hidden_units]) * projected_up[..., hidden_units:]
    ).astype(jnp.bfloat16)
    result = jnp.einsum("erf,efd->erd", acts, down, preferred_element_type=jnp.float32).astype(
        jnp.bfloat16
    )
    return result.reshape(local_experts, n_source, slot_num, width).transpose(1, 2, 0, 3)


def shards(
    hidden,
    perm,
    seq_lens,
    page_table,
    kv_cache,
    attn_gain,
    qkv_weight,
    out_weight,
    ffn_gain,
    router,
    routes,
    gate_up,
    down,
):
    req_index = lax.axis_index("req")
    kv_index = lax.axis_index("kv")
    n_req = lax.axis_size("req")
    n_kv = lax.axis_size("kv")
    local_rows, col_width = hidden.shape
    width = n_kv * col_width
    spread = jnp.broadcast_to(hidden[None], (n_kv, local_rows, col_width))
    block_parts = lax.all_to_all(spread, "kv", split_axis=0, concat_axis=0, tiled=True)
    deal = local_rows // n_req
    source_block = (perm // local_rows).reshape(n_req, local_rows)
    source_row = (perm % local_rows).reshape(n_req, local_rows)
    mine = source_block == req_index
    rank_sent = jnp.cumsum(mine.astype(jnp.int32), axis=1) - 1
    send_key = jnp.where(mine, rank_sent * local_rows + source_row, -1)
    send_ids = jnp.arange(deal * local_rows, dtype=jnp.int32)
    send_pick = jnp.any(send_key[:, :, None] == send_ids[None, None, :], axis=1)
    send_pick = send_pick.reshape(n_req, deal, local_rows).astype(hidden.dtype)
    outgoing_rows = jnp.einsum(
        "dir,jrc->dijc", send_pick, block_parts, preferred_element_type=jnp.float32
    ).astype(hidden.dtype)
    arrived_rows = lax.all_to_all(
        outgoing_rows.reshape(n_req, deal, width), "req", split_axis=0, concat_axis=0, tiled=True
    ).reshape(n_req * deal, width)
    my_source = lax.dynamic_slice_in_dim(perm, req_index * local_rows, local_rows) // local_rows
    slot_ids = jnp.arange(local_rows, dtype=jnp.int32)
    same_before = (my_source[None, :] == my_source[:, None]) & (slot_ids[None, :] < slot_ids[:, None])
    rank_got = jnp.sum(same_before.astype(jnp.int32), axis=1)
    take_key = my_source * deal + rank_got
    take_pick = (take_key[:, None] == slot_ids[None, :]).astype(hidden.dtype)
    tokens = jnp.dot(take_pick, arrived_rows, preferred_element_type=jnp.float32).astype(
        hidden.dtype
    )
    normed = rms_norm(tokens, attn_gain)
    head_out = attend(normed, seq_lens, page_table, kv_cache, qkv_weight)
    sub_rows = routes.shape[0]
    width = n_kv * col_width
    out_flat = out_weight.reshape(-1, out_weight.shape[2])
    partial = jnp.dot(head_out, out_flat, preferred_element_type=jnp.float32).astype(jnp.bfloat16)
    partial_parts = lax.all_to_all(
        partial.reshape(n_kv, sub_rows, partial.shape[1]), "kv", split_axis=0, concat_axis=0, tiled=True
    )
    attn_rows = jnp.sum(partial_parts.astype(jnp.float32), axis=0)
    own_tokens = lax.dynamic_slice_in_dim(tokens, kv_index * sub_rows, sub_rows, 0)
    residual = (own_tokens.astype(jnp.float32) + attn_rows).astype(jnp.bfloat16)
    normed_ffn = rms_norm(residual, ffn_gain)
    logits = jnp.dot(normed_ffn, router, preferred_element_type=jnp.float32)
    chosen = jnp.take_along_axis(logits, routes, axis=1)
    sigmoid_vals = jax.nn.sigmoid(chosen)
    gates = sigmoid_vals / jnp.sum(sigmoid_vals, axis=1, keepdims=True)
    experts_all = router.shape[1]
    local_experts = gate_up.shape[0]
    capacity = max(2, 2 * sub_rows // experts_all + 1)
    flat_routes = routes.reshape(-1)
    onehot_int = (flat_routes[:, None] == jnp.arange(experts_all, dtype=jnp.int32)[None, :]).astype(
        jnp.int32
    )
    earlier = jnp.cumsum(onehot_int, axis=0) - onehot_int
    rank_in = jnp.sum(earlier * onehot_int, axis=1)
    place_at = (
        flat_routes // local_experts * capacity * local_experts
        + rank_in * local_experts
        + flat_routes % local_experts
    )
    placement_plan = (
        place_at[:, None] == jnp.arange(experts_all * capacity, dtype=jnp.int32)[None, :]
    ).astype(jnp.bfloat16)
    paired_rows = jnp.repeat(normed_ffn, 2, axis=0)
    outgoing = jnp.einsum(
        "qe,qd->ed", placement_plan, paired_rows, preferred_element_type=jnp.float32
    )
    outgoing = outgoing.astype(jnp.bfloat16).reshape(n_req, capacity * local_experts, width)
    arrived = lax.all_to_all(outgoing, "req", split_axis=0, concat_axis=0, tiled=True)
    expert_rows = expert_apply(
        arrived.reshape(n_req, capacity, local_experts, width), gate_up, down
    ).reshape(n_req, capacity * local_experts, width)
    returned = lax.all_to_all(expert_rows, "req", split_axis=0, concat_axis=0, tiled=True)
    back_rows = returned.reshape(experts_all * capacity, width)
    paired_output = jnp.dot(placement_plan, back_rows, preferred_element_type=jnp.float32).reshape(
        sub_rows, 2, width
    )
    mixed = residual.astype(jnp.float32) + jnp.sum(gates[:, :, None] * paired_output, axis=1)
    return mixed.astype(jnp.bfloat16)


def solution(mesh):
    in_specs = (
        P("req", "kv"),
        P(),
        P("req"),
        P("req", None),
        P("req", "kv", None, None),
        P(),
        P("kv", None, None),
        P("kv", None, None),
        P(),
        P(),
        P(("req", "kv"), None),
        P("req", None, None),
        P("req", None, None),
    )
    out_specs = P(("req", "kv"), None)
    return jax.shard_map(shards, mesh=mesh, in_specs=in_specs, out_specs=out_specs, check_vma=False)
```

```python
import jax
import jax.numpy as jnp
from jax import lax
from jax.sharding import PartitionSpec as P

REQ_DEV = 64


NEG_FILL = -1e30
EPS_NORM = 1e-05


def rms_norm(values, gain_vec):
    values = values.astype(jnp.float32)
    factor = lax.rsqrt(jnp.mean(values * values, axis=-1, keepdims=True) + EPS_NORM)
    return (values * factor * gain_vec).astype(jnp.bfloat16)


def attend(normed, seq_lens, page_table, kv_cache, qkv_weight):
    pool_pages, local_heads, twice_hd, page_len = kv_cache.shape
    head_dim = twice_hd // 2
    slot_count = normed.shape[0]
    groups = qkv_weight.shape[2] // head_dim - 2
    max_pages = page_table.shape[1]
    projected = jnp.einsum("sd,hdc->shc", normed, qkv_weight, preferred_element_type=jnp.float32)
    queries = (
        projected[:, :, : groups * head_dim]
        .reshape(slot_count, local_heads, groups, head_dim)
        .astype(jnp.bfloat16)
    )
    key_new = projected[:, :, groups * head_dim : (groups + 1) * head_dim].astype(jnp.bfloat16)
    value_new = projected[:, :, (groups + 1) * head_dim :].astype(jnp.bfloat16)
    page_need = (seq_lens + page_len - 1) // page_len
    page_ids = jnp.arange(max_pages, dtype=jnp.int32)
    in_use = page_ids[None, :] < page_need[:, None]
    pool_ids = jnp.arange(pool_pages, dtype=jnp.int32)
    entry_slot = jnp.broadcast_to(
        jnp.arange(slot_count, dtype=jnp.int32)[:, None], (slot_count, max_pages)
    ).reshape(-1)
    entry_page = jnp.where(in_use, page_table, -1).reshape(-1)
    entry_order = jnp.broadcast_to(page_ids[None, :], (slot_count, max_pages)).reshape(-1)
    entry_len = jnp.broadcast_to(seq_lens[:, None], (slot_count, max_pages)).reshape(-1)
    len_unit = 64
    facts = jnp.concatenate(
        [
            (entry_slot[None, :] == jnp.arange(slot_count, dtype=jnp.int32)[:, None]).astype(jnp.float32),
            entry_order[None, :].astype(jnp.float32),
            (entry_len // len_unit)[None, :].astype(jnp.float32),
            (entry_len % len_unit)[None, :].astype(jnp.float32),
        ],
        axis=0,
    ).astype(jnp.bfloat16)
    entry_hit = (entry_page[:, None] == pool_ids[None, :]).astype(jnp.bfloat16)
    page_facts = jnp.dot(facts, entry_hit, preferred_element_type=jnp.float32)
    belongs = page_facts[:slot_count] > 0.5
    page_order = page_facts[slot_count].astype(jnp.int32)
    owner_len = (
        page_facts[slot_count + 1].astype(jnp.int32) * len_unit
        + page_facts[slot_count + 2].astype(jnp.int32)
    )
    position = page_order[:, None] * page_len + jnp.arange(page_len, dtype=jnp.int32)[None, :]
    live = position < owner_len[:, None]
    scale_factor = head_dim ** (-0.5)
    page_queries = jnp.einsum(
        "sp,skgd->pkgd", belongs.astype(jnp.bfloat16), queries, preferred_element_type=jnp.float32
    ).astype(jnp.bfloat16)
    scores = (
        jnp.einsum(
            "pkgd,pkdt->pkgt",
            page_queries,
            kv_cache[:, :, :head_dim, :],
            preferred_element_type=jnp.float32,
        )
        * scale_factor
    )
    scores = jnp.where(live[:, None, None, :], scores, NEG_FILL)
    score_new = (
        jnp.einsum("skgd,skd->skg", queries, key_new, preferred_element_type=jnp.float32)
        * scale_factor
    )
    page_peak = jnp.max(scores, axis=3)
    slot_peak = jnp.max(jnp.where(belongs[:, :, None, None], page_peak[None], NEG_FILL), axis=1)
    slot_peak = jnp.maximum(slot_peak, score_new)
    page_peak_of_owner = jnp.max(
        jnp.where(belongs[:, :, None, None], slot_peak[:, None], NEG_FILL), axis=0
    )
    weights = jnp.where(
        live[:, None, None, :],
        jnp.exp(scores - page_peak_of_owner[..., None]),
        0.0,
    )
    page_total = jnp.sum(weights, axis=3)
    rounded_weights = lax.optimization_barrier(weights.astype(jnp.bfloat16))
    page_value = jnp.einsum(
        "pkgt,pkdt->pkgd",
        rounded_weights,
        kv_cache[:, :, head_dim:, :],
        preferred_element_type=jnp.float32,
    )
    belongs_f = belongs.astype(jnp.float32)
    total_sum = jnp.einsum("sp,pkg->skg", belongs_f, page_total, precision=lax.Precision.HIGHEST)
    value_sum = jnp.einsum(
        "sp,pkgd->skgd", belongs_f, page_value, precision=lax.Precision.HIGHEST
    )
    weight_new = jnp.exp(score_new - slot_peak)
    total_sum = total_sum + weight_new
    rounded_new = lax.optimization_barrier(weight_new.astype(jnp.bfloat16)).astype(jnp.float32)
    value_sum = value_sum + rounded_new[..., None] * value_new.astype(jnp.float32)[:, :, None, :]
    return (value_sum / total_sum[..., None]).astype(jnp.bfloat16).reshape(slot_count, -1)


def expert_apply(piece, gate_up, down):
    n_source, slot_num, local_experts, width = piece.shape
    rows_in = piece.transpose(2, 0, 1, 3).reshape(local_experts, n_source * slot_num, width)
    projected_up = jnp.einsum("erd,edf->erf", rows_in, gate_up, preferred_element_type=jnp.float32)
    hidden_units = gate_up.shape[2] // 2
    acts = (
        jax.nn.silu(projected_up[..., :hidden_units]) * projected_up[..., hidden_units:]
    ).astype(jnp.bfloat16)
    result = jnp.einsum("erf,efd->erd", acts, down, preferred_element_type=jnp.float32).astype(
        jnp.bfloat16
    )
    return result.reshape(local_experts, n_source, slot_num, width).transpose(1, 2, 0, 3)


def shards(
    hidden,
    perm,
    seq_lens,
    page_table,
    kv_cache,
    attn_gain,
    qkv_weight,
    out_weight,
    ffn_gain,
    router,
    routes,
    gate_up,
    down,
):
    req_index = lax.axis_index("req")
    kv_index = lax.axis_index("kv")
    n_req = lax.axis_size("req")
    n_kv = lax.axis_size("kv")
    local_rows, col_width = hidden.shape
    width = n_kv * col_width
    spread = jnp.broadcast_to(hidden[None], (n_kv, local_rows, col_width))
    block_parts = lax.all_to_all(spread, "kv", split_axis=0, concat_axis=0, tiled=True)
    deal = local_rows // n_req
    source_block = (perm // local_rows).reshape(n_req, local_rows)
    source_row = (perm % local_rows).reshape(n_req, local_rows)
    mine = source_block == req_index
    rank_sent = jnp.cumsum(mine.astype(jnp.int32), axis=1) - 1
    send_key = jnp.where(mine, rank_sent * local_rows + source_row, -1)
    send_ids = jnp.arange(deal * local_rows, dtype=jnp.int32)
    send_pick = jnp.any(send_key[:, :, None] == send_ids[None, None, :], axis=1)
    send_pick = send_pick.reshape(n_req, deal, local_rows).astype(hidden.dtype)
    outgoing_rows = jnp.einsum(
        "dir,jrc->dijc", send_pick, block_parts, preferred_element_type=jnp.float32
    ).astype(hidden.dtype)
    arrived_rows = lax.all_to_all(
        outgoing_rows.reshape(n_req, deal, width), "req", split_axis=0, concat_axis=0, tiled=True
    ).reshape(n_req * deal, width)
    my_source = lax.dynamic_slice_in_dim(perm, req_index * local_rows, local_rows) // local_rows
    slot_ids = jnp.arange(local_rows, dtype=jnp.int32)
    same_before = (my_source[None, :] == my_source[:, None]) & (slot_ids[None, :] < slot_ids[:, None])
    rank_got = jnp.sum(same_before.astype(jnp.int32), axis=1)
    take_key = my_source * deal + rank_got
    take_pick = (take_key[:, None] == slot_ids[None, :]).astype(hidden.dtype)
    tokens = jnp.dot(take_pick, arrived_rows, preferred_element_type=jnp.float32).astype(
        hidden.dtype
    )
    normed = rms_norm(tokens, attn_gain)
    head_out = attend(normed, seq_lens, page_table, kv_cache, qkv_weight)
    sub_rows = routes.shape[0]
    width = n_kv * col_width
    out_flat = out_weight.reshape(-1, out_weight.shape[2])
    partial = jnp.dot(head_out, out_flat, preferred_element_type=jnp.float32).astype(jnp.bfloat16)
    partial_parts = lax.all_to_all(
        partial.reshape(n_kv, sub_rows, partial.shape[1]), "kv", split_axis=0, concat_axis=0, tiled=True
    )
    attn_rows = jnp.sum(partial_parts.astype(jnp.float32), axis=0)
    own_tokens = lax.dynamic_slice_in_dim(tokens, kv_index * sub_rows, sub_rows, 0)
    residual = (own_tokens.astype(jnp.float32) + attn_rows).astype(jnp.bfloat16)
    normed_ffn = rms_norm(residual, ffn_gain)
    logits = jnp.dot(normed_ffn, router, preferred_element_type=jnp.float32)
    chosen = jnp.take_along_axis(logits, routes, axis=1)
    sigmoid_vals = jax.nn.sigmoid(chosen)
    gates = sigmoid_vals / jnp.sum(sigmoid_vals, axis=1, keepdims=True)
    experts_all = router.shape[1]
    local_experts = gate_up.shape[0]
    capacity = max(2, 2 * sub_rows // experts_all + 1)
    flat_routes = routes.reshape(-1)
    onehot_int = (flat_routes[:, None] == jnp.arange(experts_all, dtype=jnp.int32)[None, :]).astype(
        jnp.int32
    )
    earlier = jnp.cumsum(onehot_int, axis=0) - onehot_int
    rank_in = jnp.sum(earlier * onehot_int, axis=1)
    place_at = (
        flat_routes // local_experts * capacity * local_experts
        + rank_in * local_experts
        + flat_routes % local_experts
    )
    placement_plan = (
        place_at[:, None] == jnp.arange(experts_all * capacity, dtype=jnp.int32)[None, :]
    ).astype(jnp.bfloat16)
    paired_rows = jnp.repeat(normed_ffn, 2, axis=0)
    outgoing = jnp.einsum(
        "qe,qd->ed", placement_plan, paired_rows, preferred_element_type=jnp.float32
    )
    outgoing = outgoing.astype(jnp.bfloat16).reshape(n_req, capacity * local_experts, width)
    arrived = lax.all_to_all(outgoing, "req", split_axis=0, concat_axis=0, tiled=True)
    expert_rows = expert_apply(
        arrived.reshape(n_req, capacity, local_experts, width), gate_up, down
    ).reshape(n_req, capacity * local_experts, width)
    returned = lax.all_to_all(expert_rows, "req", split_axis=0, concat_axis=0, tiled=True)
    back_rows = returned.reshape(experts_all * capacity, width)
    paired_output = jnp.dot(placement_plan, back_rows, preferred_element_type=jnp.float32).reshape(
        sub_rows, 2, width
    )
    mixed = residual.astype(jnp.float32) + jnp.sum(gates[:, :, None] * paired_output, axis=1)
    return mixed.astype(jnp.bfloat16)


def solution(mesh):
    in_specs = (
        P("req", "kv"),
        P(),
        P("req"),
        P("req", None),
        P("req", "kv", None, None),
        P(),
        P("kv", None, None),
        P("kv", None, None),
        P(),
        P(),
        P(("req", "kv"), None),
        P("req", None, None),
        P("req", None, None),
    )
    out_specs = P(("req", "kv"), None)
    return jax.shard_map(shards, mesh=mesh, in_specs=in_specs, out_specs=out_specs, check_vma=False)
```

```python
import jax
import jax.numpy as jnp
from jax import lax
from jax.sharding import PartitionSpec as P

REQ_DEV = 64


NEG_FILL = -1e30
EPS_NORM = 1e-05


def rms_norm(values, gain_vec):
    values = values.astype(jnp.float32)
    factor = lax.rsqrt(jnp.mean(values * values, axis=-1, keepdims=True) + EPS_NORM)
    return (values * factor * gain_vec).astype(jnp.bfloat16)


def attend(normed, seq_lens, page_table, kv_cache, qkv_weight):
    pool_pages, local_heads, twice_hd, page_len = kv_cache.shape
    head_dim = twice_hd // 2
    slot_count = normed.shape[0]
    groups = qkv_weight.shape[2] // head_dim - 2
    max_pages = page_table.shape[1]
    projected = jnp.einsum("sd,hdc->shc", normed, qkv_weight, preferred_element_type=jnp.float32)
    queries = (
        projected[:, :, : groups * head_dim]
        .reshape(slot_count, local_heads, groups, head_dim)
        .astype(jnp.bfloat16)
    )
    key_new = projected[:, :, groups * head_dim : (groups + 1) * head_dim].astype(jnp.bfloat16)
    value_new = projected[:, :, (groups + 1) * head_dim :].astype(jnp.bfloat16)
    page_need = (seq_lens + page_len - 1) // page_len
    page_ids = jnp.arange(max_pages, dtype=jnp.int32)
    in_use = page_ids[None, :] < page_need[:, None]
    pool_ids = jnp.arange(pool_pages, dtype=jnp.int32)
    entry_slot = jnp.broadcast_to(
        jnp.arange(slot_count, dtype=jnp.int32)[:, None], (slot_count, max_pages)
    ).reshape(-1)
    entry_page = jnp.where(in_use, page_table, -1).reshape(-1)
    entry_order = jnp.broadcast_to(page_ids[None, :], (slot_count, max_pages)).reshape(-1)
    entry_len = jnp.broadcast_to(seq_lens[:, None], (slot_count, max_pages)).reshape(-1)
    len_unit = 64
    facts = jnp.concatenate(
        [
            (entry_slot[None, :] == jnp.arange(slot_count, dtype=jnp.int32)[:, None]).astype(jnp.float32),
            entry_order[None, :].astype(jnp.float32),
            (entry_len // len_unit)[None, :].astype(jnp.float32),
            (entry_len % len_unit)[None, :].astype(jnp.float32),
        ],
        axis=0,
    ).astype(jnp.bfloat16)
    entry_hit = (entry_page[:, None] == pool_ids[None, :]).astype(jnp.bfloat16)
    page_facts = jnp.dot(facts, entry_hit, preferred_element_type=jnp.float32)
    belongs = page_facts[:slot_count] > 0.5
    page_order = page_facts[slot_count].astype(jnp.int32)
    owner_len = (
        page_facts[slot_count + 1].astype(jnp.int32) * len_unit
        + page_facts[slot_count + 2].astype(jnp.int32)
    )
    position = page_order[:, None] * page_len + jnp.arange(page_len, dtype=jnp.int32)[None, :]
    live = position < owner_len[:, None]
    scale_factor = head_dim ** (-0.5)
    page_queries = jnp.einsum(
        "sp,skgd->pkgd", belongs.astype(jnp.bfloat16), queries, preferred_element_type=jnp.float32
    ).astype(jnp.bfloat16)
    scores = (
        jnp.einsum(
            "pkgd,pkdt->pkgt",
            page_queries,
            kv_cache[:, :, :head_dim, :],
            preferred_element_type=jnp.float32,
        )
        * scale_factor
    )
    scores = jnp.where(live[:, None, None, :], scores, NEG_FILL)
    score_new = (
        jnp.einsum("skgd,skd->skg", queries, key_new, preferred_element_type=jnp.float32)
        * scale_factor
    )
    page_peak = jnp.max(scores, axis=3)
    slot_peak = jnp.max(jnp.where(belongs[:, :, None, None], page_peak[None], NEG_FILL), axis=1)
    slot_peak = jnp.maximum(slot_peak, score_new)
    page_peak_of_owner = jnp.max(
        jnp.where(belongs[:, :, None, None], slot_peak[:, None], NEG_FILL), axis=0
    )
    weights = jnp.where(
        live[:, None, None, :],
        jnp.exp(scores - page_peak_of_owner[..., None]),
        0.0,
    )
    page_total = jnp.sum(weights, axis=3)
    rounded_weights = lax.optimization_barrier(weights.astype(jnp.bfloat16))
    page_value = jnp.einsum(
        "pkgt,pkdt->pkgd",
        rounded_weights,
        kv_cache[:, :, head_dim:, :],
        preferred_element_type=jnp.float32,
    )
    belongs_f = belongs.astype(jnp.float32)
    total_sum = jnp.einsum("sp,pkg->skg", belongs_f, page_total, precision=lax.Precision.HIGHEST)
    value_sum = jnp.einsum(
        "sp,pkgd->skgd", belongs_f, page_value, precision=lax.Precision.HIGHEST
    )
    weight_new = jnp.exp(score_new - slot_peak)
    total_sum = total_sum + weight_new
    rounded_new = lax.optimization_barrier(weight_new.astype(jnp.bfloat16)).astype(jnp.float32)
    value_sum = value_sum + rounded_new[..., None] * value_new.astype(jnp.float32)[:, :, None, :]
    return (value_sum / total_sum[..., None]).astype(jnp.bfloat16).reshape(slot_count, -1)


def expert_apply(piece, gate_up, down):
    n_source, slot_num, local_experts, width = piece.shape
    rows_in = piece.transpose(2, 0, 1, 3).reshape(local_experts, n_source * slot_num, width)
    projected_up = jnp.einsum("erd,edf->erf", rows_in, gate_up, preferred_element_type=jnp.float32)
    hidden_units = gate_up.shape[2] // 2
    acts = (
        jax.nn.silu(projected_up[..., :hidden_units]) * projected_up[..., hidden_units:]
    ).astype(jnp.bfloat16)
    result = jnp.einsum("erf,efd->erd", acts, down, preferred_element_type=jnp.float32).astype(
        jnp.bfloat16
    )
    return result.reshape(local_experts, n_source, slot_num, width).transpose(1, 2, 0, 3)


def shards(
    hidden,
    perm,
    seq_lens,
    page_table,
    kv_cache,
    attn_gain,
    qkv_weight,
    out_weight,
    ffn_gain,
    router,
    routes,
    gate_up,
    down,
):
    req_index = lax.axis_index("req")
    kv_index = lax.axis_index("kv")
    n_req = lax.axis_size("req")
    n_kv = lax.axis_size("kv")
    local_rows, col_width = hidden.shape
    width = n_kv * col_width
    spread = jnp.broadcast_to(hidden[None], (n_kv, local_rows, col_width))
    block_parts = lax.all_to_all(spread, "kv", split_axis=0, concat_axis=0, tiled=True)
    deal = local_rows // n_req
    perm_blocks = perm.reshape(n_req, local_rows)
    source_block = perm_blocks // local_rows
    source_row = perm_blocks - source_block * local_rows
    mine = source_block == req_index
    rank_sent = jnp.cumsum(mine.astype(jnp.int32), axis=1) - 1
    send_key = jnp.where(mine, rank_sent * local_rows + source_row, -1)
    send_ids = jnp.arange(deal * local_rows, dtype=jnp.int32)
    send_pick = jnp.any(send_key[:, :, None] == send_ids[None, None, :], axis=1)
    send_pick = send_pick.reshape(n_req, deal, local_rows).astype(hidden.dtype)
    outgoing_rows = jnp.einsum(
        "dir,jrc->dijc", send_pick, block_parts, preferred_element_type=jnp.float32
    ).astype(hidden.dtype)
    arrived_rows = lax.all_to_all(
        outgoing_rows.reshape(n_req, deal, width), "req", split_axis=0, concat_axis=0, tiled=True
    ).reshape(n_req * deal, width)
    my_source = lax.dynamic_slice_in_dim(source_block, req_index, 1, 0).reshape(local_rows)
    slot_ids = jnp.arange(local_rows, dtype=jnp.int32)
    same_before = (my_source[None, :] == my_source[:, None]) & (slot_ids[None, :] < slot_ids[:, None])
    rank_got = jnp.sum(same_before.astype(jnp.int32), axis=1)
    take_key = my_source * deal + rank_got
    take_pick = (take_key[:, None] == slot_ids[None, :]).astype(hidden.dtype)
    tokens = jnp.dot(take_pick, arrived_rows, preferred_element_type=jnp.float32).astype(
        hidden.dtype
    )
    normed = rms_norm(tokens, attn_gain)
    head_out = attend(normed, seq_lens, page_table, kv_cache, qkv_weight)
    sub_rows = routes.shape[0]
    width = n_kv * col_width
    out_flat = out_weight.reshape(-1, out_weight.shape[2])
    partial = jnp.dot(head_out, out_flat, preferred_element_type=jnp.float32).astype(jnp.bfloat16)
    partial_parts = lax.all_to_all(
        partial.reshape(n_kv, sub_rows, partial.shape[1]), "kv", split_axis=0, concat_axis=0, tiled=True
    )
    attn_rows = jnp.sum(partial_parts.astype(jnp.float32), axis=0)
    own_tokens = lax.dynamic_slice_in_dim(tokens, kv_index * sub_rows, sub_rows, 0)
    residual = (own_tokens.astype(jnp.float32) + attn_rows).astype(jnp.bfloat16)
    normed_ffn = rms_norm(residual, ffn_gain)
    logits = jnp.dot(normed_ffn, router, preferred_element_type=jnp.float32)
    chosen = jnp.take_along_axis(logits, routes, axis=1)
    sigmoid_vals = jax.nn.sigmoid(chosen)
    gates = sigmoid_vals / jnp.sum(sigmoid_vals, axis=1, keepdims=True)
    experts_all = router.shape[1]
    local_experts = gate_up.shape[0]
    capacity = max(2, 2 * sub_rows // experts_all + 1)
    flat_routes = routes.reshape(-1)
    onehot_int = (flat_routes[:, None] == jnp.arange(experts_all, dtype=jnp.int32)[None, :]).astype(
        jnp.int32
    )
    earlier = jnp.cumsum(onehot_int, axis=0) - onehot_int
    rank_in = jnp.sum(earlier * onehot_int, axis=1)
    place_at = (
        flat_routes // local_experts * capacity * local_experts
        + rank_in * local_experts
        + flat_routes % local_experts
    )
    placement_plan = (
        place_at[:, None] == jnp.arange(experts_all * capacity, dtype=jnp.int32)[None, :]
    ).astype(jnp.bfloat16)
    paired_rows = jnp.repeat(normed_ffn, 2, axis=0)
    outgoing = jnp.einsum(
        "qe,qd->ed", placement_plan, paired_rows, preferred_element_type=jnp.float32
    )
    outgoing = outgoing.astype(jnp.bfloat16).reshape(n_req, capacity * local_experts, width)
    arrived = lax.all_to_all(outgoing, "req", split_axis=0, concat_axis=0, tiled=True)
    expert_rows = expert_apply(
        arrived.reshape(n_req, capacity, local_experts, width), gate_up, down
    ).reshape(n_req, capacity * local_experts, width)
    returned = lax.all_to_all(expert_rows, "req", split_axis=0, concat_axis=0, tiled=True)
    back_rows = returned.reshape(experts_all * capacity, width)
    paired_output = jnp.dot(placement_plan, back_rows, preferred_element_type=jnp.float32).reshape(
        sub_rows, 2, width
    )
    mixed = residual.astype(jnp.float32) + jnp.sum(gates[:, :, None] * paired_output, axis=1)
    return mixed.astype(jnp.bfloat16)


def solution(mesh):
    in_specs = (
        P("req", "kv"),
        P(),
        P("req"),
        P("req", None),
        P("req", "kv", None, None),
        P(),
        P("kv", None, None),
        P("kv", None, None),
        P(),
        P(),
        P(("req", "kv"), None),
        P("req", None, None),
        P("req", None, None),
    )
    out_specs = P(("req", "kv"), None)
    return jax.shard_map(shards, mesh=mesh, in_specs=in_specs, out_specs=out_specs, check_vma=False)
```

```python
import jax
import jax.numpy as jnp
from jax import lax
from jax.sharding import PartitionSpec as P

REQ_DEV = 64


NEG_FILL = -1e30
EPS_NORM = 1e-05


def rms_norm(values, gain_vec):
    values = values.astype(jnp.float32)
    factor = lax.rsqrt(jnp.mean(values * values, axis=-1, keepdims=True) + EPS_NORM)
    return (values * factor * gain_vec).astype(jnp.bfloat16)


def attend(normed, seq_lens, page_table, kv_cache, qkv_weight):
    pool_pages, local_heads, twice_hd, page_len = kv_cache.shape
    head_dim = twice_hd // 2
    slot_count = normed.shape[0]
    groups = qkv_weight.shape[2] // head_dim - 2
    max_pages = page_table.shape[1]
    projected = jnp.einsum("sd,hdc->shc", normed, qkv_weight, preferred_element_type=jnp.float32)
    queries = (
        projected[:, :, : groups * head_dim]
        .reshape(slot_count, local_heads, groups, head_dim)
        .astype(jnp.bfloat16)
    )
    key_new = projected[:, :, groups * head_dim : (groups + 1) * head_dim].astype(jnp.bfloat16)
    value_new = projected[:, :, (groups + 1) * head_dim :].astype(jnp.bfloat16)
    page_need = lax.div(seq_lens + page_len - 1, page_len)
    page_ids = jnp.arange(max_pages, dtype=jnp.int32)
    in_use = page_ids[None, :] < page_need[:, None]
    pool_ids = jnp.arange(pool_pages, dtype=jnp.int32)
    entry_slot = jnp.broadcast_to(
        jnp.arange(slot_count, dtype=jnp.int32)[:, None], (slot_count, max_pages)
    ).reshape(-1)
    entry_page = jnp.where(in_use, page_table, -1).reshape(-1)
    entry_order = jnp.broadcast_to(page_ids[None, :], (slot_count, max_pages)).reshape(-1)
    entry_len = jnp.broadcast_to(seq_lens[:, None], (slot_count, max_pages)).reshape(-1)
    len_unit = 64
    facts = jnp.concatenate(
        [
            (entry_slot[None, :] == jnp.arange(slot_count, dtype=jnp.int32)[:, None]).astype(jnp.float32),
            entry_order[None, :].astype(jnp.float32),
            lax.div(entry_len, len_unit)[None, :].astype(jnp.float32),
            lax.rem(entry_len, len_unit)[None, :].astype(jnp.float32),
        ],
        axis=0,
    ).astype(jnp.bfloat16)
    entry_hit = (entry_page[:, None] == pool_ids[None, :]).astype(jnp.bfloat16)
    page_facts = jnp.dot(facts, entry_hit, preferred_element_type=jnp.float32)
    belongs = page_facts[:slot_count] > 0.5
    page_order = page_facts[slot_count].astype(jnp.int32)
    owner_len = (
        page_facts[slot_count + 1].astype(jnp.int32) * len_unit
        + page_facts[slot_count + 2].astype(jnp.int32)
    )
    position = page_order[:, None] * page_len + jnp.arange(page_len, dtype=jnp.int32)[None, :]
    live = position < owner_len[:, None]
    scale_factor = head_dim ** (-0.5)
    page_queries = jnp.einsum(
        "sp,skgd->pkgd", belongs.astype(jnp.bfloat16), queries, preferred_element_type=jnp.float32
    ).astype(jnp.bfloat16)
    scores = (
        jnp.einsum(
            "pkgd,pkdt->pkgt",
            page_queries,
            kv_cache[:, :, :head_dim, :],
            preferred_element_type=jnp.float32,
        )
        * scale_factor
    )
    scores = jnp.where(live[:, None, None, :], scores, NEG_FILL)
    score_new = (
        jnp.einsum("skgd,skd->skg", queries, key_new, preferred_element_type=jnp.float32)
        * scale_factor
    )
    page_peak = jnp.max(scores, axis=3)
    slot_peak = jnp.max(jnp.where(belongs[:, :, None, None], page_peak[None], NEG_FILL), axis=1)
    slot_peak = jnp.maximum(slot_peak, score_new)
    page_peak_of_owner = jnp.max(
        jnp.where(belongs[:, :, None, None], slot_peak[:, None], NEG_FILL), axis=0
    )
    weights = jnp.where(
        live[:, None, None, :],
        jnp.exp(scores - page_peak_of_owner[..., None]),
        0.0,
    )
    page_total = jnp.sum(weights, axis=3)
    rounded_weights = lax.optimization_barrier(weights.astype(jnp.bfloat16))
    page_value = jnp.einsum(
        "pkgt,pkdt->pkgd",
        rounded_weights,
        kv_cache[:, :, head_dim:, :],
        preferred_element_type=jnp.float32,
    )
    belongs_f = belongs.astype(jnp.float32)
    total_sum = jnp.einsum("sp,pkg->skg", belongs_f, page_total, precision=lax.Precision.HIGHEST)
    value_sum = jnp.einsum(
        "sp,pkgd->skgd", belongs_f, page_value, precision=lax.Precision.HIGHEST
    )
    weight_new = jnp.exp(score_new - slot_peak)
    total_sum = total_sum + weight_new
    rounded_new = lax.optimization_barrier(weight_new.astype(jnp.bfloat16)).astype(jnp.float32)
    value_sum = value_sum + rounded_new[..., None] * value_new.astype(jnp.float32)[:, :, None, :]
    return (value_sum / total_sum[..., None]).astype(jnp.bfloat16).reshape(slot_count, -1)


def expert_apply(piece, gate_up, down):
    n_source, slot_num, local_experts, width = piece.shape
    rows_in = piece.transpose(2, 0, 1, 3).reshape(local_experts, n_source * slot_num, width)
    projected_up = jnp.einsum("erd,edf->erf", rows_in, gate_up, preferred_element_type=jnp.float32)
    hidden_units = gate_up.shape[2] // 2
    acts = (
        jax.nn.silu(projected_up[..., :hidden_units]) * projected_up[..., hidden_units:]
    ).astype(jnp.bfloat16)
    result = jnp.einsum("erf,efd->erd", acts, down, preferred_element_type=jnp.float32).astype(
        jnp.bfloat16
    )
    return result.reshape(local_experts, n_source, slot_num, width).transpose(1, 2, 0, 3)


def shards(
    hidden,
    perm,
    seq_lens,
    page_table,
    kv_cache,
    attn_gain,
    qkv_weight,
    out_weight,
    ffn_gain,
    router,
    routes,
    gate_up,
    down,
):
    req_index = lax.axis_index("req")
    kv_index = lax.axis_index("kv")
    n_req = lax.axis_size("req")
    n_kv = lax.axis_size("kv")
    local_rows, col_width = hidden.shape
    width = n_kv * col_width
    spread = jnp.broadcast_to(hidden[None], (n_kv, local_rows, col_width))
    block_parts = lax.all_to_all(spread, "kv", split_axis=0, concat_axis=0, tiled=True)
    deal = local_rows // n_req
    perm_blocks = perm.reshape(n_req, local_rows)
    source_block = lax.div(perm_blocks, local_rows)
    source_row = perm_blocks - source_block * local_rows
    mine = source_block == req_index
    rank_sent = jnp.cumsum(mine.astype(jnp.int32), axis=1) - 1
    send_key = jnp.where(mine, rank_sent * local_rows + source_row, -1)
    send_ids = jnp.arange(deal * local_rows, dtype=jnp.int32)
    send_pick = jnp.any(send_key[:, :, None] == send_ids[None, None, :], axis=1)
    send_pick = send_pick.reshape(n_req, deal, local_rows).astype(hidden.dtype)
    outgoing_rows = jnp.einsum(
        "dir,jrc->dijc", send_pick, block_parts, preferred_element_type=jnp.float32
    ).astype(hidden.dtype)
    arrived_rows = lax.all_to_all(
        outgoing_rows.reshape(n_req, deal, width), "req", split_axis=0, concat_axis=0, tiled=True
    ).reshape(n_req * deal, width)
    my_source = lax.dynamic_slice_in_dim(source_block, req_index, 1, 0).reshape(local_rows)
    slot_ids = jnp.arange(local_rows, dtype=jnp.int32)
    same_before = (my_source[None, :] == my_source[:, None]) & (slot_ids[None, :] < slot_ids[:, None])
    rank_got = jnp.sum(same_before.astype(jnp.int32), axis=1)
    take_key = my_source * deal + rank_got
    take_pick = (take_key[:, None] == slot_ids[None, :]).astype(hidden.dtype)
    tokens = jnp.dot(take_pick, arrived_rows, preferred_element_type=jnp.float32).astype(
        hidden.dtype
    )
    normed = rms_norm(tokens, attn_gain)
    head_out = attend(normed, seq_lens, page_table, kv_cache, qkv_weight)
    sub_rows = routes.shape[0]
    width = n_kv * col_width
    out_flat = out_weight.reshape(-1, out_weight.shape[2])
    partial = jnp.dot(head_out, out_flat, preferred_element_type=jnp.float32).astype(jnp.bfloat16)
    partial_parts = lax.all_to_all(
        partial.reshape(n_kv, sub_rows, partial.shape[1]), "kv", split_axis=0, concat_axis=0, tiled=True
    )
    attn_rows = jnp.sum(partial_parts.astype(jnp.float32), axis=0)
    own_tokens = lax.dynamic_slice_in_dim(tokens, kv_index * sub_rows, sub_rows, 0)
    residual = (own_tokens.astype(jnp.float32) + attn_rows).astype(jnp.bfloat16)
    normed_ffn = rms_norm(residual, ffn_gain)
    logits = jnp.dot(normed_ffn, router, preferred_element_type=jnp.float32)
    chosen = jnp.take_along_axis(logits, routes, axis=1)
    sigmoid_vals = jax.nn.sigmoid(chosen)
    gates = sigmoid_vals / jnp.sum(sigmoid_vals, axis=1, keepdims=True)
    experts_all = router.shape[1]
    local_experts = gate_up.shape[0]
    capacity = max(2, 2 * sub_rows // experts_all + 1)
    flat_routes = routes.reshape(-1)
    onehot_int = (flat_routes[:, None] == jnp.arange(experts_all, dtype=jnp.int32)[None, :]).astype(
        jnp.int32
    )
    earlier = jnp.cumsum(onehot_int, axis=0) - onehot_int
    rank_in = jnp.sum(earlier * onehot_int, axis=1)
    place_at = (
        flat_routes // local_experts * capacity * local_experts
        + rank_in * local_experts
        + flat_routes % local_experts
    )
    placement_plan = (
        place_at[:, None] == jnp.arange(experts_all * capacity, dtype=jnp.int32)[None, :]
    ).astype(jnp.bfloat16)
    paired_rows = jnp.repeat(normed_ffn, 2, axis=0)
    outgoing = jnp.einsum(
        "qe,qd->ed", placement_plan, paired_rows, preferred_element_type=jnp.float32
    )
    outgoing = outgoing.astype(jnp.bfloat16).reshape(n_req, capacity * local_experts, width)
    arrived = lax.all_to_all(outgoing, "req", split_axis=0, concat_axis=0, tiled=True)
    expert_rows = expert_apply(
        arrived.reshape(n_req, capacity, local_experts, width), gate_up, down
    ).reshape(n_req, capacity * local_experts, width)
    returned = lax.all_to_all(expert_rows, "req", split_axis=0, concat_axis=0, tiled=True)
    back_rows = returned.reshape(experts_all * capacity, width)
    paired_output = jnp.dot(placement_plan, back_rows, preferred_element_type=jnp.float32).reshape(
        sub_rows, 2, width
    )
    mixed = residual.astype(jnp.float32) + jnp.sum(gates[:, :, None] * paired_output, axis=1)
    return mixed.astype(jnp.bfloat16)


def solution(mesh):
    in_specs = (
        P("req", "kv"),
        P(),
        P("req"),
        P("req", None),
        P("req", "kv", None, None),
        P(),
        P("kv", None, None),
        P("kv", None, None),
        P(),
        P(),
        P(("req", "kv"), None),
        P("req", None, None),
        P("req", None, None),
    )
    out_specs = P(("req", "kv"), None)
    return jax.shard_map(shards, mesh=mesh, in_specs=in_specs, out_specs=out_specs, check_vma=False)
```

```python
import jax
import jax.numpy as jnp
from jax import lax
from jax.sharding import PartitionSpec as P

REQ_DEV = 64


NEG_FILL = -1e30
EPS_NORM = 1e-05


def rms_norm(values, gain_vec):
    values = values.astype(jnp.float32)
    factor = lax.rsqrt(jnp.mean(values * values, axis=-1, keepdims=True) + EPS_NORM)
    return (values * factor * gain_vec).astype(jnp.bfloat16)


def attend(normed, seq_lens, page_table, kv_cache, qkv_weight):
    pool_pages, local_heads, twice_hd, page_len = kv_cache.shape
    head_dim = twice_hd // 2
    slot_count = normed.shape[0]
    groups = qkv_weight.shape[2] // head_dim - 2
    max_pages = page_table.shape[1]
    projected = jnp.einsum("sd,hdc->shc", normed, qkv_weight, preferred_element_type=jnp.float32)
    queries = (
        projected[:, :, : groups * head_dim]
        .reshape(slot_count, local_heads, groups, head_dim)
        .astype(jnp.bfloat16)
    )
    key_new = projected[:, :, groups * head_dim : (groups + 1) * head_dim].astype(jnp.bfloat16)
    value_new = projected[:, :, (groups + 1) * head_dim :].astype(jnp.bfloat16)
    page_need = lax.div(seq_lens + page_len - 1, page_len)
    page_ids = jnp.arange(max_pages, dtype=jnp.int32)
    in_use = page_ids[None, :] < page_need[:, None]
    pool_ids = jnp.arange(pool_pages, dtype=jnp.int32)
    entry_slot = jnp.broadcast_to(
        jnp.arange(slot_count, dtype=jnp.int32)[:, None], (slot_count, max_pages)
    ).reshape(-1)
    entry_page = jnp.where(in_use, page_table, -1).reshape(-1)
    entry_order = jnp.broadcast_to(page_ids[None, :], (slot_count, max_pages)).reshape(-1)
    entry_len = jnp.broadcast_to(seq_lens[:, None], (slot_count, max_pages)).reshape(-1)
    len_unit = 64
    facts = jnp.concatenate(
        [
            (entry_slot[None, :] == jnp.arange(slot_count, dtype=jnp.int32)[:, None]).astype(jnp.float32),
            entry_order[None, :].astype(jnp.float32),
            lax.div(entry_len, len_unit)[None, :].astype(jnp.float32),
            lax.rem(entry_len, len_unit)[None, :].astype(jnp.float32),
        ],
        axis=0,
    ).astype(jnp.bfloat16)
    entry_hit = (entry_page[:, None] == pool_ids[None, :]).astype(jnp.bfloat16)
    page_facts = jnp.dot(facts, entry_hit, preferred_element_type=jnp.float32)
    belongs = page_facts[:slot_count] > 0.5
    page_order = page_facts[slot_count].astype(jnp.int32)
    owner_len = (
        page_facts[slot_count + 1].astype(jnp.int32) * len_unit
        + page_facts[slot_count + 2].astype(jnp.int32)
    )
    position = page_order[:, None] * page_len + jnp.arange(page_len, dtype=jnp.int32)[None, :]
    live = position < owner_len[:, None]
    scale_factor = head_dim ** (-0.5)
    page_queries = jnp.einsum(
        "sp,skgd->pkgd", belongs.astype(jnp.bfloat16), queries, preferred_element_type=jnp.float32
    ).astype(jnp.bfloat16)
    scores = (
        jnp.einsum(
            "pkgd,pkdt->pkgt",
            page_queries,
            kv_cache[:, :, :head_dim, :],
            preferred_element_type=jnp.float32,
        )
        * scale_factor
    )
    scores = jnp.where(live[:, None, None, :], scores, NEG_FILL)
    score_new = (
        jnp.einsum("skgd,skd->skg", queries, key_new, preferred_element_type=jnp.float32)
        * scale_factor
    )
    page_peak = jnp.max(scores, axis=3)
    slot_peak = jnp.max(jnp.where(belongs[:, :, None, None], page_peak[None], NEG_FILL), axis=1)
    slot_peak = jnp.maximum(slot_peak, score_new)
    page_peak_of_owner = jnp.max(
        jnp.where(belongs[:, :, None, None], slot_peak[:, None], NEG_FILL), axis=0
    )
    weights = jnp.where(
        live[:, None, None, :],
        jnp.exp(scores - page_peak_of_owner[..., None]),
        0.0,
    )
    page_total = jnp.sum(weights, axis=3)
    rounded_weights = lax.optimization_barrier(weights.astype(jnp.bfloat16))
    page_value = jnp.einsum(
        "pkgt,pkdt->pkgd",
        rounded_weights,
        kv_cache[:, :, head_dim:, :],
        preferred_element_type=jnp.float32,
    )
    belongs_f = belongs.astype(jnp.float32)
    total_sum = jnp.einsum("sp,pkg->skg", belongs_f, page_total, precision=lax.Precision.HIGHEST)
    value_sum = jnp.einsum(
        "sp,pkgd->skgd", belongs_f, page_value, precision=lax.Precision.HIGHEST
    )
    weight_new = jnp.exp(score_new - slot_peak)
    total_sum = total_sum + weight_new
    rounded_new = lax.optimization_barrier(weight_new.astype(jnp.bfloat16)).astype(jnp.float32)
    value_sum = value_sum + rounded_new[..., None] * value_new.astype(jnp.float32)[:, :, None, :]
    return (value_sum / total_sum[..., None]).astype(jnp.bfloat16).reshape(slot_count, -1)


def expert_apply(piece, gate_up, down):
    n_source, slot_num, local_experts, width = piece.shape
    rows_in = piece.transpose(2, 0, 1, 3).reshape(local_experts, n_source * slot_num, width)
    projected_up = jnp.einsum("erd,edf->erf", rows_in, gate_up, preferred_element_type=jnp.float32)
    hidden_units = gate_up.shape[2] // 2
    acts = (
        jax.nn.silu(projected_up[..., :hidden_units]) * projected_up[..., hidden_units:]
    ).astype(jnp.bfloat16)
    result = jnp.einsum("erf,efd->erd", acts, down, preferred_element_type=jnp.float32).astype(
        jnp.bfloat16
    )
    return result.reshape(local_experts, n_source, slot_num, width).transpose(1, 2, 0, 3)


def shards(
    hidden,
    perm,
    seq_lens,
    page_table,
    kv_cache,
    attn_gain,
    qkv_weight,
    out_weight,
    ffn_gain,
    router,
    routes,
    gate_up,
    down,
):
    req_index = lax.axis_index("req")
    kv_index = lax.axis_index("kv")
    n_req = lax.axis_size("req")
    n_kv = lax.axis_size("kv")
    local_rows, col_width = hidden.shape
    width = n_kv * col_width
    spread = jnp.broadcast_to(hidden[None], (n_kv, local_rows, col_width))
    block_parts = lax.all_to_all(spread, "kv", split_axis=0, concat_axis=0, tiled=True)
    deal = local_rows // n_req
    perm_blocks = perm.reshape(n_req, local_rows)
    source_block = lax.div(perm_blocks, local_rows)
    source_row = perm_blocks - source_block * local_rows
    mine = source_block == req_index
    rank_sent = jnp.cumsum(mine.astype(jnp.int32), axis=1) - 1
    send_key = jnp.where(mine, rank_sent * local_rows + source_row, -1)
    send_ids = jnp.arange(deal * local_rows, dtype=jnp.int32)
    send_pick = jnp.any(send_key[:, :, None] == send_ids[None, None, :], axis=1)
    send_pick = send_pick.reshape(n_req, deal, local_rows).astype(hidden.dtype)
    outgoing_rows = jnp.einsum(
        "dir,jrc->dijc", send_pick, block_parts, preferred_element_type=jnp.float32
    ).astype(hidden.dtype)
    arrived_rows = lax.all_to_all(
        outgoing_rows.reshape(n_req, deal, width), "req", split_axis=0, concat_axis=0, tiled=True
    ).reshape(n_req * deal, width)
    my_source = lax.dynamic_slice_in_dim(source_block, req_index, 1, 0).reshape(local_rows)
    slot_ids = jnp.arange(local_rows, dtype=jnp.int32)
    same_before = (my_source[None, :] == my_source[:, None]) & (slot_ids[None, :] < slot_ids[:, None])
    rank_got = jnp.sum(same_before.astype(jnp.int32), axis=1)
    take_key = my_source * deal + rank_got
    take_pick = (take_key[:, None] == slot_ids[None, :]).astype(hidden.dtype)
    tokens = jnp.dot(take_pick, arrived_rows, preferred_element_type=jnp.float32).astype(
        hidden.dtype
    )
    normed = rms_norm(tokens, attn_gain)
    head_out = attend(normed, seq_lens, page_table, kv_cache, qkv_weight)
    sub_rows = routes.shape[0]
    width = n_kv * col_width
    out_flat = out_weight.reshape(-1, out_weight.shape[2])
    partial = jnp.dot(head_out, out_flat, preferred_element_type=jnp.float32).astype(jnp.bfloat16)
    partial_parts = lax.all_to_all(
        partial.reshape(n_kv, sub_rows, partial.shape[1]), "kv", split_axis=0, concat_axis=0, tiled=True
    )
    attn_rows = jnp.sum(partial_parts.astype(jnp.float32), axis=0)
    own_tokens = lax.dynamic_slice_in_dim(tokens, kv_index * sub_rows, sub_rows, 0)
    residual = (own_tokens.astype(jnp.float32) + attn_rows).astype(jnp.bfloat16)
    normed_ffn = rms_norm(residual, ffn_gain)
    logits = jnp.dot(normed_ffn, router, preferred_element_type=jnp.float32)
    expert_ids = jnp.arange(logits.shape[1], dtype=jnp.int32)
    chosen = jnp.sum(
        jnp.where(routes[:, :, None] == expert_ids[None, None, :], logits[:, None, :], 0.0), axis=2
    )
    sigmoid_vals = jax.nn.sigmoid(chosen)
    gates = sigmoid_vals / jnp.sum(sigmoid_vals, axis=1, keepdims=True)
    experts_all = router.shape[1]
    local_experts = gate_up.shape[0]
    capacity = max(2, 2 * sub_rows // experts_all + 1)
    entry_ids = jnp.arange(routes.size, dtype=jnp.int32).reshape(routes.shape)
    same_expert = routes[:, :, None, None] == routes[None, None, :, :]
    earlier = entry_ids[None, None, :, :] < entry_ids[:, :, None, None]
    rank_in = jnp.sum((same_expert & earlier).astype(jnp.int32), axis=(2, 3))
    place_at = (
        lax.div(routes, local_experts) * capacity * local_experts
        + rank_in * local_experts
        + lax.rem(routes, local_experts)
    )
    slots_per_dest = capacity * local_experts
    dest_slot = (
        jnp.arange(n_req, dtype=jnp.int32)[:, None] * slots_per_dest
        + jnp.arange(slots_per_dest, dtype=jnp.int32)[None, :]
    )
    placement_plan = (place_at[:, :, None, None] == dest_slot[None, None, :, :]).astype(jnp.bfloat16)
    outgoing = jnp.einsum(
        "rjnc,rd->ncd", placement_plan, normed_ffn, preferred_element_type=jnp.float32
    ).astype(jnp.bfloat16)
    arrived = lax.all_to_all(outgoing, "req", split_axis=0, concat_axis=0, tiled=True)
    expert_rows = expert_apply(
        arrived.reshape(n_req, capacity, local_experts, width), gate_up, down
    ).reshape(n_req, slots_per_dest, width)
    returned = lax.all_to_all(expert_rows, "req", split_axis=0, concat_axis=0, tiled=True)
    paired_output = jnp.einsum(
        "rjnc,ncd->rjd", placement_plan, returned, preferred_element_type=jnp.float32
    )
    mixed = residual.astype(jnp.float32) + jnp.sum(gates[:, :, None] * paired_output, axis=1)
    return mixed.astype(jnp.bfloat16)


def solution(mesh):
    in_specs = (
        P("req", "kv"),
        P(),
        P("req"),
        P("req", None),
        P("req", "kv", None, None),
        P(),
        P("kv", None, None),
        P("kv", None, None),
        P(),
        P(),
        P(("req", "kv"), None),
        P("req", None, None),
        P("req", None, None),
    )
    out_specs = P(("req", "kv"), None)
    return jax.shard_map(shards, mesh=mesh, in_specs=in_specs, out_specs=out_specs, check_vma=False)
```

```python
import jax
import jax.numpy as jnp
from jax import lax
from jax.sharding import PartitionSpec as P

REQ_DEV = 64


NEG_FILL = -1e30
EPS_NORM = 1e-05


def rms_norm(values, gain_vec):
    values = values.astype(jnp.float32)
    factor = lax.rsqrt(jnp.mean(values * values, axis=-1, keepdims=True) + EPS_NORM)
    return (values * factor * gain_vec).astype(jnp.bfloat16)


def attend(normed, seq_lens, page_table, kv_cache, qkv_weight):
    pool_pages, local_heads, twice_hd, page_len = kv_cache.shape
    head_dim = twice_hd // 2
    slot_count = normed.shape[0]
    groups = qkv_weight.shape[2] // head_dim - 2
    max_pages = page_table.shape[1]
    projected = jnp.einsum("sd,hdc->shc", normed, qkv_weight, preferred_element_type=jnp.float32)
    queries = (
        projected[:, :, : groups * head_dim]
        .reshape(slot_count, local_heads, groups, head_dim)
        .astype(jnp.bfloat16)
    )
    key_new = projected[:, :, groups * head_dim : (groups + 1) * head_dim].astype(jnp.bfloat16)
    value_new = projected[:, :, (groups + 1) * head_dim :].astype(jnp.bfloat16)
    page_need = lax.div(seq_lens + page_len - 1, page_len)
    page_ids = jnp.arange(max_pages, dtype=jnp.int32)
    in_use = page_ids[None, :] < page_need[:, None]
    pool_ids = jnp.arange(pool_pages, dtype=jnp.int32)
    entry_slot = jnp.broadcast_to(
        jnp.arange(slot_count, dtype=jnp.int32)[:, None], (slot_count, max_pages)
    ).reshape(-1)
    entry_page = jnp.where(in_use, page_table, -1).reshape(-1)
    entry_order = jnp.broadcast_to(page_ids[None, :], (slot_count, max_pages)).reshape(-1)
    facts = jnp.concatenate(
        [
            (entry_slot[None, :] == jnp.arange(slot_count, dtype=jnp.int32)[:, None]).astype(jnp.float32),
            entry_order[None, :].astype(jnp.float32),
        ],
        axis=0,
    ).astype(jnp.bfloat16)
    entry_hit = (entry_page[:, None] == pool_ids[None, :]).astype(jnp.bfloat16)
    page_facts = jnp.dot(facts, entry_hit, preferred_element_type=jnp.float32)
    belongs = page_facts[:slot_count] > 0.5
    page_order = page_facts[slot_count].astype(jnp.int32)
    owner_len = jnp.sum(jnp.where(belongs, seq_lens[:, None], 0), axis=0)
    position = page_order[:, None] * page_len + jnp.arange(page_len, dtype=jnp.int32)[None, :]
    live = position < owner_len[:, None]
    scale_factor = head_dim ** (-0.5)
    page_queries = jnp.einsum(
        "sp,skgd->pkgd", belongs.astype(jnp.bfloat16), queries, preferred_element_type=jnp.float32
    ).astype(jnp.bfloat16)
    scores = (
        jnp.einsum(
            "pkgd,pkdt->pkgt",
            page_queries,
            kv_cache[:, :, :head_dim, :],
            preferred_element_type=jnp.float32,
        )
        * scale_factor
    )
    scores = jnp.where(live[:, None, None, :], scores, NEG_FILL)
    score_new = (
        jnp.einsum("skgd,skd->skg", queries, key_new, preferred_element_type=jnp.float32)
        * scale_factor
    )
    page_peak = jnp.max(scores, axis=3)
    slot_peak = jnp.max(jnp.where(belongs[:, :, None, None], page_peak[None], NEG_FILL), axis=1)
    slot_peak = jnp.maximum(slot_peak, score_new)
    page_peak_of_owner = jnp.max(
        jnp.where(belongs[:, :, None, None], slot_peak[:, None], NEG_FILL), axis=0
    )
    weights = jnp.where(
        live[:, None, None, :],
        jnp.exp(scores - page_peak_of_owner[..., None]),
        0.0,
    )
    page_total = jnp.sum(weights, axis=3)
    rounded_weights = lax.optimization_barrier(weights.astype(jnp.bfloat16))
    page_value = jnp.einsum(
        "pkgt,pkdt->pkgd",
        rounded_weights,
        kv_cache[:, :, head_dim:, :],
        preferred_element_type=jnp.float32,
    )
    belongs_f = belongs.astype(jnp.float32)
    total_sum = jnp.einsum("sp,pkg->skg", belongs_f, page_total, precision=lax.Precision.HIGHEST)
    value_sum = jnp.einsum(
        "sp,pkgd->skgd", belongs_f, page_value, precision=lax.Precision.HIGHEST
    )
    weight_new = jnp.exp(score_new - slot_peak)
    total_sum = total_sum + weight_new
    rounded_new = lax.optimization_barrier(weight_new.astype(jnp.bfloat16)).astype(jnp.float32)
    value_sum = value_sum + rounded_new[..., None] * value_new.astype(jnp.float32)[:, :, None, :]
    return (value_sum / total_sum[..., None]).astype(jnp.bfloat16).reshape(slot_count, -1)


def expert_apply(piece, gate_up, down):
    n_source, slot_num, local_experts, width = piece.shape
    rows_in = piece.transpose(2, 0, 1, 3).reshape(local_experts, n_source * slot_num, width)
    projected_up = jnp.einsum("erd,edf->erf", rows_in, gate_up, preferred_element_type=jnp.float32)
    hidden_units = gate_up.shape[2] // 2
    acts = (
        jax.nn.silu(projected_up[..., :hidden_units]) * projected_up[..., hidden_units:]
    ).astype(jnp.bfloat16)
    result = jnp.einsum("erf,efd->erd", acts, down, preferred_element_type=jnp.float32).astype(
        jnp.bfloat16
    )
    return result.reshape(local_experts, n_source, slot_num, width).transpose(1, 2, 0, 3)


def shards(
    hidden,
    perm,
    seq_lens,
    page_table,
    kv_cache,
    attn_gain,
    qkv_weight,
    out_weight,
    ffn_gain,
    router,
    routes,
    gate_up,
    down,
):
    req_index = lax.axis_index("req")
    kv_index = lax.axis_index("kv")
    n_req = lax.axis_size("req")
    n_kv = lax.axis_size("kv")
    local_rows, col_width = hidden.shape
    width = n_kv * col_width
    spread = jnp.broadcast_to(hidden[None], (n_kv, local_rows, col_width))
    block_parts = lax.all_to_all(spread, "kv", split_axis=0, concat_axis=0, tiled=True)
    deal = local_rows // n_req
    perm_blocks = perm.reshape(n_req, local_rows)
    source_block = lax.div(perm_blocks, local_rows)
    source_row = perm_blocks - source_block * local_rows
    mine = source_block == req_index
    rank_sent = jnp.cumsum(mine.astype(jnp.int32), axis=1) - 1
    send_key = jnp.where(mine, rank_sent * local_rows + source_row, -1)
    send_ids = jnp.arange(deal * local_rows, dtype=jnp.int32)
    send_pick = jnp.any(send_key[:, :, None] == send_ids[None, None, :], axis=1)
    send_pick = send_pick.reshape(n_req, deal, local_rows).astype(hidden.dtype)
    outgoing_rows = jnp.einsum(
        "dir,jrc->dijc", send_pick, block_parts, preferred_element_type=jnp.float32
    ).astype(hidden.dtype)
    arrived_rows = lax.all_to_all(
        outgoing_rows.reshape(n_req, deal, width), "req", split_axis=0, concat_axis=0, tiled=True
    ).reshape(n_req * deal, width)
    my_source = lax.dynamic_slice_in_dim(source_block, req_index, 1, 0).reshape(local_rows)
    slot_ids = jnp.arange(local_rows, dtype=jnp.int32)
    same_before = (my_source[None, :] == my_source[:, None]) & (slot_ids[None, :] < slot_ids[:, None])
    rank_got = jnp.sum(same_before.astype(jnp.int32), axis=1)
    take_key = my_source * deal + rank_got
    take_pick = (take_key[:, None] == slot_ids[None, :]).astype(hidden.dtype)
    tokens = jnp.dot(take_pick, arrived_rows, preferred_element_type=jnp.float32).astype(
        hidden.dtype
    )
    normed = rms_norm(tokens, attn_gain)
    head_out = attend(normed, seq_lens, page_table, kv_cache, qkv_weight)
    sub_rows = routes.shape[0]
    width = n_kv * col_width
    out_flat = out_weight.reshape(-1, out_weight.shape[2])
    partial = jnp.dot(head_out, out_flat, preferred_element_type=jnp.float32).astype(jnp.bfloat16)
    partial_parts = lax.all_to_all(
        partial.reshape(n_kv, sub_rows, partial.shape[1]), "kv", split_axis=0, concat_axis=0, tiled=True
    )
    attn_rows = jnp.sum(partial_parts.astype(jnp.float32), axis=0)
    own_tokens = lax.dynamic_slice_in_dim(tokens, kv_index * sub_rows, sub_rows, 0)
    residual = (own_tokens.astype(jnp.float32) + attn_rows).astype(jnp.bfloat16)
    normed_ffn = rms_norm(residual, ffn_gain)
    logits = jnp.dot(normed_ffn, router, preferred_element_type=jnp.float32)
    expert_ids = jnp.arange(logits.shape[1], dtype=jnp.int32)
    chosen = jnp.sum(
        jnp.where(routes[:, :, None] == expert_ids[None, None, :], logits[:, None, :], 0.0), axis=2
    )
    sigmoid_vals = jax.nn.sigmoid(chosen)
    gates = sigmoid_vals / jnp.sum(sigmoid_vals, axis=1, keepdims=True)
    experts_all = router.shape[1]
    local_experts = gate_up.shape[0]
    capacity = max(2, 2 * sub_rows // experts_all + 1)
    entry_ids = jnp.arange(routes.size, dtype=jnp.int32).reshape(routes.shape)
    same_expert = routes[:, :, None, None] == routes[None, None, :, :]
    earlier = entry_ids[None, None, :, :] < entry_ids[:, :, None, None]
    rank_in = jnp.sum((same_expert & earlier).astype(jnp.int32), axis=(2, 3))
    place_at = (
        lax.div(routes, local_experts) * capacity * local_experts
        + rank_in * local_experts
        + lax.rem(routes, local_experts)
    )
    slots_per_dest = capacity * local_experts
    dest_slot = (
        jnp.arange(n_req, dtype=jnp.int32)[:, None] * slots_per_dest
        + jnp.arange(slots_per_dest, dtype=jnp.int32)[None, :]
    )
    placement_plan = (place_at[:, :, None, None] == dest_slot[None, None, :, :]).astype(jnp.bfloat16)
    outgoing = jnp.einsum(
        "rjnc,rd->ncd", placement_plan, normed_ffn, preferred_element_type=jnp.float32
    ).astype(jnp.bfloat16)
    arrived = lax.all_to_all(outgoing, "req", split_axis=0, concat_axis=0, tiled=True)
    expert_rows = expert_apply(
        arrived.reshape(n_req, capacity, local_experts, width), gate_up, down
    ).reshape(n_req, slots_per_dest, width)
    returned = lax.all_to_all(expert_rows, "req", split_axis=0, concat_axis=0, tiled=True)
    paired_output = jnp.einsum(
        "rjnc,ncd->rjd", placement_plan, returned, preferred_element_type=jnp.float32
    )
    mixed = residual.astype(jnp.float32) + jnp.sum(gates[:, :, None] * paired_output, axis=1)
    return mixed.astype(jnp.bfloat16)


def solution(mesh):
    in_specs = (
        P("req", "kv"),
        P(),
        P("req"),
        P("req", None),
        P("req", "kv", None, None),
        P(),
        P("kv", None, None),
        P("kv", None, None),
        P(),
        P(),
        P(("req", "kv"), None),
        P("req", None, None),
        P("req", None, None),
    )
    out_specs = P(("req", "kv"), None)
    return jax.shard_map(shards, mesh=mesh, in_specs=in_specs, out_specs=out_specs, check_vma=False)
```

```python
import jax
import jax.numpy as jnp
from jax import lax
from jax.sharding import PartitionSpec as P

REQ_DEV = 64


NEG_FILL = -1e30
EPS_NORM = 1e-05


def rms_norm(values, gain_vec):
    values = values.astype(jnp.float32)
    factor = lax.rsqrt(jnp.mean(values * values, axis=-1, keepdims=True) + EPS_NORM)
    return (values * factor * gain_vec).astype(jnp.bfloat16)


def attend(normed, seq_lens, page_table, kv_cache, qkv_weight):
    pool_pages, local_heads, twice_hd, page_len = kv_cache.shape
    head_dim = twice_hd // 2
    slot_count = normed.shape[0]
    groups = qkv_weight.shape[2] // head_dim - 2
    max_pages = page_table.shape[1]
    projected = jnp.einsum("sd,hdc->shc", normed, qkv_weight, preferred_element_type=jnp.float32)
    queries = (
        projected[:, :, : groups * head_dim]
        .reshape(slot_count, local_heads, groups, head_dim)
        .astype(jnp.bfloat16)
    )
    key_new = projected[:, :, groups * head_dim : (groups + 1) * head_dim].astype(jnp.bfloat16)
    value_new = projected[:, :, (groups + 1) * head_dim :].astype(jnp.bfloat16)
    page_need = lax.div(seq_lens + page_len - 1, page_len)
    page_ids = jnp.arange(max_pages, dtype=jnp.int32)
    in_use = page_ids[None, :] < page_need[:, None]
    pool_ids = jnp.arange(pool_pages, dtype=jnp.int32)
    entry_slot = jnp.broadcast_to(
        jnp.arange(slot_count, dtype=jnp.int32)[:, None], (slot_count, max_pages)
    ).reshape(-1)
    entry_page = jnp.where(in_use, page_table, -1).reshape(-1)
    entry_order = jnp.broadcast_to(page_ids[None, :], (slot_count, max_pages)).reshape(-1)
    entry_len = jnp.broadcast_to(seq_lens[:, None], (slot_count, max_pages)).reshape(-1)
    len_unit = 64
    facts = jnp.concatenate(
        [
            (entry_slot[None, :] == jnp.arange(slot_count, dtype=jnp.int32)[:, None]).astype(jnp.float32),
            entry_order[None, :].astype(jnp.float32),
            lax.div(entry_len, len_unit)[None, :].astype(jnp.float32),
            lax.rem(entry_len, len_unit)[None, :].astype(jnp.float32),
        ],
        axis=0,
    ).astype(jnp.bfloat16)
    entry_hit = (entry_page[:, None] == pool_ids[None, :]).astype(jnp.bfloat16)
    page_facts = jnp.dot(facts, entry_hit, preferred_element_type=jnp.float32)
    belongs = page_facts[:slot_count] > 0.5
    page_order = page_facts[slot_count].astype(jnp.int32)
    owner_len = (
        page_facts[slot_count + 1].astype(jnp.int32) * len_unit
        + page_facts[slot_count + 2].astype(jnp.int32)
    )
    position = page_order[:, None] * page_len + jnp.arange(page_len, dtype=jnp.int32)[None, :]
    live = position < owner_len[:, None]
    scale_factor = head_dim ** (-0.5)
    page_queries = jnp.einsum(
        "sp,skgd->pkgd", belongs.astype(jnp.bfloat16), queries, preferred_element_type=jnp.float32
    ).astype(jnp.bfloat16)
    scores = (
        jnp.einsum(
            "pkgd,pkdt->pkgt",
            page_queries,
            kv_cache[:, :, :head_dim, :],
            preferred_element_type=jnp.float32,
        )
        * scale_factor
    )
    scores = jnp.where(live[:, None, None, :], scores, NEG_FILL)
    score_new = (
        jnp.einsum("skgd,skd->skg", queries, key_new, preferred_element_type=jnp.float32)
        * scale_factor
    )
    page_peak = jnp.max(scores, axis=3)
    slot_peak = jnp.max(jnp.where(belongs[:, :, None, None], page_peak[None], NEG_FILL), axis=1)
    slot_peak = jnp.maximum(slot_peak, score_new)
    page_peak_of_owner = jnp.max(
        jnp.where(belongs[:, :, None, None], slot_peak[:, None], NEG_FILL), axis=0
    )
    weights = jnp.where(
        live[:, None, None, :],
        jnp.exp(scores - page_peak_of_owner[..., None]),
        0.0,
    )
    page_total = jnp.sum(weights, axis=3)
    rounded_weights = lax.optimization_barrier(weights.astype(jnp.bfloat16))
    page_value = jnp.einsum(
        "pkgt,pkdt->pkgd",
        rounded_weights,
        kv_cache[:, :, head_dim:, :],
        preferred_element_type=jnp.float32,
    )
    belongs_f = belongs.astype(jnp.float32)
    total_sum = jnp.einsum("sp,pkg->skg", belongs_f, page_total, precision=lax.Precision.HIGHEST)
    value_sum = jnp.einsum(
        "sp,pkgd->skgd", belongs_f, page_value, precision=lax.Precision.HIGHEST
    )
    weight_new = jnp.exp(score_new - slot_peak)
    total_sum = total_sum + weight_new
    rounded_new = lax.optimization_barrier(weight_new.astype(jnp.bfloat16)).astype(jnp.float32)
    value_sum = value_sum + rounded_new[..., None] * value_new.astype(jnp.float32)[:, :, None, :]
    return (value_sum / total_sum[..., None]).astype(jnp.bfloat16).reshape(slot_count, -1)


def expert_apply(piece, gate_up, down):
    n_source, slot_num, local_experts, width = piece.shape
    rows_in = piece.transpose(2, 0, 1, 3).reshape(local_experts, n_source * slot_num, width)
    hidden_units = gate_up.shape[2] // 2
    gate_part = jnp.einsum(
        "erd,edf->erf", rows_in, gate_up[:, :, :hidden_units], preferred_element_type=jnp.float32
    )
    up_part = jnp.einsum(
        "erd,edf->erf", rows_in, gate_up[:, :, hidden_units:], preferred_element_type=jnp.float32
    )
    acts = (jax.nn.silu(gate_part) * up_part).astype(jnp.bfloat16)
    result = jnp.einsum("erf,efd->erd", acts, down, preferred_element_type=jnp.float32).astype(
        jnp.bfloat16
    )
    return result.reshape(local_experts, n_source, slot_num, width).transpose(1, 2, 0, 3)


def shards(
    hidden,
    perm,
    seq_lens,
    page_table,
    kv_cache,
    attn_gain,
    qkv_weight,
    out_weight,
    ffn_gain,
    router,
    routes,
    gate_up,
    down,
):
    req_index = lax.axis_index("req")
    kv_index = lax.axis_index("kv")
    n_req = lax.axis_size("req")
    n_kv = lax.axis_size("kv")
    local_rows, col_width = hidden.shape
    width = n_kv * col_width
    spread = jnp.broadcast_to(hidden[None], (n_kv, local_rows, col_width))
    block_parts = lax.all_to_all(spread, "kv", split_axis=0, concat_axis=0, tiled=True)
    deal = local_rows // n_req
    perm_blocks = perm.reshape(n_req, local_rows)
    source_block = lax.div(perm_blocks, local_rows)
    source_row = perm_blocks - source_block * local_rows
    mine = source_block == req_index
    rank_sent = jnp.cumsum(mine.astype(jnp.int32), axis=1) - 1
    send_key = jnp.where(mine, rank_sent * local_rows + source_row, -1)
    send_ids = jnp.arange(deal * local_rows, dtype=jnp.int32)
    send_pick = jnp.any(send_key[:, :, None] == send_ids[None, None, :], axis=1)
    send_pick = send_pick.reshape(n_req, deal, local_rows).astype(hidden.dtype)
    outgoing_rows = jnp.einsum(
        "dir,jrc->dijc", send_pick, block_parts, preferred_element_type=jnp.float32
    ).astype(hidden.dtype)
    arrived_rows = lax.all_to_all(
        outgoing_rows.reshape(n_req, deal, width), "req", split_axis=0, concat_axis=0, tiled=True
    ).reshape(n_req * deal, width)
    my_source = lax.dynamic_slice_in_dim(source_block, req_index, 1, 0).reshape(local_rows)
    slot_ids = jnp.arange(local_rows, dtype=jnp.int32)
    same_before = (my_source[None, :] == my_source[:, None]) & (slot_ids[None, :] < slot_ids[:, None])
    rank_got = jnp.sum(same_before.astype(jnp.int32), axis=1)
    take_key = my_source * deal + rank_got
    take_pick = (take_key[:, None] == slot_ids[None, :]).astype(hidden.dtype)
    tokens = jnp.dot(take_pick, arrived_rows, preferred_element_type=jnp.float32).astype(
        hidden.dtype
    )
    normed = rms_norm(tokens, attn_gain)
    head_out = attend(normed, seq_lens, page_table, kv_cache, qkv_weight)
    sub_rows = routes.shape[0]
    width = n_kv * col_width
    out_flat = out_weight.reshape(-1, out_weight.shape[2])
    partial = jnp.dot(head_out, out_flat, preferred_element_type=jnp.float32).astype(jnp.bfloat16)
    partial_parts = lax.all_to_all(
        partial.reshape(n_kv, sub_rows, partial.shape[1]), "kv", split_axis=0, concat_axis=0, tiled=True
    )
    attn_rows = jnp.sum(partial_parts.astype(jnp.float32), axis=0)
    own_tokens = lax.dynamic_slice_in_dim(tokens, kv_index * sub_rows, sub_rows, 0)
    residual = (own_tokens.astype(jnp.float32) + attn_rows).astype(jnp.bfloat16)
    normed_ffn = rms_norm(residual, ffn_gain)
    logits = jnp.dot(normed_ffn, router, preferred_element_type=jnp.float32)
    expert_ids = jnp.arange(logits.shape[1], dtype=jnp.int32)
    chosen = jnp.sum(
        jnp.where(routes[:, :, None] == expert_ids[None, None, :], logits[:, None, :], 0.0), axis=2
    )
    sigmoid_vals = jax.nn.sigmoid(chosen)
    gates = sigmoid_vals / jnp.sum(sigmoid_vals, axis=1, keepdims=True)
    experts_all = router.shape[1]
    local_experts = gate_up.shape[0]
    capacity = max(2, 2 * sub_rows // experts_all + 1)
    entry_ids = jnp.arange(routes.size, dtype=jnp.int32).reshape(routes.shape)
    same_expert = routes[:, :, None, None] == routes[None, None, :, :]
    earlier = entry_ids[None, None, :, :] < entry_ids[:, :, None, None]
    rank_in = jnp.sum((same_expert & earlier).astype(jnp.int32), axis=(2, 3))
    place_at = (
        lax.div(routes, local_experts) * capacity * local_experts
        + rank_in * local_experts
        + lax.rem(routes, local_experts)
    )
    slots_per_dest = capacity * local_experts
    dest_slot = (
        jnp.arange(n_req, dtype=jnp.int32)[:, None] * slots_per_dest
        + jnp.arange(slots_per_dest, dtype=jnp.int32)[None, :]
    )
    placement_plan = (place_at[:, :, None, None] == dest_slot[None, None, :, :]).astype(jnp.bfloat16)
    outgoing = jnp.einsum(
        "rjnc,rd->ncd", placement_plan, normed_ffn, preferred_element_type=jnp.float32
    ).astype(jnp.bfloat16)
    arrived = lax.all_to_all(outgoing, "req", split_axis=0, concat_axis=0, tiled=True)
    expert_rows = expert_apply(
        arrived.reshape(n_req, capacity, local_experts, width), gate_up, down
    ).reshape(n_req, slots_per_dest, width)
    returned = lax.all_to_all(expert_rows, "req", split_axis=0, concat_axis=0, tiled=True)
    paired_output = jnp.einsum(
        "rjnc,ncd->rjd", placement_plan, returned, preferred_element_type=jnp.float32
    )
    mixed = residual.astype(jnp.float32) + jnp.sum(gates[:, :, None] * paired_output, axis=1)
    return mixed.astype(jnp.bfloat16)


def solution(mesh):
    in_specs = (
        P("req", "kv"),
        P(),
        P("req"),
        P("req", None),
        P("req", "kv", None, None),
        P(),
        P("kv", None, None),
        P("kv", None, None),
        P(),
        P(),
        P(("req", "kv"), None),
        P("req", None, None),
        P("req", None, None),
    )
    out_specs = P(("req", "kv"), None)
    return jax.shard_map(shards, mesh=mesh, in_specs=in_specs, out_specs=out_specs, check_vma=False)
```

```python
import jax
import jax.numpy as jnp
from jax import lax
from jax.sharding import PartitionSpec as P

REQ_DEV = 64


NEG_FILL = -1e30
EPS_NORM = 1e-05


def rms_norm(values, gain_vec):
    values = values.astype(jnp.float32)
    factor = lax.rsqrt(jnp.mean(values * values, axis=-1, keepdims=True) + EPS_NORM)
    return (values * factor * gain_vec).astype(jnp.bfloat16)


def attend(normed, seq_lens, page_table, kv_cache, qkv_weight):
    pool_pages, local_heads, twice_hd, page_len = kv_cache.shape
    head_dim = twice_hd // 2
    slot_count = normed.shape[0]
    groups = qkv_weight.shape[2] // head_dim - 2
    max_pages = page_table.shape[1]
    projected = jnp.einsum("sd,hdc->shc", normed, qkv_weight, preferred_element_type=jnp.float32)
    queries = (
        projected[:, :, : groups * head_dim]
        .reshape(slot_count, local_heads, groups, head_dim)
        .astype(jnp.bfloat16)
    )
    key_new = projected[:, :, groups * head_dim : (groups + 1) * head_dim].astype(jnp.bfloat16)
    value_new = projected[:, :, (groups + 1) * head_dim :].astype(jnp.bfloat16)
    page_need = lax.div(seq_lens + page_len - 1, page_len)
    page_ids = jnp.arange(max_pages, dtype=jnp.int32)
    in_use = page_ids[None, :] < page_need[:, None]
    pool_ids = jnp.arange(pool_pages, dtype=jnp.int32)
    entry_slot = jnp.broadcast_to(
        jnp.arange(slot_count, dtype=jnp.int32)[:, None], (slot_count, max_pages)
    ).reshape(-1)
    entry_page = jnp.where(in_use, page_table, -1).reshape(-1)
    entry_order = jnp.broadcast_to(page_ids[None, :], (slot_count, max_pages)).reshape(-1)
    entry_len = jnp.broadcast_to(seq_lens[:, None], (slot_count, max_pages)).reshape(-1)
    len_unit = 64
    facts = jnp.concatenate(
        [
            (entry_slot[None, :] == jnp.arange(slot_count, dtype=jnp.int32)[:, None]).astype(jnp.float32),
            entry_order[None, :].astype(jnp.float32),
            lax.div(entry_len, len_unit)[None, :].astype(jnp.float32),
            lax.rem(entry_len, len_unit)[None, :].astype(jnp.float32),
        ],
        axis=0,
    ).astype(jnp.bfloat16)
    entry_hit = (entry_page[:, None] == pool_ids[None, :]).astype(jnp.bfloat16)
    page_facts = jnp.dot(facts, entry_hit, preferred_element_type=jnp.float32)
    belongs = page_facts[:slot_count] > 0.5
    page_order = page_facts[slot_count].astype(jnp.int32)
    owner_len = (
        page_facts[slot_count + 1].astype(jnp.int32) * len_unit
        + page_facts[slot_count + 2].astype(jnp.int32)
    )
    position = page_order[:, None] * page_len + jnp.arange(page_len, dtype=jnp.int32)[None, :]
    live = position < owner_len[:, None]
    scale_factor = head_dim ** (-0.5)
    page_queries = jnp.einsum(
        "sp,skgd->pkgd", belongs.astype(jnp.bfloat16), queries, preferred_element_type=jnp.float32
    ).astype(jnp.bfloat16)
    scores = (
        jnp.einsum(
            "pkgd,pkdt->pkgt",
            page_queries,
            kv_cache[:, :, :head_dim, :],
            preferred_element_type=jnp.float32,
        )
        * scale_factor
    )
    scores = jnp.where(live[:, None, None, :], scores, NEG_FILL)
    score_new = (
        jnp.einsum("skgd,skd->skg", queries, key_new, preferred_element_type=jnp.float32)
        * scale_factor
    )
    page_peak = jnp.max(scores, axis=3)
    slot_peak = jnp.max(jnp.where(belongs[:, :, None, None], page_peak[None], NEG_FILL), axis=1)
    slot_peak = jnp.maximum(slot_peak, score_new)
    page_peak_of_owner = jnp.max(
        jnp.where(belongs[:, :, None, None], slot_peak[:, None], NEG_FILL), axis=0
    )
    weights = jnp.where(
        live[:, None, None, :],
        jnp.exp(scores - page_peak_of_owner[..., None]),
        0.0,
    )
    page_total = jnp.sum(weights, axis=3)
    rounded_weights = lax.optimization_barrier(weights.astype(jnp.bfloat16))
    page_value = jnp.einsum(
        "pkgt,pkdt->pkgd",
        rounded_weights,
        kv_cache[:, :, head_dim:, :],
        preferred_element_type=jnp.float32,
    )
    belongs_f = belongs.astype(jnp.float32)
    total_sum = jnp.einsum("sp,pkg->skg", belongs_f, page_total, precision=lax.Precision.HIGHEST)
    value_sum = jnp.einsum(
        "sp,pkgd->skgd", belongs_f, page_value, precision=lax.Precision.HIGHEST
    )
    weight_new = jnp.exp(score_new - slot_peak)
    total_sum = total_sum + weight_new
    rounded_new = lax.optimization_barrier(weight_new.astype(jnp.bfloat16)).astype(jnp.float32)
    value_sum = value_sum + rounded_new[..., None] * value_new.astype(jnp.float32)[:, :, None, :]
    return (value_sum / total_sum[..., None]).astype(jnp.bfloat16).reshape(slot_count, -1)


def expert_apply(piece, gate_up, down):
    n_source, slot_num, local_experts, width = piece.shape
    rows_in = piece.transpose(2, 0, 1, 3).reshape(local_experts, n_source * slot_num, width)
    projected_up = jnp.einsum("erd,edf->erf", rows_in, gate_up, preferred_element_type=jnp.float32)
    hidden_units = gate_up.shape[2] // 2
    acts = (
        jax.nn.silu(projected_up[..., :hidden_units]) * projected_up[..., hidden_units:]
    ).astype(jnp.bfloat16)
    result = jnp.einsum("erf,efd->erd", acts, down, preferred_element_type=jnp.float32).astype(
        jnp.bfloat16
    )
    return result.reshape(local_experts, n_source, slot_num, width).transpose(1, 2, 0, 3)


def shards(
    hidden,
    perm,
    seq_lens,
    page_table,
    kv_cache,
    attn_gain,
    qkv_weight,
    out_weight,
    ffn_gain,
    router,
    routes,
    gate_up,
    down,
):
    req_index = lax.axis_index("req")
    kv_index = lax.axis_index("kv")
    n_req = lax.axis_size("req")
    n_kv = lax.axis_size("kv")
    local_rows, col_width = hidden.shape
    width = n_kv * col_width
    spread = jnp.broadcast_to(hidden[None], (n_kv, local_rows, col_width))
    block_parts = lax.all_to_all(spread, "kv", split_axis=0, concat_axis=0, tiled=True)
    deal = local_rows // n_req
    perm_blocks = perm.reshape(n_req, local_rows)
    source_block = lax.div(perm_blocks, local_rows)
    source_row = perm_blocks - source_block * local_rows
    mine = source_block == req_index
    rank_sent = jnp.cumsum(mine.astype(jnp.int32), axis=1) - 1
    send_key = jnp.where(mine, rank_sent * local_rows + source_row, -1)
    send_ids = jnp.arange(deal * local_rows, dtype=jnp.int32)
    send_pick = jnp.any(send_key[:, :, None] == send_ids[None, None, :], axis=1)
    send_pick = send_pick.reshape(n_req, deal, local_rows).astype(hidden.dtype)
    outgoing_rows = jnp.einsum(
        "dir,jrc->dijc", send_pick, block_parts, preferred_element_type=jnp.float32
    ).astype(hidden.dtype)
    arrived_rows = lax.all_to_all(outgoing_rows, "req", split_axis=0, concat_axis=0, tiled=True)
    my_source = lax.dynamic_slice_in_dim(source_block, req_index, 1, 0).reshape(local_rows)
    slot_ids = jnp.arange(local_rows, dtype=jnp.int32)
    same_before = (my_source[None, :] == my_source[:, None]) & (slot_ids[None, :] < slot_ids[:, None])
    rank_got = jnp.sum(same_before.astype(jnp.int32), axis=1)
    take_key = my_source * deal + rank_got
    take_pick = (take_key[:, None] == slot_ids[None, :]).astype(hidden.dtype)
    tokens = jnp.einsum(
        "sri,rijc->sjc", take_pick.reshape(local_rows, n_req, deal), arrived_rows,
        preferred_element_type=jnp.float32,
    ).astype(hidden.dtype).reshape(local_rows, width)
    normed = rms_norm(tokens, attn_gain)
    head_out = attend(normed, seq_lens, page_table, kv_cache, qkv_weight)
    sub_rows = routes.shape[0]
    width = n_kv * col_width
    out_flat = out_weight.reshape(-1, out_weight.shape[2])
    partial = jnp.dot(head_out, out_flat, preferred_element_type=jnp.float32).astype(jnp.bfloat16)
    partial_parts = lax.all_to_all(
        partial.reshape(n_kv, sub_rows, partial.shape[1]), "kv", split_axis=0, concat_axis=0, tiled=True
    )
    attn_rows = jnp.sum(partial_parts.astype(jnp.float32), axis=0)
    own_tokens = lax.dynamic_slice_in_dim(tokens, kv_index * sub_rows, sub_rows, 0)
    residual = (own_tokens.astype(jnp.float32) + attn_rows).astype(jnp.bfloat16)
    normed_ffn = rms_norm(residual, ffn_gain)
    logits = jnp.dot(normed_ffn, router, preferred_element_type=jnp.float32)
    expert_ids = jnp.arange(logits.shape[1], dtype=jnp.int32)
    chosen = jnp.sum(
        jnp.where(routes[:, :, None] == expert_ids[None, None, :], logits[:, None, :], 0.0), axis=2
    )
    sigmoid_vals = jax.nn.sigmoid(chosen)
    gates = sigmoid_vals / jnp.sum(sigmoid_vals, axis=1, keepdims=True)
    experts_all = router.shape[1]
    local_experts = gate_up.shape[0]
    capacity = max(2, 2 * sub_rows // experts_all + 1)
    entry_ids = jnp.arange(routes.size, dtype=jnp.int32).reshape(routes.shape)
    same_expert = routes[:, :, None, None] == routes[None, None, :, :]
    earlier = entry_ids[None, None, :, :] < entry_ids[:, :, None, None]
    rank_in = jnp.sum((same_expert & earlier).astype(jnp.int32), axis=(2, 3))
    place_at = (
        lax.div(routes, local_experts) * capacity * local_experts
        + rank_in * local_experts
        + lax.rem(routes, local_experts)
    )
    slots_per_dest = capacity * local_experts
    dest_slot = (
        jnp.arange(n_req, dtype=jnp.int32)[:, None] * slots_per_dest
        + jnp.arange(slots_per_dest, dtype=jnp.int32)[None, :]
    )
    placement_plan = (place_at[:, :, None, None] == dest_slot[None, None, :, :]).astype(jnp.bfloat16)
    outgoing = jnp.einsum(
        "rjnc,rd->ncd", placement_plan, normed_ffn, preferred_element_type=jnp.float32
    ).astype(jnp.bfloat16)
    arrived = lax.all_to_all(outgoing, "req", split_axis=0, concat_axis=0, tiled=True)
    expert_rows = expert_apply(
        arrived.reshape(n_req, capacity, local_experts, width), gate_up, down
    ).reshape(n_req, slots_per_dest, width)
    returned = lax.all_to_all(expert_rows, "req", split_axis=0, concat_axis=0, tiled=True)
    paired_output = jnp.einsum(
        "rjnc,ncd->rjd", placement_plan, returned, preferred_element_type=jnp.float32
    )
    mixed = residual.astype(jnp.float32) + jnp.sum(gates[:, :, None] * paired_output, axis=1)
    return mixed.astype(jnp.bfloat16)


def solution(mesh):
    in_specs = (
        P("req", "kv"),
        P(),
        P("req"),
        P("req", None),
        P("req", "kv", None, None),
        P(),
        P("kv", None, None),
        P("kv", None, None),
        P(),
        P(),
        P(("req", "kv"), None),
        P("req", None, None),
        P("req", None, None),
    )
    out_specs = P(("req", "kv"), None)
    return jax.shard_map(shards, mesh=mesh, in_specs=in_specs, out_specs=out_specs, check_vma=False)
```
